32 devices in a mesh: ctx: 4 (over z), fsdp: 2 (over y), rep: 4 (over x, core).
Axes of the slice: x: 2, y: 2, z: 4, core: 2. Of those that a mesh axis runs over, the one named last changes fastest.
Arguments:
- frames_in: bfloat16 [8, 512, 1024], P('rep', 'ctx', 'fsdp'), parts along dimension 0, may hold values from -6 to 6
- lengths: int32 [8], P('rep'), parts along dimension 0, may hold values from 128 to 512, as said below
- conv_weight: bfloat16 [16, 128, 64, 64], P('fsdp'), may hold values from -0.0625 to 0.0625
- conv_bias: bfloat16 [1024], P('fsdp'), may hold values from -3 to 3
- norm_gain: float32 [1024], replicated, may hold values from 0.1 to 1.9
- norm_shift: float32 [1024], replicated, may hold values from -3 to 3
- w_query: bfloat16 [1024, 512], replicated
- w_key: bfloat16 [1024, 512], replicated
- w_value: bfloat16 [1024, 512], replicated, may hold values from -0.1875 to 0.1875
Outputs:
- hidden: bfloat16 [8, 512, 1024], P('rep', 'ctx', 'fsdp'), parts along dimension 0
- context: bfloat16 [8, 512, 512], P(('rep', 'fsdp'), 'ctx'), parts along dimension 0
The draws below stay inside these ranges and needn't reach their ends.
There are 4 independent parts, one for each index of `rep`. The reference program is written for one: setup_inputs(seed, part) draws one part's arguments, and reference() takes and returns one part's arrays. A program takes and returns all parts, laid end to end along the dimension named above; an argument that names none is the same for every part. Nothing has to cross between parts.
Inputs may be any that keep to these rules, and one draw needn't show every extreme that they name: `lengths`: one recording in every draw has all 512 frames live.
All inputs are finite; a program needn't handle non-finite values.
Results may differ from the reference program's by a relative error of at most 0.012.
Values may be sent and summed in bfloat16 or wider, within the bound.
No kernel may reach another device: no remote copies, remote signals or barrier semaphores. Data moves between devices by JAX's collectives and lax.ppermute only.
A program may use at most 128 MiB of HBM per device.

```python
import math
import jax
import jax.numpy as jnp
from jax import lax

D = 1024
G = 16
KW = 128
HEADS = 8
HD = 64
CG = 64
RECS = 2
FRAMES = 512


def shared_keys(key):
    return jax.random.normal(jax.random.fold_in(key, 7), (D, HEADS * HD), jnp.float32) / math.sqrt(D)


def draw_w_key(key, part):
    return shared_keys(key).astype(jnp.bfloat16)


def draw_w_query(key, part):
    own = 3.0 * jax.random.normal(jax.random.fold_in(key, 11), (D, HEADS * HD), jnp.float32) / math.sqrt(D)
    return own.astype(jnp.bfloat16)


def draw_lengths(key, part):
    drawn = jax.random.randint(jax.random.fold_in(key, 3), (RECS,), FRAMES // 4, FRAMES + 1, dtype=jnp.int32)
    full_one = jax.random.randint(jax.random.fold_in(key, 5), (), 0, RECS, dtype=jnp.int32)
    return jnp.where(jnp.arange(RECS, dtype=jnp.int32) == full_one, FRAMES, drawn).astype(jnp.int32)


def block_levels(stream_key, extent, split, low, largest):
    gain, own = 1.0, jax.random.fold_in(stream_key, 6)
    for dim, parts in split:
        heights = jnp.exp(jax.random.uniform(jax.random.fold_in(own, dim), (parts,), jnp.float32, low / len(split), largest / len(split)))
        gain = gain * jnp.repeat(heights, extent[dim] // parts).reshape([-1 if axis == dim else 1 for axis in range(len(extent))])
    return gain


def gaussian(key, shape, scale, limit, shards=(), kind=jnp.bfloat16):
    gain = block_levels(key, shape, shards, -0.22, 0.18) if shards else 1.0
    values = jax.random.normal(key, shape, jnp.float32) * scale * gain
    return jnp.minimum(jnp.maximum(values, -limit), limit).astype(kind)


def setup_inputs(seed: int = 0, part: int = 0) -> dict:
    splits = jax.random.split(jax.random.key(seed), 10)
    own_keys = jax.random.split(jax.random.fold_in(splits[9], part), 10)
    return {
        "frames_in": gaussian(own_keys[0], (RECS, FRAMES, D), 1.0, 6.0, ((1, 4), (2, 2))),
        "lengths": draw_lengths(jax.random.fold_in(jax.random.fold_in(splits[9], part), 71), part),
        "conv_weight": gaussian(splits[2], (G, KW, CG, CG), (KW * CG) ** -0.5, 0.0625, ((0, 2),)),
        "conv_bias": gaussian(splits[3], (D,), 0.5, 3.0, ((0, 2),)),
        "norm_gain": jnp.clip(1.0 + 0.18 * jax.random.normal(splits[4], (D,), jnp.float32), 0.1, 1.9),
        "norm_shift": gaussian(splits[5], (D,), 0.5, 3.0, (), jnp.float32),
        "w_query": draw_w_query(jax.random.fold_in(splits[9], 71), part),
        "w_key": draw_w_key(jax.random.fold_in(splits[9], 71), part),
        "w_value": gaussian(splits[8], (D, HEADS * HD), D ** -0.5, 0.1875),
    }


def one_head(query_h, key_h, value_h, length):
    scores = jnp.dot(query_h, key_h.T, preferred_element_type=jnp.float32) / math.sqrt(HD)
    key_pos = jnp.arange(FRAMES, dtype=jnp.int32)
    valid = (key_pos < length)[None, :]
    scores = jnp.where(valid, scores, -1e+30)
    rowmax = lax.optimization_barrier(jnp.max(scores, axis=1, keepdims=True))
    weights = jnp.where(valid, jnp.exp(scores - rowmax), 0.0)
    total = lax.optimization_barrier(jnp.sum(weights, axis=1, keepdims=True))
    summed = jnp.dot(weights.astype(jnp.bfloat16), value_h, preferred_element_type=jnp.float32)
    return summed / total

def one_record(hidden_rec, length, norm_gain, norm_shift, w_query, w_key, w_value):
    flat = hidden_rec.astype(jnp.float32)
    centre = lax.optimization_barrier(jnp.mean(flat, axis=1, keepdims=True))
    spread = lax.optimization_barrier(jnp.mean((flat - centre) ** 2, axis=1, keepdims=True))
    normed = ((flat - centre) / jnp.sqrt(spread + 1e-05) * norm_gain + norm_shift).astype(jnp.bfloat16)
    query = jnp.dot(normed, w_query, preferred_element_type=jnp.float32).astype(jnp.bfloat16)
    keys = jnp.dot(normed, w_key, preferred_element_type=jnp.float32).astype(jnp.bfloat16)
    values = jnp.dot(normed, w_value, preferred_element_type=jnp.float32).astype(jnp.bfloat16)
    query = query.reshape(FRAMES, HEADS, HD).transpose(1, 0, 2)
    keys = keys.reshape(FRAMES, HEADS, HD).transpose(1, 0, 2)
    values = values.reshape(FRAMES, HEADS, HD).transpose(1, 0, 2)
    outs = lax.map(lambda trio: one_head(trio[0], trio[1], trio[2], length), (query, keys, values))
    outs = outs.transpose(1, 0, 2).reshape(FRAMES, HEADS * HD)
    live = (jnp.arange(FRAMES, dtype=jnp.int32) < length)[:, None]
    return jnp.where(live, outs, 0.0).astype(jnp.bfloat16)

def reference(frames_in, lengths, conv_weight, conv_bias, norm_gain, norm_shift, w_query, w_key, w_value):
    positions = jnp.arange(FRAMES, dtype=jnp.int32)
    live = positions[None, :] < lengths[:, None]
    masked = jnp.where(live[:, :, None], frames_in, jnp.zeros((), frames_in.dtype))
    kernel = conv_weight.astype(jnp.float32).transpose(1, 2, 0, 3).reshape(KW, CG, D)
    conv = lax.conv_general_dilated(masked.astype(jnp.float32), kernel, (1,), [(KW // 2, KW // 2 - 1)], dimension_numbers=('NWC', 'WIO', 'NWC'), feature_group_count=G, precision=lax.Precision.HIGHEST)
    hidden = (masked.astype(jnp.float32) + jax.nn.gelu(conv + conv_bias.astype(jnp.float32), approximate=False)).astype(jnp.bfloat16)
    context = lax.map(lambda pair: one_record(pair[0], pair[1], norm_gain, norm_shift, w_query, w_key, w_value), (hidden, lengths))
    return (hidden, context)
```

```python
import math

import jax
import jax.numpy as jnp
from jax import lax
from jax.sharding import PartitionSpec as P

HD = 64


def padded_2(x, sides, width):
    for axis, dim in sides:
        size, length = (lax.axis_size(axis), x.shape[dim])
        up = [(i, (i + 1) % size) for i in range(size - 1)]
        down = [(j, i) for i, j in up]
        last = lax.slice_in_dim(x, length - width, length, axis=dim)
        first = lax.slice_in_dim(x, 0, width, axis=dim)
        before = lax.ppermute(last, axis, up)
        after = lax.ppermute(first, axis, down)
        x = jnp.concatenate([before, x, after], axis=dim)
    return x


def attend(carry, piece, start, queries, own_length):
    best, total, accum = carry
    keys_part, vals_part = piece
    count = keys_part.shape[0]
    head_count = queries.shape[1]
    keys_part = keys_part.reshape(count, head_count, HD)
    vals_part = vals_part.reshape(count, head_count, HD)
    scores = jnp.einsum(
        "fhd,nhd->fhn", queries, keys_part, preferred_element_type=jnp.float32
    ) / math.sqrt(HD)
    valid = (start + jnp.arange(count, dtype=jnp.int32) < own_length)[None, None, :]
    scores = jnp.where(valid, scores, -1e30)
    fresh = jnp.maximum(best, jnp.max(scores, axis=2))
    weights = jnp.where(valid, jnp.exp(scores - fresh[:, :, None]), 0.0)
    factor = jnp.exp(best - fresh)
    total = total * factor + jnp.sum(weights, axis=2)
    accum = accum * factor[:, :, None] + jnp.einsum(
        "fhn,nhd->fhd", weights.astype(jnp.bfloat16), vals_part, preferred_element_type=jnp.float32
    )
    return (fresh, total, accum)


def start_state(rows, heads_here):
    return (
        jnp.full((rows, heads_here), -1e30, jnp.float32),
        jnp.zeros((rows, heads_here), jnp.float32),
        jnp.zeros((rows, heads_here, HD), jnp.float32),
    )


def blockwise(carry, all_keys, all_vals, queries, own_length, block_rows):
    block_count = all_keys.shape[0] // block_rows

    def block_step(state, index):
        begin = index * block_rows
        piece = (
            lax.dynamic_slice_in_dim(all_keys, begin, block_rows, 0),
            lax.dynamic_slice_in_dim(all_vals, begin, block_rows, 0),
        )
        return (attend(state, piece, begin, queries, own_length), None)

    final, unused = lax.scan(block_step, carry, jnp.arange(block_count, dtype=jnp.int32))
    return final


def finish(final, query_pos, own_length):
    best, total, accum = final
    result = accum / total[:, :, None]
    query_live = (query_pos < own_length)[:, None, None]
    result = jnp.where(query_live, result, 0.0)
    return result.reshape(result.shape[0], result.shape[1] * HD).astype(jnp.bfloat16)


def per_device(
    frames_in, lengths, conv_weight, conv_bias, norm_gain, norm_shift, w_query, w_key, w_value
):
    record_count, frame_rows, channels = frames_in.shape
    ctx_place = lax.axis_index("ctx")
    positions = ctx_place * frame_rows + jnp.arange(frame_rows, dtype=jnp.int32)
    live = positions[None, :] < lengths[:, None]
    masked = jnp.where(live[:, :, None], frames_in, jnp.zeros((), frames_in.dtype))
    groups_here, kernel_width, group_in, group_out = conv_weight.shape
    half_width = kernel_width // 2
    padded = padded_2(masked, (("ctx", 1),), half_width)
    kernel = conv_weight.transpose(1, 2, 0, 3).reshape(
        kernel_width, group_in, groups_here * group_out
    )
    conv_out = lax.conv_general_dilated(
        padded[:, : frame_rows + kernel_width - 1],
        kernel,
        (1,),
        "VALID",
        dimension_numbers=("NWC", "WIO", "NWC"),
        feature_group_count=groups_here,
        preferred_element_type=jnp.float32,
    )
    hidden = (
        masked.astype(jnp.float32)
        + jax.nn.gelu(conv_out + conv_bias.astype(jnp.float32), approximate=False)
    ).astype(jnp.bfloat16)
    record = lax.all_to_all(hidden, "fsdp", split_axis=0, concat_axis=2, tiled=True)
    own_length = lax.dynamic_index_in_dim(lengths, lax.axis_index("fsdp"), 0, keepdims=False)
    flat = record[0].astype(jnp.float32)
    centre = jnp.mean(flat, axis=1, keepdims=True)
    spread = jnp.mean((flat - centre) ** 2, axis=1, keepdims=True)
    normed = ((flat - centre) / jnp.sqrt(spread + 1e-05) * norm_gain + norm_shift).astype(
        jnp.bfloat16
    )
    query_flat = jnp.dot(normed, w_query, preferred_element_type=jnp.float32).astype(jnp.bfloat16)
    key_flat = jnp.dot(normed, w_key, preferred_element_type=jnp.float32).astype(jnp.bfloat16)
    val_flat = jnp.dot(normed, w_value, preferred_element_type=jnp.float32).astype(jnp.bfloat16)
    head_count = query_flat.shape[1] // HD
    queries = query_flat.reshape(frame_rows, head_count, HD)
    block_rows = 4 * frame_rows
    both = lax.all_gather(jnp.concatenate([key_flat, val_flat], axis=1), "ctx", axis=0, tiled=True)
    whole_keys, whole_vals = both[:, : key_flat.shape[1]], both[:, key_flat.shape[1] :]
    final = blockwise(
        start_state(frame_rows, head_count), whole_keys, whole_vals, queries, own_length, block_rows
    )
    result = finish(final, positions, own_length).reshape(1, frame_rows, head_count * HD)
    return (hidden, result)


def solution(mesh):
    in_specs = (
        P("rep", "ctx", "fsdp"),
        P("rep"),
        P("fsdp", None, None, None),
        P("fsdp"),
        P(),
        P(),
        P(),
        P(),
        P(),
    )
    out_specs = (P("rep", "ctx", "fsdp"), P(("rep", "fsdp"), "ctx", None))
    return jax.shard_map(
        per_device, mesh=mesh, in_specs=in_specs, out_specs=out_specs, check_vma=False
    )
```

```python
import math

import jax
import jax.numpy as jnp
from jax import lax
from jax.sharding import PartitionSpec as P
from jax.experimental import pallas as pl
from jax.experimental.pallas import tpu as pltpu

HD = 64


def padded_2(x, sides, width):
    for axis, dim in sides:
        size, length = (lax.axis_size(axis), x.shape[dim])
        up = [(i, (i + 1) % size) for i in range(size - 1)]
        down = [(j, i) for i, j in up]
        last = lax.slice_in_dim(x, length - width, length, axis=dim)
        first = lax.slice_in_dim(x, 0, width, axis=dim)
        before = lax.ppermute(last, axis, up)
        after = lax.ppermute(first, axis, down)
        x = jnp.concatenate([before, x, after], axis=dim)
    return x


TAP_STEP = 16


def conv_body(x_ref, w_ref, out_ref):
    recs, rows, width = x_ref.shape[1], out_ref.shape[2], x_ref.shape[3]
    taps = w_ref.shape[1]
    acc = jnp.zeros((recs * rows, w_ref.shape[3]), jnp.float32)
    for chunk in range(taps // TAP_STEP):
        lhs = x_ref[0, :, chunk * TAP_STEP : chunk * TAP_STEP + rows, :].reshape(recs * rows, width)
        rhs = w_ref[0, chunk * TAP_STEP : (chunk + 1) * TAP_STEP].reshape(width, w_ref.shape[3])
        acc = acc + jnp.dot(lhs, rhs, preferred_element_type=jnp.float32)
    out_ref[0] = acc.reshape(recs, rows, w_ref.shape[3])


def grouped_conv(padded, conv_weight, frame_rows):
    recs = padded.shape[0]
    groups_here, taps, group_in, group_out = conv_weight.shape
    span = frame_rows + taps - TAP_STEP
    grouped = padded.reshape(recs, padded.shape[1], groups_here, group_in)
    shifted = jnp.stack([grouped[:, j : j + span] for j in range(TAP_STEP)], axis=3)
    expanded = shifted.transpose(2, 0, 1, 3, 4).reshape(groups_here, recs, span, TAP_STEP * group_in)
    out = pl.pallas_call(
        conv_body,
        grid=(groups_here,),
        in_specs=[
            pl.BlockSpec((1, recs, span, TAP_STEP * group_in), lambda g: (g, 0, 0, 0)),
            pl.BlockSpec((1, taps, group_in, group_out), lambda g: (g, 0, 0, 0)),
        ],
        out_specs=pl.BlockSpec((1, recs, frame_rows, group_out), lambda g: (g, 0, 0, 0)),
        out_shape=jax.ShapeDtypeStruct((groups_here, recs, frame_rows, group_out), jnp.float32),
        cost_estimate=pl.CostEstimate(
            flops=2 * groups_here * recs * frame_rows * taps * group_in * group_out,
            bytes_accessed=expanded.size * 2 + conv_weight.size * 2 + groups_here * recs * frame_rows * group_out * 4,
            transcendentals=0,
        ),
    )(expanded, conv_weight)
    return out.transpose(1, 2, 0, 3).reshape(recs, frame_rows, groups_here * group_out)


def attend(carry, piece, start, queries, own_length):
    best, total, accum = carry
    keys_part, vals_part = piece
    count = keys_part.shape[0]
    head_count = queries.shape[1]
    keys_part = keys_part.reshape(count, head_count, HD)
    vals_part = vals_part.reshape(count, head_count, HD)
    scores = jnp.einsum(
        "fhd,nhd->fhn", queries, keys_part, preferred_element_type=jnp.float32
    ) / math.sqrt(HD)
    valid = (start + jnp.arange(count, dtype=jnp.int32) < own_length)[None, None, :]
    scores = jnp.where(valid, scores, -1e30)
    fresh = jnp.maximum(best, jnp.max(scores, axis=2))
    weights = jnp.where(valid, jnp.exp(scores - fresh[:, :, None]), 0.0)
    factor = jnp.exp(best - fresh)
    total = total * factor + jnp.sum(weights, axis=2)
    accum = accum * factor[:, :, None] + jnp.einsum(
        "fhn,nhd->fhd", weights.astype(jnp.bfloat16), vals_part, preferred_element_type=jnp.float32
    )
    return (fresh, total, accum)


def start_state(rows, heads_here):
    return (
        jnp.full((rows, heads_here), -1e30, jnp.float32),
        jnp.zeros((rows, heads_here), jnp.float32),
        jnp.zeros((rows, heads_here, HD), jnp.float32),
    )


def blockwise(carry, all_keys, all_vals, queries, own_length, block_rows):
    block_count = all_keys.shape[0] // block_rows

    def block_step(state, index):
        begin = index * block_rows
        piece = (
            lax.dynamic_slice_in_dim(all_keys, begin, block_rows, 0),
            lax.dynamic_slice_in_dim(all_vals, begin, block_rows, 0),
        )
        return (attend(state, piece, begin, queries, own_length), None)

    final, unused = lax.scan(block_step, carry, jnp.arange(block_count, dtype=jnp.int32))
    return final


def finish(final, query_pos, own_length):
    best, total, accum = final
    result = accum / total[:, :, None]
    query_live = (query_pos < own_length)[:, None, None]
    result = jnp.where(query_live, result, 0.0)
    return result.reshape(result.shape[0], result.shape[1] * HD).astype(jnp.bfloat16)


def per_device(
    frames_in, lengths, conv_weight, conv_bias, norm_gain, norm_shift, w_query, w_key, w_value
):
    record_count, frame_rows, channels = frames_in.shape
    ctx_place = lax.axis_index("ctx")
    positions = ctx_place * frame_rows + jnp.arange(frame_rows, dtype=jnp.int32)
    live = positions[None, :] < lengths[:, None]
    masked = jnp.where(live[:, :, None], frames_in, jnp.zeros((), frames_in.dtype))
    groups_here, kernel_width, group_in, group_out = conv_weight.shape
    half_width = kernel_width // 2
    padded = padded_2(masked, (("ctx", 1),), half_width)
    conv_out = grouped_conv(padded, conv_weight, frame_rows)
    hidden = (
        masked.astype(jnp.float32)
        + jax.nn.gelu(conv_out + conv_bias.astype(jnp.float32), approximate=False)
    ).astype(jnp.bfloat16)
    record = lax.all_to_all(hidden, "fsdp", split_axis=0, concat_axis=2, tiled=True)
    own_length = lax.dynamic_index_in_dim(lengths, lax.axis_index("fsdp"), 0, keepdims=False)
    flat = record[0].astype(jnp.float32)
    centre = jnp.mean(flat, axis=1, keepdims=True)
    spread = jnp.mean((flat - centre) ** 2, axis=1, keepdims=True)
    normed = ((flat - centre) / jnp.sqrt(spread + 1e-05) * norm_gain + norm_shift).astype(
        jnp.bfloat16
    )
    query_flat = jnp.dot(normed, w_query, preferred_element_type=jnp.float32).astype(jnp.bfloat16)
    key_flat = jnp.dot(normed, w_key, preferred_element_type=jnp.float32).astype(jnp.bfloat16)
    val_flat = jnp.dot(normed, w_value, preferred_element_type=jnp.float32).astype(jnp.bfloat16)
    head_count = query_flat.shape[1] // HD
    queries = query_flat.reshape(frame_rows, head_count, HD)
    block_rows = 4 * frame_rows
    whole_keys, whole_vals = (
        lax.all_gather(key_flat, "ctx", axis=0, tiled=True),
        lax.all_gather(val_flat, "ctx", axis=0, tiled=True),
    )
    final = blockwise(
        start_state(frame_rows, head_count), whole_keys, whole_vals, queries, own_length, block_rows
    )
    result = finish(final, positions, own_length).reshape(1, frame_rows, head_count * HD)
    return (hidden, result)


def solution(mesh):
    in_specs = (
        P("rep", "ctx", "fsdp"),
        P("rep"),
        P("fsdp", None, None, None),
        P("fsdp"),
        P(),
        P(),
        P(),
        P(),
        P(),
    )
    out_specs = (P("rep", "ctx", "fsdp"), P(("rep", "fsdp"), "ctx", None))
    return jax.shard_map(
        per_device, mesh=mesh, in_specs=in_specs, out_specs=out_specs, check_vma=False
    )
```

```python
import math

import jax
import jax.numpy as jnp
from jax import lax
from jax.sharding import PartitionSpec as P
from jax.experimental import pallas as pl
from jax.experimental.pallas import tpu as pltpu

HD = 64


def padded_2(x, sides, width):
    for axis, dim in sides:
        size, length = (lax.axis_size(axis), x.shape[dim])
        up = [(i, (i + 1) % size) for i in range(size - 1)]
        down = [(j, i) for i, j in up]
        last = lax.slice_in_dim(x, length - width, length, axis=dim)
        first = lax.slice_in_dim(x, 0, width, axis=dim)
        before = lax.ppermute(last, axis, up)
        after = lax.ppermute(first, axis, down)
        x = jnp.concatenate([before, x, after], axis=dim)
    return x


TAP_STEP = 16


def conv_body(x_ref, w_ref, out_ref):
    recs, rows, width = x_ref.shape[1], out_ref.shape[2], x_ref.shape[3]
    taps = w_ref.shape[1]
    acc = jnp.zeros((recs * rows, w_ref.shape[3]), jnp.float32)
    for chunk in range(taps // TAP_STEP):
        lhs = x_ref[0, :, chunk * TAP_STEP : chunk * TAP_STEP + rows, :].reshape(recs * rows, width)
        rhs = w_ref[0, chunk * TAP_STEP : (chunk + 1) * TAP_STEP].reshape(width, w_ref.shape[3])
        acc = acc + jnp.dot(lhs, rhs, preferred_element_type=jnp.float32)
    out_ref[0] = acc.reshape(recs, rows, w_ref.shape[3])


def grouped_conv(padded, conv_weight, frame_rows):
    recs = padded.shape[0]
    groups_here, taps, group_in, group_out = conv_weight.shape
    span = frame_rows + taps - TAP_STEP
    grouped = padded.reshape(recs, padded.shape[1], groups_here, group_in).transpose(2, 0, 1, 3)
    expanded = jnp.concatenate([grouped[:, :, j : j + span] for j in range(TAP_STEP)], axis=3)
    out = pl.pallas_call(
        conv_body,
        grid=(groups_here,),
        in_specs=[
            pl.BlockSpec((1, recs, span, TAP_STEP * group_in), lambda g: (g, 0, 0, 0)),
            pl.BlockSpec((1, taps, group_in, group_out), lambda g: (g, 0, 0, 0)),
        ],
        out_specs=pl.BlockSpec((1, recs, frame_rows, group_out), lambda g: (g, 0, 0, 0)),
        out_shape=jax.ShapeDtypeStruct((groups_here, recs, frame_rows, group_out), jnp.float32),
        cost_estimate=pl.CostEstimate(
            flops=2 * groups_here * recs * frame_rows * taps * group_in * group_out,
            bytes_accessed=expanded.size * 2 + conv_weight.size * 2 + groups_here * recs * frame_rows * group_out * 4,
            transcendentals=0,
        ),
    )(expanded, conv_weight)
    return out.transpose(1, 2, 0, 3).reshape(recs, frame_rows, groups_here * group_out)


def gather_ring(x, axis, rows):
    size = lax.axis_size(axis)
    place = lax.axis_index(axis)
    pieces, starts = [x], [place * rows]
    for shift in range(1, size):
        pairs = [(i, (i + shift) % size) for i in range(size)]
        pieces.append(lax.ppermute(x, axis, pairs))
        starts.append(((place - shift) % size) * rows)
    return pieces, starts


def attend(carry, piece, start, queries, own_length):
    best, total, accum = carry
    keys_part, vals_part = piece
    count = keys_part.shape[0]
    head_count = queries.shape[1]
    keys_part = keys_part.reshape(count, head_count, HD)
    vals_part = vals_part.reshape(count, head_count, HD)
    scores = jnp.einsum(
        "fhd,nhd->fhn", queries, keys_part, preferred_element_type=jnp.float32
    ) / math.sqrt(HD)
    valid = (start + jnp.arange(count, dtype=jnp.int32) < own_length)[None, None, :]
    scores = jnp.where(valid, scores, -1e30)
    fresh = jnp.maximum(best, jnp.max(scores, axis=2))
    weights = jnp.where(valid, jnp.exp(scores - fresh[:, :, None]), 0.0)
    factor = jnp.exp(best - fresh)
    total = total * factor + jnp.sum(weights, axis=2)
    accum = accum * factor[:, :, None] + jnp.einsum(
        "fhn,nhd->fhd", weights.astype(jnp.bfloat16), vals_part, preferred_element_type=jnp.float32
    )
    return (fresh, total, accum)


def start_state(rows, heads_here):
    return (
        jnp.full((rows, heads_here), -1e30, jnp.float32),
        jnp.zeros((rows, heads_here), jnp.float32),
        jnp.zeros((rows, heads_here, HD), jnp.float32),
    )


def blockwise(carry, all_keys, all_vals, queries, own_length, block_rows):
    block_count = all_keys.shape[0] // block_rows

    def block_step(state, index):
        begin = index * block_rows
        piece = (
            lax.dynamic_slice_in_dim(all_keys, begin, block_rows, 0),
            lax.dynamic_slice_in_dim(all_vals, begin, block_rows, 0),
        )
        return (attend(state, piece, begin, queries, own_length), None)

    final, unused = lax.scan(block_step, carry, jnp.arange(block_count, dtype=jnp.int32))
    return final


def finish(final, query_pos, own_length):
    best, total, accum = final
    result = accum / total[:, :, None]
    query_live = (query_pos < own_length)[:, None, None]
    result = jnp.where(query_live, result, 0.0)
    return result.reshape(result.shape[0], result.shape[1] * HD).astype(jnp.bfloat16)


def per_device(
    frames_in, lengths, conv_weight, conv_bias, norm_gain, norm_shift, w_query, w_key, w_value
):
    record_count, frame_rows, channels = frames_in.shape
    ctx_place = lax.axis_index("ctx")
    positions = ctx_place * frame_rows + jnp.arange(frame_rows, dtype=jnp.int32)
    live = positions[None, :] < lengths[:, None]
    masked = jnp.where(live[:, :, None], frames_in, jnp.zeros((), frames_in.dtype))
    groups_here, kernel_width, group_in, group_out = conv_weight.shape
    half_width = kernel_width // 2
    padded = padded_2(masked, (("ctx", 1),), half_width)
    conv_out = grouped_conv(padded, conv_weight, frame_rows)
    hidden = (
        masked.astype(jnp.float32)
        + jax.nn.gelu(conv_out + conv_bias.astype(jnp.float32), approximate=False)
    ).astype(jnp.bfloat16)
    record = lax.all_to_all(hidden, "fsdp", split_axis=0, concat_axis=2, tiled=True)
    own_length = lax.dynamic_index_in_dim(lengths, lax.axis_index("fsdp"), 0, keepdims=False)
    flat = record[0].astype(jnp.float32)
    centre = jnp.mean(flat, axis=1, keepdims=True)
    spread = jnp.mean((flat - centre) ** 2, axis=1, keepdims=True)
    normed = ((flat - centre) / jnp.sqrt(spread + 1e-05) * norm_gain + norm_shift).astype(
        jnp.bfloat16
    )
    query_flat = jnp.dot(normed, w_query, preferred_element_type=jnp.float32).astype(jnp.bfloat16)
    key_flat = jnp.dot(normed, w_key, preferred_element_type=jnp.float32).astype(jnp.bfloat16)
    val_flat = jnp.dot(normed, w_value, preferred_element_type=jnp.float32).astype(jnp.bfloat16)
    head_count = query_flat.shape[1] // HD
    width = key_flat.shape[1]
    both = jnp.concatenate([key_flat, val_flat], axis=1)
    pieces, starts = gather_ring(both, "ctx", frame_rows)
    whole = jnp.concatenate(pieces, axis=0)
    key_pos = jnp.concatenate(
        [start + jnp.arange(frame_rows, dtype=jnp.int32) for start in starts]
    )
    queries = query_flat.reshape(frame_rows, head_count, HD)
    keys = whole[:, :width].reshape(-1, head_count, HD)
    vals = whole[:, width:].reshape(-1, head_count, HD)
    scores = jnp.einsum(
        "fhd,nhd->hfn", queries, keys, preferred_element_type=jnp.float32
    ) / math.sqrt(HD)
    valid = (key_pos < own_length)[None, None, :]
    scores = jnp.where(valid, scores, -1e30)
    rowmax = jnp.max(scores, axis=2, keepdims=True)
    weights = jnp.where(valid, jnp.exp(scores - rowmax), 0.0)
    total = jnp.sum(weights, axis=2, keepdims=True)
    summed = jnp.einsum(
        "hfn,nhd->hfd", weights.astype(jnp.bfloat16), vals, preferred_element_type=jnp.float32
    )
    out = summed / total
    query_live = (positions < own_length)[None, :, None]
    out = jnp.where(query_live, out, 0.0).transpose(1, 0, 2)
    result = out.reshape(1, frame_rows, head_count * HD).astype(jnp.bfloat16)
    return (hidden, result)


def solution(mesh):
    in_specs = (
        P("rep", "ctx", "fsdp"),
        P("rep"),
        P("fsdp", None, None, None),
        P("fsdp"),
        P(),
        P(),
        P(),
        P(),
        P(),
    )
    out_specs = (P("rep", "ctx", "fsdp"), P(("rep", "fsdp"), "ctx", None))
    return jax.shard_map(
        per_device, mesh=mesh, in_specs=in_specs, out_specs=out_specs, check_vma=False
    )
```

```python
import math

import jax
import jax.numpy as jnp
from jax import lax
from jax.sharding import PartitionSpec as P
from jax.experimental import pallas as pl
from jax.experimental.pallas import tpu as pltpu

HD = 64


def padded_2(x, sides, width):
    for axis, dim in sides:
        size, length = (lax.axis_size(axis), x.shape[dim])
        up = [(i, (i + 1) % size) for i in range(size - 1)]
        down = [(j, i) for i, j in up]
        last = lax.slice_in_dim(x, length - width, length, axis=dim)
        first = lax.slice_in_dim(x, 0, width, axis=dim)
        before = lax.ppermute(last, axis, up)
        after = lax.ppermute(first, axis, down)
        x = jnp.concatenate([before, x, after], axis=dim)
    return x


def conv_body(x_ref, w_ref, out_ref):
    recs, chans, lanes = x_ref.shape[1], x_ref.shape[2], x_ref.shape[3]
    taps = w_ref.shape[3]
    rows = out_ref.shape[2]
    outs = w_ref.shape[2]

    def octet_step(q, acc):
        base = pl.multiple_of(q * 8, 8)
        hankels = []
        for r in range(recs):
            block = x_ref[0, r, pl.ds(base, 8), :]
            per_chan = []
            for c in range(8):
                row = jnp.broadcast_to(block[c : c + 1, :], (rows, lanes))
                rolled = pltpu.roll(row, 0, 1, stride=1, stride_axis=0)
                per_chan.append(rolled[:, :taps].astype(jnp.bfloat16))
            hankels.append(per_chan)
        for pair in range(4):
            lhs = jnp.concatenate(
                [jnp.concatenate(hankels[r][2 * pair : 2 * pair + 2], axis=1) for r in range(recs)],
                axis=0,
            )
            rhs = jnp.concatenate(
                [w_ref[0, base + 2 * pair], w_ref[0, base + 2 * pair + 1]], axis=1
            )
            acc = acc + lax.dot_general(
                lhs, rhs, (((1,), (1,)), ((), ())), preferred_element_type=jnp.float32
            )
        return acc

    acc = lax.fori_loop(0, chans // 8, octet_step, jnp.zeros((recs * rows, outs), jnp.float32))
    out_ref[0] = acc.reshape(recs, rows, outs)


def hankel_conv(xt, wv, rows):
    groups, recs, chans, lanes = xt.shape
    taps, outs = wv.shape[3], wv.shape[2]
    return pl.pallas_call(
        conv_body,
        grid=(groups,),
        in_specs=[pl.BlockSpec((1, recs, chans, lanes), lambda g: (g, 0, 0, 0)),
                  pl.BlockSpec((1, chans, outs, taps), lambda g: (g, 0, 0, 0))],
        out_specs=pl.BlockSpec((1, recs, rows, outs), lambda g: (g, 0, 0, 0)),
        out_shape=jax.ShapeDtypeStruct((groups, recs, rows, outs), jnp.float32),
        cost_estimate=pl.CostEstimate(
            flops=2 * groups * recs * rows * taps * chans * outs,
            bytes_accessed=xt.size * 4 + wv.size * 2 + groups * recs * rows * outs * 4,
            transcendentals=0,
        ),
    )(xt, wv)


def grouped_conv(padded, conv_weight, frame_rows):
    recs, span = padded.shape[0], padded.shape[1]
    groups_here, taps, group_in, group_out = conv_weight.shape
    lanes = -(-(frame_rows + taps - 1) // 128) * 128
    grouped = jnp.pad(padded, ((0, 0), (0, lanes - span), (0, 0)))
    grouped = jnp.roll(grouped, 1 - frame_rows, axis=1)
    grouped = grouped.reshape(recs, lanes, groups_here, group_in).transpose(2, 0, 3, 1)
    out = hankel_conv(grouped.astype(jnp.float32), jnp.transpose(conv_weight, (0, 2, 3, 1)), frame_rows)
    out = jnp.flip(out, axis=2)
    return out.transpose(1, 2, 0, 3).reshape(recs, frame_rows, groups_here * group_out)


def gather_ring(x, axis, rows):
    size = lax.axis_size(axis)
    place = lax.axis_index(axis)
    pieces, starts = [x], [place * rows]
    for shift in range(1, size):
        pairs = [(i, (i + shift) % size) for i in range(size)]
        pieces.append(lax.ppermute(x, axis, pairs))
        starts.append(((place - shift) % size) * rows)
    return pieces, starts


def attend(carry, piece, start, queries, own_length):
    best, total, accum = carry
    keys_part, vals_part = piece
    count = keys_part.shape[0]
    head_count = queries.shape[1]
    keys_part = keys_part.reshape(count, head_count, HD)
    vals_part = vals_part.reshape(count, head_count, HD)
    scores = jnp.einsum(
        "fhd,nhd->fhn", queries, keys_part, preferred_element_type=jnp.float32
    ) / math.sqrt(HD)
    valid = (start + jnp.arange(count, dtype=jnp.int32) < own_length)[None, None, :]
    scores = jnp.where(valid, scores, -1e30)
    fresh = jnp.maximum(best, jnp.max(scores, axis=2))
    weights = jnp.where(valid, jnp.exp(scores - fresh[:, :, None]), 0.0)
    factor = jnp.exp(best - fresh)
    total = total * factor + jnp.sum(weights, axis=2)
    accum = accum * factor[:, :, None] + jnp.einsum(
        "fhn,nhd->fhd", weights.astype(jnp.bfloat16), vals_part, preferred_element_type=jnp.float32
    )
    return (fresh, total, accum)


def start_state(rows, heads_here):
    return (
        jnp.full((rows, heads_here), -1e30, jnp.float32),
        jnp.zeros((rows, heads_here), jnp.float32),
        jnp.zeros((rows, heads_here, HD), jnp.float32),
    )


def blockwise(carry, all_keys, all_vals, queries, own_length, block_rows):
    block_count = all_keys.shape[0] // block_rows

    def block_step(state, index):
        begin = index * block_rows
        piece = (
            lax.dynamic_slice_in_dim(all_keys, begin, block_rows, 0),
            lax.dynamic_slice_in_dim(all_vals, begin, block_rows, 0),
        )
        return (attend(state, piece, begin, queries, own_length), None)

    final, unused = lax.scan(block_step, carry, jnp.arange(block_count, dtype=jnp.int32))
    return final


def finish(final, query_pos, own_length):
    best, total, accum = final
    result = accum / total[:, :, None]
    query_live = (query_pos < own_length)[:, None, None]
    result = jnp.where(query_live, result, 0.0)
    return result.reshape(result.shape[0], result.shape[1] * HD).astype(jnp.bfloat16)


def per_device(
    frames_in, lengths, conv_weight, conv_bias, norm_gain, norm_shift, w_query, w_key, w_value
):
    record_count, frame_rows, channels = frames_in.shape
    ctx_place = lax.axis_index("ctx")
    positions = ctx_place * frame_rows + jnp.arange(frame_rows, dtype=jnp.int32)
    live = positions[None, :] < lengths[:, None]
    masked = jnp.where(live[:, :, None], frames_in, jnp.zeros((), frames_in.dtype))
    groups_here, kernel_width, group_in, group_out = conv_weight.shape
    half_width = kernel_width // 2
    padded = padded_2(masked, (("ctx", 1),), half_width)
    conv_out = grouped_conv(padded, conv_weight, frame_rows)
    hidden = (
        masked.astype(jnp.float32)
        + jax.nn.gelu(conv_out + conv_bias.astype(jnp.float32), approximate=False)
    ).astype(jnp.bfloat16)
    record = lax.all_to_all(hidden, "fsdp", split_axis=0, concat_axis=2, tiled=True)
    own_length = lax.dynamic_index_in_dim(lengths, lax.axis_index("fsdp"), 0, keepdims=False)
    flat = record[0].astype(jnp.float32)
    centre = jnp.mean(flat, axis=1, keepdims=True)
    spread = jnp.mean((flat - centre) ** 2, axis=1, keepdims=True)
    normed = ((flat - centre) / jnp.sqrt(spread + 1e-05) * norm_gain + norm_shift).astype(
        jnp.bfloat16
    )
    query_flat = jnp.dot(normed, w_query, preferred_element_type=jnp.float32).astype(jnp.bfloat16)
    key_flat = jnp.dot(normed, w_key, preferred_element_type=jnp.float32).astype(jnp.bfloat16)
    val_flat = jnp.dot(normed, w_value, preferred_element_type=jnp.float32).astype(jnp.bfloat16)
    head_count = query_flat.shape[1] // HD
    width = key_flat.shape[1]
    both = jnp.concatenate([key_flat, val_flat], axis=1)
    pieces, starts = gather_ring(both, "ctx", frame_rows)
    whole = jnp.concatenate(pieces, axis=0)
    key_pos = jnp.concatenate(
        [start + jnp.arange(frame_rows, dtype=jnp.int32) for start in starts]
    )
    queries = query_flat.reshape(frame_rows, head_count, HD)
    keys = whole[:, :width].reshape(-1, head_count, HD)
    vals = whole[:, width:].reshape(-1, head_count, HD)
    scores = jnp.einsum(
        "fhd,nhd->hfn", queries, keys, preferred_element_type=jnp.float32
    ) / math.sqrt(HD)
    valid = (key_pos < own_length)[None, None, :]
    scores = jnp.where(valid, scores, -1e30)
    rowmax = jnp.max(scores, axis=2, keepdims=True)
    weights = jnp.where(valid, jnp.exp(scores - rowmax), 0.0)
    total = jnp.sum(weights, axis=2, keepdims=True)
    summed = jnp.einsum(
        "hfn,nhd->hfd", weights.astype(jnp.bfloat16), vals, preferred_element_type=jnp.float32
    )
    out = summed / total
    query_live = (positions < own_length)[None, :, None]
    out = jnp.where(query_live, out, 0.0).transpose(1, 0, 2)
    result = out.reshape(1, frame_rows, head_count * HD).astype(jnp.bfloat16)
    return (hidden, result)


def solution(mesh):
    in_specs = (
        P("rep", "ctx", "fsdp"),
        P("rep"),
        P("fsdp", None, None, None),
        P("fsdp"),
        P(),
        P(),
        P(),
        P(),
        P(),
    )
    out_specs = (P("rep", "ctx", "fsdp"), P(("rep", "fsdp"), "ctx", None))
    return jax.shard_map(
        per_device, mesh=mesh, in_specs=in_specs, out_specs=out_specs, check_vma=False
    )
```

```python
import math

import jax
import jax.numpy as jnp
from jax import lax
from jax.sharding import PartitionSpec as P
from jax.experimental import pallas as pl
from jax.experimental.pallas import tpu as pltpu

HD = 64


def padded_2(x, sides, width):
    for axis, dim in sides:
        size, length = (lax.axis_size(axis), x.shape[dim])
        up = [(i, (i + 1) % size) for i in range(size - 1)]
        down = [(j, i) for i, j in up]
        last = lax.slice_in_dim(x, length - width, length, axis=dim)
        first = lax.slice_in_dim(x, 0, width, axis=dim)
        before = lax.ppermute(last, axis, up)
        after = lax.ppermute(first, axis, down)
        x = jnp.concatenate([before, x, after], axis=dim)
    return x


def conv_body(x_ref, w_ref, out_ref):
    recs, chans, lanes = x_ref.shape[1], x_ref.shape[2], x_ref.shape[3]
    taps = w_ref.shape[3]
    rows = out_ref.shape[2]
    outs = w_ref.shape[2]

    def octet_step(q, acc):
        base = pl.multiple_of(q * 8, 8)
        hankels = []
        for r in range(recs):
            block = x_ref[0, r, pl.ds(base, 8), :]
            per_chan = []
            for c in range(8):
                row = jnp.broadcast_to(block[c : c + 1, :], (rows, lanes))
                rolled = pltpu.roll(row, 0, 1, stride=1, stride_axis=0)
                per_chan.append(rolled[:, :taps].astype(jnp.bfloat16))
            hankels.append(per_chan)
        for pair in range(4):
            lhs = jnp.concatenate(
                [jnp.concatenate(hankels[r][2 * pair : 2 * pair + 2], axis=1) for r in range(recs)],
                axis=0,
            )
            rhs = jnp.concatenate(
                [w_ref[0, base + 2 * pair], w_ref[0, base + 2 * pair + 1]], axis=1
            )
            acc = acc + lax.dot_general(
                lhs, rhs, (((1,), (1,)), ((), ())), preferred_element_type=jnp.float32
            )
        return acc

    acc = lax.fori_loop(0, chans // 8, octet_step, jnp.zeros((recs * rows, outs), jnp.float32))
    across = lax.broadcasted_iota(jnp.int32, (rows, rows), 0) + lax.broadcasted_iota(
        jnp.int32, (rows, rows), 1
    )
    flip = jnp.where(across == rows - 1, 1.0, 0.0).astype(jnp.bfloat16)
    for r in range(recs):
        part = acc[r * rows : (r + 1) * rows]
        high = part.astype(jnp.bfloat16)
        rest = part - high.astype(jnp.float32)
        middle = rest.astype(jnp.bfloat16)
        low = (rest - middle.astype(jnp.float32)).astype(jnp.bfloat16)
        total = jnp.dot(flip, high, preferred_element_type=jnp.float32)
        total = total + jnp.dot(flip, middle, preferred_element_type=jnp.float32)
        out_ref[0, r] = total + jnp.dot(flip, low, preferred_element_type=jnp.float32)


def hankel_conv(xt, wv, rows):
    groups, recs, chans, lanes = xt.shape
    taps, outs = wv.shape[3], wv.shape[2]
    return pl.pallas_call(
        conv_body,
        grid=(groups,),
        in_specs=[pl.BlockSpec((1, recs, chans, lanes), lambda g: (g, 0, 0, 0)),
                  pl.BlockSpec((1, chans, outs, taps), lambda g: (g, 0, 0, 0))],
        out_specs=pl.BlockSpec((1, recs, rows, outs), lambda g: (g, 0, 0, 0)),
        out_shape=jax.ShapeDtypeStruct((groups, recs, rows, outs), jnp.float32),
        cost_estimate=pl.CostEstimate(
            flops=2 * groups * recs * rows * taps * chans * outs,
            bytes_accessed=xt.size * 4 + wv.size * 2 + groups * recs * rows * outs * 4,
            transcendentals=0,
        ),
    )(xt, wv)


def grouped_conv(padded, conv_weight, frame_rows):
    recs, span = padded.shape[0], padded.shape[1]
    groups_here, taps, group_in, group_out = conv_weight.shape
    lanes = -(-(frame_rows + taps - 1) // 128) * 128
    grouped = jnp.pad(padded, ((0, 0), (0, lanes - span), (0, 0)))
    grouped = jnp.roll(grouped, 1 - frame_rows, axis=1)
    grouped = grouped.reshape(recs, lanes, groups_here, group_in).transpose(2, 0, 3, 1)
    out = hankel_conv(grouped.astype(jnp.float32), jnp.transpose(conv_weight, (0, 2, 3, 1)), frame_rows)
    return out.transpose(1, 2, 0, 3).reshape(recs, frame_rows, groups_here * group_out)


def gather_ring(x, axis, rows):
    size = lax.axis_size(axis)
    place = lax.axis_index(axis)
    ups = [(i, i + 1) for i in range(size - 1)]
    downs = [(i + 1, i) for i in range(size - 1)]
    from_below, from_above = [x], [x]
    for step in range(1, size):
        from_below.append(lax.ppermute(from_below[-1], axis, ups))
        from_above.append(lax.ppermute(from_above[-1], axis, downs))
    pieces, starts = [x], [place * rows]
    for offset in range(1, size):
        above = place + offset < size
        pieces.append(jnp.where(above, from_above[offset], from_below[size - offset]))
        starts.append(((place + offset) % size) * rows)
    return pieces, starts


def attend(carry, piece, start, queries, own_length):
    best, total, accum = carry
    keys_part, vals_part = piece
    count = keys_part.shape[0]
    head_count = queries.shape[1]
    keys_part = keys_part.reshape(count, head_count, HD)
    vals_part = vals_part.reshape(count, head_count, HD)
    scores = jnp.einsum(
        "fhd,nhd->fhn", queries, keys_part, preferred_element_type=jnp.float32
    ) / math.sqrt(HD)
    valid = (start + jnp.arange(count, dtype=jnp.int32) < own_length)[None, None, :]
    scores = jnp.where(valid, scores, -1e30)
    fresh = jnp.maximum(best, jnp.max(scores, axis=2))
    weights = jnp.where(valid, jnp.exp(scores - fresh[:, :, None]), 0.0)
    factor = jnp.exp(best - fresh)
    total = total * factor + jnp.sum(weights, axis=2)
    accum = accum * factor[:, :, None] + jnp.einsum(
        "fhn,nhd->fhd", weights.astype(jnp.bfloat16), vals_part, preferred_element_type=jnp.float32
    )
    return (fresh, total, accum)


def start_state(rows, heads_here):
    return (
        jnp.full((rows, heads_here), -1e30, jnp.float32),
        jnp.zeros((rows, heads_here), jnp.float32),
        jnp.zeros((rows, heads_here, HD), jnp.float32),
    )


def blockwise(carry, all_keys, all_vals, queries, own_length, block_rows):
    block_count = all_keys.shape[0] // block_rows

    def block_step(state, index):
        begin = index * block_rows
        piece = (
            lax.dynamic_slice_in_dim(all_keys, begin, block_rows, 0),
            lax.dynamic_slice_in_dim(all_vals, begin, block_rows, 0),
        )
        return (attend(state, piece, begin, queries, own_length), None)

    final, unused = lax.scan(block_step, carry, jnp.arange(block_count, dtype=jnp.int32))
    return final


def finish(final, query_pos, own_length):
    best, total, accum = final
    result = accum / total[:, :, None]
    query_live = (query_pos < own_length)[:, None, None]
    result = jnp.where(query_live, result, 0.0)
    return result.reshape(result.shape[0], result.shape[1] * HD).astype(jnp.bfloat16)


def per_device(
    frames_in, lengths, conv_weight, conv_bias, norm_gain, norm_shift, w_query, w_key, w_value
):
    record_count, frame_rows, channels = frames_in.shape
    ctx_place = lax.axis_index("ctx")
    positions = ctx_place * frame_rows + jnp.arange(frame_rows, dtype=jnp.int32)
    live = positions[None, :] < lengths[:, None]
    masked = jnp.where(live[:, :, None], frames_in, jnp.zeros((), frames_in.dtype))
    groups_here, kernel_width, group_in, group_out = conv_weight.shape
    half_width = kernel_width // 2
    padded = padded_2(masked, (("ctx", 1),), half_width)
    conv_out = grouped_conv(padded, conv_weight, frame_rows)
    hidden = (
        masked.astype(jnp.float32)
        + jax.nn.gelu(conv_out + conv_bias.astype(jnp.float32), approximate=False)
    ).astype(jnp.bfloat16)
    record = lax.all_to_all(hidden, "fsdp", split_axis=0, concat_axis=2, tiled=True)
    own_length = lax.dynamic_index_in_dim(lengths, lax.axis_index("fsdp"), 0, keepdims=False)
    flat = record[0].astype(jnp.float32)
    centre = jnp.mean(flat, axis=1, keepdims=True)
    spread = jnp.mean((flat - centre) ** 2, axis=1, keepdims=True)
    normed = ((flat - centre) / jnp.sqrt(spread + 1e-05) * norm_gain + norm_shift).astype(
        jnp.bfloat16
    )
    query_flat = jnp.dot(normed, w_query, preferred_element_type=jnp.float32).astype(jnp.bfloat16)
    key_flat = jnp.dot(normed, w_key, preferred_element_type=jnp.float32).astype(jnp.bfloat16)
    val_flat = jnp.dot(normed, w_value, preferred_element_type=jnp.float32).astype(jnp.bfloat16)
    head_count = query_flat.shape[1] // HD
    width = key_flat.shape[1]
    both = jnp.concatenate([key_flat, val_flat], axis=1)
    pieces, starts = gather_ring(both, "ctx", frame_rows)
    whole = jnp.concatenate(pieces, axis=0)
    key_pos = jnp.concatenate(
        [start + jnp.arange(frame_rows, dtype=jnp.int32) for start in starts]
    )
    queries = query_flat.reshape(frame_rows, head_count, HD)
    keys = whole[:, :width].reshape(-1, head_count, HD)
    vals = whole[:, width:].reshape(-1, head_count, HD)
    scores = jnp.einsum(
        "fhd,nhd->hfn", queries, keys, preferred_element_type=jnp.float32
    ) / math.sqrt(HD)
    valid = (key_pos < own_length)[None, None, :]
    scores = jnp.where(valid, scores, -1e30)
    rowmax = jnp.max(scores, axis=2, keepdims=True)
    weights = jnp.where(valid, jnp.exp(scores - rowmax), 0.0)
    total = jnp.sum(weights, axis=2, keepdims=True)
    summed = jnp.einsum(
        "hfn,nhd->hfd", weights.astype(jnp.bfloat16), vals, preferred_element_type=jnp.float32
    )
    out = summed / total
    query_live = (positions < own_length)[None, :, None]
    out = jnp.where(query_live, out, 0.0).transpose(1, 0, 2)
    result = out.reshape(1, frame_rows, head_count * HD).astype(jnp.bfloat16)
    return (hidden, result)


def solution(mesh):
    in_specs = (
        P("rep", "ctx", "fsdp"),
        P("rep"),
        P("fsdp", None, None, None),
        P("fsdp"),
        P(),
        P(),
        P(),
        P(),
        P(),
    )
    out_specs = (P("rep", "ctx", "fsdp"), P(("rep", "fsdp"), "ctx", None))
    return jax.shard_map(
        per_device, mesh=mesh, in_specs=in_specs, out_specs=out_specs, check_vma=False
    )
```

```python
import math

import jax
import jax.numpy as jnp
from jax import lax
from jax.sharding import PartitionSpec as P
from jax.experimental import pallas as pl
from jax.experimental.pallas import tpu as pltpu

HD = 64


def padded_2(x, sides, width):
    for axis, dim in sides:
        size, length = (lax.axis_size(axis), x.shape[dim])
        up = [(i, (i + 1) % size) for i in range(size - 1)]
        down = [(j, i) for i, j in up]
        last = lax.slice_in_dim(x, length - width, length, axis=dim)
        first = lax.slice_in_dim(x, 0, width, axis=dim)
        before = lax.ppermute(last, axis, up)
        after = lax.ppermute(first, axis, down)
        x = jnp.concatenate([before, x, after], axis=dim)
    return x


def conv_body(x_ref, w_ref, out_ref):
    recs, chans, lanes = x_ref.shape[1], x_ref.shape[2], x_ref.shape[3]
    taps = w_ref.shape[3]
    rows = out_ref.shape[2]
    outs = w_ref.shape[2]

    def octet_step(q, acc):
        base = pl.multiple_of(q * 8, 8)
        hankels = []
        for r in range(recs):
            block = x_ref[0, r, pl.ds(base, 8), :]
            per_chan = []
            for c in range(8):
                row = jnp.broadcast_to(block[c : c + 1, :], (rows, lanes))
                rolled = pltpu.roll(row, 0, 1, stride=1, stride_axis=0)
                per_chan.append(rolled[:, :taps].astype(jnp.bfloat16))
            hankels.append(per_chan)
        for pair in range(4):
            lhs = jnp.concatenate(
                [jnp.concatenate(hankels[r][2 * pair : 2 * pair + 2], axis=1) for r in range(recs)],
                axis=0,
            )
            rhs = jnp.concatenate(
                [w_ref[0, base + 2 * pair], w_ref[0, base + 2 * pair + 1]], axis=1
            )
            acc = acc + lax.dot_general(
                lhs, rhs, (((1,), (1,)), ((), ())), preferred_element_type=jnp.float32
            )
        return acc

    acc = lax.fori_loop(0, chans // 8, octet_step, jnp.zeros((recs * rows, outs), jnp.float32))
    across = lax.broadcasted_iota(jnp.int32, (rows, rows), 0) + lax.broadcasted_iota(
        jnp.int32, (rows, rows), 1
    )
    flip = jnp.where(across == rows - 1, 1.0, 0.0).astype(jnp.bfloat16)
    for r in range(recs):
        part = acc[r * rows : (r + 1) * rows]
        high = part.astype(jnp.bfloat16)
        rest = part - high.astype(jnp.float32)
        middle = rest.astype(jnp.bfloat16)
        low = (rest - middle.astype(jnp.float32)).astype(jnp.bfloat16)
        total = jnp.dot(flip, high, preferred_element_type=jnp.float32)
        total = total + jnp.dot(flip, middle, preferred_element_type=jnp.float32)
        out_ref[0, r] = total + jnp.dot(flip, low, preferred_element_type=jnp.float32)


def hankel_conv(xt, wv, rows):
    groups, recs, chans, lanes = xt.shape
    taps, outs = wv.shape[3], wv.shape[2]
    return pl.pallas_call(
        conv_body,
        grid=(groups,),
        in_specs=[pl.BlockSpec((1, recs, chans, lanes), lambda g: (g, 0, 0, 0)),
                  pl.BlockSpec((1, chans, outs, taps), lambda g: (g, 0, 0, 0))],
        out_specs=pl.BlockSpec((1, recs, rows, outs), lambda g: (g, 0, 0, 0)),
        out_shape=jax.ShapeDtypeStruct((groups, recs, rows, outs), jnp.float32),
        cost_estimate=pl.CostEstimate(
            flops=2 * groups * recs * rows * taps * chans * outs,
            bytes_accessed=xt.size * 4 + wv.size * 2 + groups * recs * rows * outs * 4,
            transcendentals=0,
        ),
    )(xt, wv)


def grouped_conv(padded, conv_weight, frame_rows):
    recs, span = padded.shape[0], padded.shape[1]
    groups_here, taps, group_in, group_out = conv_weight.shape
    lanes = -(-(frame_rows + taps - 1) // 128) * 128
    grouped = jnp.pad(padded, ((0, 0), (0, lanes - span), (0, 0)))
    grouped = jnp.roll(grouped, 1 - frame_rows, axis=1)
    grouped = grouped.reshape(recs, lanes, groups_here, group_in).transpose(2, 0, 3, 1)
    out = hankel_conv(grouped.astype(jnp.float32), jnp.transpose(conv_weight, (0, 2, 3, 1)), frame_rows)
    return out.transpose(1, 2, 0, 3).reshape(recs, frame_rows, groups_here * group_out)


def gather_ring(x, axis, rows, offset):
    size = lax.axis_size(axis)
    place = lax.axis_index(axis)
    pieces, starts = [x], [place * rows + offset]
    for shift in range(1, size):
        pairs = [(i, (i + shift) % size) for i in range(size)]
        pieces.append(lax.ppermute(x, axis, pairs))
        starts.append(((place - shift) % size) * rows + offset)
    return pieces, starts


def attend(carry, piece, start, queries, own_length):
    best, total, accum = carry
    keys_part, vals_part = piece
    count = keys_part.shape[0]
    head_count = queries.shape[1]
    keys_part = keys_part.reshape(count, head_count, HD)
    vals_part = vals_part.reshape(count, head_count, HD)
    scores = jnp.einsum(
        "fhd,nhd->fhn", queries, keys_part, preferred_element_type=jnp.float32
    ) / math.sqrt(HD)
    valid = (start + jnp.arange(count, dtype=jnp.int32) < own_length)[None, None, :]
    scores = jnp.where(valid, scores, -1e30)
    fresh = jnp.maximum(best, jnp.max(scores, axis=2))
    weights = jnp.where(valid, jnp.exp(scores - fresh[:, :, None]), 0.0)
    factor = jnp.exp(best - fresh)
    total = total * factor + jnp.sum(weights, axis=2)
    accum = accum * factor[:, :, None] + jnp.einsum(
        "fhn,nhd->fhd", weights.astype(jnp.bfloat16), vals_part, preferred_element_type=jnp.float32
    )
    return (fresh, total, accum)


def start_state(rows, heads_here):
    return (
        jnp.full((rows, heads_here), -1e30, jnp.float32),
        jnp.zeros((rows, heads_here), jnp.float32),
        jnp.zeros((rows, heads_here, HD), jnp.float32),
    )


def blockwise(carry, all_keys, all_vals, queries, own_length, block_rows):
    block_count = all_keys.shape[0] // block_rows

    def block_step(state, index):
        begin = index * block_rows
        piece = (
            lax.dynamic_slice_in_dim(all_keys, begin, block_rows, 0),
            lax.dynamic_slice_in_dim(all_vals, begin, block_rows, 0),
        )
        return (attend(state, piece, begin, queries, own_length), None)

    final, unused = lax.scan(block_step, carry, jnp.arange(block_count, dtype=jnp.int32))
    return final


def finish(final, query_pos, own_length):
    best, total, accum = final
    result = accum / total[:, :, None]
    query_live = (query_pos < own_length)[:, None, None]
    result = jnp.where(query_live, result, 0.0)
    return result.reshape(result.shape[0], result.shape[1] * HD).astype(jnp.bfloat16)


def per_device(
    frames_in, lengths, conv_weight, conv_bias, norm_gain, norm_shift, w_query, w_key, w_value
):
    record_count, frame_rows, channels = frames_in.shape
    ctx_place = lax.axis_index("ctx")
    positions = ctx_place * frame_rows + jnp.arange(frame_rows, dtype=jnp.int32)
    live = positions[None, :] < lengths[:, None]
    masked = jnp.where(live[:, :, None], frames_in, jnp.zeros((), frames_in.dtype))
    groups_here, kernel_width, group_in, group_out = conv_weight.shape
    half_width = kernel_width // 2
    padded = padded_2(masked, (("ctx", 1),), half_width)
    own_length = lax.dynamic_index_in_dim(lengths, lax.axis_index("fsdp"), 0, keepdims=False)
    chunks = 2 if frame_rows % 16 == 0 else 1
    rows = frame_rows // chunks
    hidden_parts, query_parts, pieces, starts = [], [], [], []
    size_of_ring = lax.axis_size("ctx")
    for chunk in range(chunks):
        low = chunk * rows
        window = padded[:, low : low + rows + kernel_width - 1]
        if pieces:
            window, unused = lax.optimization_barrier((window, pieces[-size_of_ring]))
        conv_out = grouped_conv(window, conv_weight, rows)
        hidden_part = (
            masked[:, low : low + rows].astype(jnp.float32)
            + jax.nn.gelu(conv_out + conv_bias.astype(jnp.float32), approximate=False)
        ).astype(jnp.bfloat16)
        hidden_parts.append(hidden_part)
        record = lax.all_to_all(hidden_part, "fsdp", split_axis=0, concat_axis=2, tiled=True)
        flat = record[0].astype(jnp.float32)
        centre = jnp.mean(flat, axis=1, keepdims=True)
        spread = jnp.mean((flat - centre) ** 2, axis=1, keepdims=True)
        normed = ((flat - centre) / jnp.sqrt(spread + 1e-05) * norm_gain + norm_shift).astype(
            jnp.bfloat16
        )
        query_parts.append(
            jnp.dot(normed, w_query, preferred_element_type=jnp.float32).astype(jnp.bfloat16)
        )
        key_flat = jnp.dot(normed, w_key, preferred_element_type=jnp.float32).astype(jnp.bfloat16)
        val_flat = jnp.dot(normed, w_value, preferred_element_type=jnp.float32).astype(jnp.bfloat16)
        width = key_flat.shape[1]
        both = jnp.concatenate([key_flat, val_flat], axis=1)
        got, at = gather_ring(both, "ctx", frame_rows, low)
        pieces += got
        starts += at
    hidden = jnp.concatenate(hidden_parts, axis=1)
    query_flat = jnp.concatenate(query_parts, axis=0)
    head_count = query_flat.shape[1] // HD
    whole = jnp.concatenate(pieces, axis=0)
    key_pos = jnp.concatenate([start + jnp.arange(rows, dtype=jnp.int32) for start in starts])
    queries = query_flat.reshape(frame_rows, head_count, HD)
    keys = whole[:, :width].reshape(-1, head_count, HD)
    vals = whole[:, width:].reshape(-1, head_count, HD)
    scores = jnp.einsum(
        "fhd,nhd->hfn", queries, keys, preferred_element_type=jnp.float32
    ) / math.sqrt(HD)
    valid = (key_pos < own_length)[None, None, :]
    scores = jnp.where(valid, scores, -1e30)
    rowmax = jnp.max(scores, axis=2, keepdims=True)
    weights = jnp.where(valid, jnp.exp(scores - rowmax), 0.0)
    total = jnp.sum(weights, axis=2, keepdims=True)
    summed = jnp.einsum(
        "hfn,nhd->hfd", weights.astype(jnp.bfloat16), vals, preferred_element_type=jnp.float32
    )
    out = summed / total
    query_live = (positions < own_length)[None, :, None]
    out = jnp.where(query_live, out, 0.0).transpose(1, 0, 2)
    result = out.reshape(1, frame_rows, head_count * HD).astype(jnp.bfloat16)
    return (hidden, result)


def solution(mesh):
    in_specs = (
        P("rep", "ctx", "fsdp"),
        P("rep"),
        P("fsdp", None, None, None),
        P("fsdp"),
        P(),
        P(),
        P(),
        P(),
        P(),
    )
    out_specs = (P("rep", "ctx", "fsdp"), P(("rep", "fsdp"), "ctx", None))
    return jax.shard_map(
        per_device, mesh=mesh, in_specs=in_specs, out_specs=out_specs, check_vma=False
    )
```

```python
import math

import jax
import jax.numpy as jnp
from jax import lax
from jax.sharding import PartitionSpec as P
from jax.experimental import pallas as pl
from jax.experimental.pallas import tpu as pltpu

HD = 64


def padded_2(x, sides, width):
    for axis, dim in sides:
        size, length = (lax.axis_size(axis), x.shape[dim])
        up = [(i, (i + 1) % size) for i in range(size - 1)]
        down = [(j, i) for i, j in up]
        last = lax.slice_in_dim(x, length - width, length, axis=dim)
        first = lax.slice_in_dim(x, 0, width, axis=dim)
        before = lax.ppermute(last, axis, up)
        after = lax.ppermute(first, axis, down)
        x = jnp.concatenate([before, x, after], axis=dim)
    return x


def conv_body(x_ref, w_ref, out_ref):
    recs, chans, lanes = x_ref.shape[1], x_ref.shape[2], x_ref.shape[3]
    taps = w_ref.shape[3]
    rows = out_ref.shape[2]
    outs = w_ref.shape[2]

    def octet_step(q, acc):
        base = pl.multiple_of(q * 8, 8)
        hankels = []
        for r in range(recs):
            block = x_ref[0, r, pl.ds(base, 8), :]
            per_chan = []
            for c in range(8):
                row = jnp.broadcast_to(block[c : c + 1, :], (taps, lanes))
                rolled = pltpu.roll(row, 0, 1, stride=1, stride_axis=0)
                per_chan.append(rolled[:, :rows].astype(jnp.bfloat16))
            hankels.append(per_chan)
        for pair in range(4):
            rhs = jnp.concatenate(
                [
                    jnp.concatenate([hankels[r][2 * pair + half] for r in range(recs)], axis=1)
                    for half in range(2)
                ],
                axis=0,
            )
            lhs = jnp.concatenate(
                [w_ref[0, base + 2 * pair], w_ref[0, base + 2 * pair + 1]], axis=1
            )
            acc = acc + jnp.dot(lhs, rhs, preferred_element_type=jnp.float32)
        return acc

    acc = lax.fori_loop(0, chans // 8, octet_step, jnp.zeros((outs, recs * rows), jnp.float32))
    across = lax.broadcasted_iota(jnp.int32, (rows, rows), 0) + lax.broadcasted_iota(
        jnp.int32, (rows, rows), 1
    )
    flip = jnp.where(across == rows - 1, 1.0, 0.0).astype(jnp.bfloat16)
    dims = (((1,), (1,)), ((), ()))
    for r in range(recs):
        part = acc[:, r * rows : (r + 1) * rows]
        high = part.astype(jnp.bfloat16)
        rest = part - high.astype(jnp.float32)
        middle = rest.astype(jnp.bfloat16)
        low = (rest - middle.astype(jnp.float32)).astype(jnp.bfloat16)
        total = lax.dot_general(flip, high, dims, preferred_element_type=jnp.float32)
        total = total + lax.dot_general(flip, middle, dims, preferred_element_type=jnp.float32)
        out_ref[0, r] = total + lax.dot_general(flip, low, dims, preferred_element_type=jnp.float32)


def hankel_conv(xt, wv, rows):
    groups, recs, chans, lanes = xt.shape
    taps, outs = wv.shape[3], wv.shape[2]
    return pl.pallas_call(
        conv_body,
        grid=(groups,),
        in_specs=[pl.BlockSpec((1, recs, chans, lanes), lambda g: (g, 0, 0, 0)),
                  pl.BlockSpec((1, chans, outs, taps), lambda g: (g, 0, 0, 0))],
        out_specs=pl.BlockSpec((1, recs, rows, outs), lambda g: (g, 0, 0, 0)),
        out_shape=jax.ShapeDtypeStruct((groups, recs, rows, outs), jnp.float32),
        cost_estimate=pl.CostEstimate(
            flops=2 * groups * recs * rows * taps * chans * outs,
            bytes_accessed=xt.size * 4 + wv.size * 2 + groups * recs * rows * outs * 4,
            transcendentals=0,
        ),
    )(xt, wv)


def grouped_conv(padded, conv_weight, frame_rows):
    recs, span = padded.shape[0], padded.shape[1]
    groups_here, taps, group_in, group_out = conv_weight.shape
    lanes = -(-(frame_rows + taps - 1) // 128) * 128
    grouped = jnp.pad(padded, ((0, 0), (0, lanes - span), (0, 0)))
    grouped = jnp.roll(jnp.flip(grouped, axis=1), frame_rows - lanes, axis=1)
    grouped = grouped.reshape(recs, lanes, groups_here, group_in).transpose(2, 0, 3, 1)
    out = hankel_conv(grouped.astype(jnp.float32), jnp.transpose(conv_weight, (0, 2, 3, 1)), frame_rows)
    return out.transpose(1, 2, 0, 3).reshape(recs, frame_rows, groups_here * group_out)


def gather_ring(x, axis, rows):
    size = lax.axis_size(axis)
    place = lax.axis_index(axis)
    pieces, starts = [x], [place * rows]
    for shift in range(1, size):
        pairs = [(i, (i + shift) % size) for i in range(size)]
        pieces.append(lax.ppermute(x, axis, pairs))
        starts.append(((place - shift) % size) * rows)
    return pieces, starts


def attend(carry, piece, start, queries, own_length):
    best, total, accum = carry
    keys_part, vals_part = piece
    count = keys_part.shape[0]
    head_count = queries.shape[1]
    keys_part = keys_part.reshape(count, head_count, HD)
    vals_part = vals_part.reshape(count, head_count, HD)
    scores = jnp.einsum(
        "fhd,nhd->fhn", queries, keys_part, preferred_element_type=jnp.float32
    ) / math.sqrt(HD)
    valid = (start + jnp.arange(count, dtype=jnp.int32) < own_length)[None, None, :]
    scores = jnp.where(valid, scores, -1e30)
    fresh = jnp.maximum(best, jnp.max(scores, axis=2))
    weights = jnp.where(valid, jnp.exp(scores - fresh[:, :, None]), 0.0)
    factor = jnp.exp(best - fresh)
    total = total * factor + jnp.sum(weights, axis=2)
    accum = accum * factor[:, :, None] + jnp.einsum(
        "fhn,nhd->fhd", weights.astype(jnp.bfloat16), vals_part, preferred_element_type=jnp.float32
    )
    return (fresh, total, accum)


def start_state(rows, heads_here):
    return (
        jnp.full((rows, heads_here), -1e30, jnp.float32),
        jnp.zeros((rows, heads_here), jnp.float32),
        jnp.zeros((rows, heads_here, HD), jnp.float32),
    )


def blockwise(carry, all_keys, all_vals, queries, own_length, block_rows):
    block_count = all_keys.shape[0] // block_rows

    def block_step(state, index):
        begin = index * block_rows
        piece = (
            lax.dynamic_slice_in_dim(all_keys, begin, block_rows, 0),
            lax.dynamic_slice_in_dim(all_vals, begin, block_rows, 0),
        )
        return (attend(state, piece, begin, queries, own_length), None)

    final, unused = lax.scan(block_step, carry, jnp.arange(block_count, dtype=jnp.int32))
    return final


def finish(final, query_pos, own_length):
    best, total, accum = final
    result = accum / total[:, :, None]
    query_live = (query_pos < own_length)[:, None, None]
    result = jnp.where(query_live, result, 0.0)
    return result.reshape(result.shape[0], result.shape[1] * HD).astype(jnp.bfloat16)


def per_device(
    frames_in, lengths, conv_weight, conv_bias, norm_gain, norm_shift, w_query, w_key, w_value
):
    record_count, frame_rows, channels = frames_in.shape
    ctx_place = lax.axis_index("ctx")
    positions = ctx_place * frame_rows + jnp.arange(frame_rows, dtype=jnp.int32)
    live = positions[None, :] < lengths[:, None]
    masked = jnp.where(live[:, :, None], frames_in, jnp.zeros((), frames_in.dtype))
    groups_here, kernel_width, group_in, group_out = conv_weight.shape
    half_width = kernel_width // 2
    padded = padded_2(masked, (("ctx", 1),), half_width)
    conv_out = grouped_conv(padded, conv_weight, frame_rows)
    hidden = (
        masked.astype(jnp.float32)
        + jax.nn.gelu(conv_out + conv_bias.astype(jnp.float32), approximate=False)
    ).astype(jnp.bfloat16)
    record = lax.all_to_all(hidden, "fsdp", split_axis=0, concat_axis=2, tiled=True)
    own_length = lax.dynamic_index_in_dim(lengths, lax.axis_index("fsdp"), 0, keepdims=False)
    flat = record[0].astype(jnp.float32)
    centre = jnp.mean(flat, axis=1, keepdims=True)
    spread = jnp.mean((flat - centre) ** 2, axis=1, keepdims=True)
    normed = ((flat - centre) / jnp.sqrt(spread + 1e-05) * norm_gain + norm_shift).astype(
        jnp.bfloat16
    )
    query_flat = jnp.dot(normed, w_query, preferred_element_type=jnp.float32).astype(jnp.bfloat16)
    key_flat = jnp.dot(normed, w_key, preferred_element_type=jnp.float32).astype(jnp.bfloat16)
    val_flat = jnp.dot(normed, w_value, preferred_element_type=jnp.float32).astype(jnp.bfloat16)
    head_count = query_flat.shape[1] // HD
    width = key_flat.shape[1]
    both = jnp.concatenate([key_flat, val_flat], axis=1)
    pieces, starts = gather_ring(both, "ctx", frame_rows)
    whole = jnp.concatenate(pieces, axis=0)
    key_pos = jnp.concatenate(
        [start + jnp.arange(frame_rows, dtype=jnp.int32) for start in starts]
    )
    queries = query_flat.reshape(frame_rows, head_count, HD)
    keys = whole[:, :width].reshape(-1, head_count, HD)
    vals = whole[:, width:].reshape(-1, head_count, HD)
    scores = jnp.einsum(
        "fhd,nhd->hfn", queries, keys, preferred_element_type=jnp.float32
    ) / math.sqrt(HD)
    valid = (key_pos < own_length)[None, None, :]
    scores = jnp.where(valid, scores, -1e30)
    rowmax = jnp.max(scores, axis=2, keepdims=True)
    weights = jnp.where(valid, jnp.exp(scores - rowmax), 0.0)
    total = jnp.sum(weights, axis=2, keepdims=True)
    summed = jnp.einsum(
        "hfn,nhd->hfd", weights.astype(jnp.bfloat16), vals, preferred_element_type=jnp.float32
    )
    out = summed / total
    query_live = (positions < own_length)[None, :, None]
    out = jnp.where(query_live, out, 0.0).transpose(1, 0, 2)
    result = out.reshape(1, frame_rows, head_count * HD).astype(jnp.bfloat16)
    return (hidden, result)


def solution(mesh):
    in_specs = (
        P("rep", "ctx", "fsdp"),
        P("rep"),
        P("fsdp", None, None, None),
        P("fsdp"),
        P(),
        P(),
        P(),
        P(),
        P(),
    )
    out_specs = (P("rep", "ctx", "fsdp"), P(("rep", "fsdp"), "ctx", None))
    return jax.shard_map(
        per_device, mesh=mesh, in_specs=in_specs, out_specs=out_specs, check_vma=False
    )
```

```python
import math

import jax
import jax.numpy as jnp
from jax import lax
from jax.sharding import PartitionSpec as P
from jax.experimental import pallas as pl
from jax.experimental.pallas import tpu as pltpu

HD = 64


def padded_2(x, sides, width):
    for axis, dim in sides:
        size, length = (lax.axis_size(axis), x.shape[dim])
        up = [(i, (i + 1) % size) for i in range(size - 1)]
        down = [(j, i) for i, j in up]
        last = lax.slice_in_dim(x, length - width, length, axis=dim)
        first = lax.slice_in_dim(x, 0, width, axis=dim)
        before = lax.ppermute(last, axis, up)
        after = lax.ppermute(first, axis, down)
        x = jnp.concatenate([before, x, after], axis=dim)
    return x


def conv_body(x_ref, w_ref, out_ref):
    recs, chans, lanes = x_ref.shape[1], x_ref.shape[2], x_ref.shape[3]
    taps = w_ref.shape[3]
    rows = out_ref.shape[2]
    outs = w_ref.shape[2]

    def octet_step(q, acc):
        base = pl.multiple_of(q * 8, 8)
        hankels = []
        for r in range(recs):
            block = x_ref[0, r, pl.ds(base, 8), :]
            per_chan = []
            for c in range(8):
                row = jnp.broadcast_to(block[c : c + 1, :], (taps, lanes))
                rolled = pltpu.roll(row, 0, 1, stride=1, stride_axis=0)
                per_chan.append(rolled[:, :rows].astype(jnp.bfloat16))
            hankels.append(per_chan)
        for pair in range(4):
            rhs = jnp.concatenate(
                [
                    jnp.concatenate([hankels[r][2 * pair + half] for r in range(recs)], axis=1)
                    for half in range(2)
                ],
                axis=0,
            )
            lhs = jnp.concatenate(
                [w_ref[0, base + 2 * pair], w_ref[0, base + 2 * pair + 1]], axis=1
            )
            acc = acc + jnp.dot(lhs, rhs, preferred_element_type=jnp.float32)
        return acc

    acc = lax.fori_loop(0, chans // 8, octet_step, jnp.zeros((outs, recs * rows), jnp.float32))
    across = lax.broadcasted_iota(jnp.int32, (rows, rows), 0) + lax.broadcasted_iota(
        jnp.int32, (rows, rows), 1
    )
    flip = jnp.where(across == rows - 1, 1.0, 0.0).astype(jnp.bfloat16)
    dims = (((1,), (1,)), ((), ()))
    for r in range(recs):
        part = acc[:, r * rows : (r + 1) * rows]
        high = part.astype(jnp.bfloat16)
        rest = part - high.astype(jnp.float32)
        middle = rest.astype(jnp.bfloat16)
        low = (rest - middle.astype(jnp.float32)).astype(jnp.bfloat16)
        total = lax.dot_general(flip, high, dims, preferred_element_type=jnp.float32)
        total = total + lax.dot_general(flip, middle, dims, preferred_element_type=jnp.float32)
        out_ref[0, r] = total + lax.dot_general(flip, low, dims, preferred_element_type=jnp.float32)


def hankel_conv(xt, wv, rows):
    groups, recs, chans, lanes = xt.shape
    taps, outs = wv.shape[3], wv.shape[2]
    return pl.pallas_call(
        conv_body,
        grid=(groups,),
        in_specs=[pl.BlockSpec((1, recs, chans, lanes), lambda g: (g, 0, 0, 0)),
                  pl.BlockSpec((1, chans, outs, taps), lambda g: (g, 0, 0, 0))],
        out_specs=pl.BlockSpec((1, recs, rows, outs), lambda g: (g, 0, 0, 0)),
        out_shape=jax.ShapeDtypeStruct((groups, recs, rows, outs), jnp.float32),
        cost_estimate=pl.CostEstimate(
            flops=2 * groups * recs * rows * taps * chans * outs,
            bytes_accessed=xt.size * 4 + wv.size * 2 + groups * recs * rows * outs * 4,
            transcendentals=0,
        ),
    )(xt, wv)


def grouped_conv(padded, conv_weight, frame_rows):
    recs, span = padded.shape[0], padded.shape[1]
    groups_here, taps, group_in, group_out = conv_weight.shape
    lanes = -(-(frame_rows + taps - 1) // 128) * 128
    grouped = jnp.pad(padded, ((0, 0), (0, lanes - span), (0, 0)))
    grouped = jnp.roll(jnp.flip(grouped, axis=1), frame_rows - lanes, axis=1)
    grouped = grouped.reshape(recs, lanes, groups_here, group_in).transpose(2, 0, 3, 1)
    out = hankel_conv(grouped.astype(jnp.float32), jnp.transpose(conv_weight, (0, 2, 3, 1)), frame_rows)
    return out.transpose(1, 2, 0, 3).reshape(recs, frame_rows, groups_here * group_out)


def swap_halves(hidden, axis):
    if lax.axis_size(axis) != 2 or hidden.shape[0] != 2:
        return lax.all_to_all(hidden, axis, split_axis=0, concat_axis=2, tiled=True)
    place = lax.axis_index(axis)
    mine = lax.dynamic_index_in_dim(hidden, place, 0, keepdims=True)
    theirs = lax.dynamic_index_in_dim(hidden, 1 - place, 0, keepdims=True)
    got = lax.ppermute(theirs, axis, [(0, 1), (1, 0)])
    return jnp.where(place == 0, jnp.concatenate([mine, got], axis=2), jnp.concatenate([got, mine], axis=2))


def gather_ring(x, axis, rows):
    size = lax.axis_size(axis)
    place = lax.axis_index(axis)
    pieces, starts = [x], [place * rows]
    for shift in range(1, size):
        pairs = [(i, (i + shift) % size) for i in range(size)]
        pieces.append(lax.ppermute(x, axis, pairs))
        starts.append(((place - shift) % size) * rows)
    return pieces, starts


def attend(carry, piece, start, queries, own_length):
    best, total, accum = carry
    keys_part, vals_part = piece
    count = keys_part.shape[0]
    head_count = queries.shape[1]
    keys_part = keys_part.reshape(count, head_count, HD)
    vals_part = vals_part.reshape(count, head_count, HD)
    scores = jnp.einsum(
        "fhd,nhd->fhn", queries, keys_part, preferred_element_type=jnp.float32
    ) / math.sqrt(HD)
    valid = (start + jnp.arange(count, dtype=jnp.int32) < own_length)[None, None, :]
    scores = jnp.where(valid, scores, -1e30)
    fresh = jnp.maximum(best, jnp.max(scores, axis=2))
    weights = jnp.where(valid, jnp.exp(scores - fresh[:, :, None]), 0.0)
    factor = jnp.exp(best - fresh)
    total = total * factor + jnp.sum(weights, axis=2)
    accum = accum * factor[:, :, None] + jnp.einsum(
        "fhn,nhd->fhd", weights.astype(jnp.bfloat16), vals_part, preferred_element_type=jnp.float32
    )
    return (fresh, total, accum)


def start_state(rows, heads_here):
    return (
        jnp.full((rows, heads_here), -1e30, jnp.float32),
        jnp.zeros((rows, heads_here), jnp.float32),
        jnp.zeros((rows, heads_here, HD), jnp.float32),
    )


def blockwise(carry, all_keys, all_vals, queries, own_length, block_rows):
    block_count = all_keys.shape[0] // block_rows

    def block_step(state, index):
        begin = index * block_rows
        piece = (
            lax.dynamic_slice_in_dim(all_keys, begin, block_rows, 0),
            lax.dynamic_slice_in_dim(all_vals, begin, block_rows, 0),
        )
        return (attend(state, piece, begin, queries, own_length), None)

    final, unused = lax.scan(block_step, carry, jnp.arange(block_count, dtype=jnp.int32))
    return final


def finish(final, query_pos, own_length):
    best, total, accum = final
    result = accum / total[:, :, None]
    query_live = (query_pos < own_length)[:, None, None]
    result = jnp.where(query_live, result, 0.0)
    return result.reshape(result.shape[0], result.shape[1] * HD).astype(jnp.bfloat16)


def per_device(
    frames_in, lengths, conv_weight, conv_bias, norm_gain, norm_shift, w_query, w_key, w_value
):
    record_count, frame_rows, channels = frames_in.shape
    ctx_place = lax.axis_index("ctx")
    positions = ctx_place * frame_rows + jnp.arange(frame_rows, dtype=jnp.int32)
    live = positions[None, :] < lengths[:, None]
    masked = jnp.where(live[:, :, None], frames_in, jnp.zeros((), frames_in.dtype))
    groups_here, kernel_width, group_in, group_out = conv_weight.shape
    half_width = kernel_width // 2
    padded = padded_2(masked, (("ctx", 1),), half_width)
    conv_out = grouped_conv(padded, conv_weight, frame_rows)
    hidden = (
        masked.astype(jnp.float32)
        + jax.nn.gelu(conv_out + conv_bias.astype(jnp.float32), approximate=False)
    ).astype(jnp.bfloat16)
    record = swap_halves(hidden, "fsdp")
    own_length = lax.dynamic_index_in_dim(lengths, lax.axis_index("fsdp"), 0, keepdims=False)
    flat = record[0].astype(jnp.float32)
    centre = jnp.mean(flat, axis=1, keepdims=True)
    spread = jnp.mean((flat - centre) ** 2, axis=1, keepdims=True)
    normed = ((flat - centre) / jnp.sqrt(spread + 1e-05) * norm_gain + norm_shift).astype(
        jnp.bfloat16
    )
    query_flat = jnp.dot(normed, w_query, preferred_element_type=jnp.float32).astype(jnp.bfloat16)
    key_flat = jnp.dot(normed, w_key, preferred_element_type=jnp.float32).astype(jnp.bfloat16)
    val_flat = jnp.dot(normed, w_value, preferred_element_type=jnp.float32).astype(jnp.bfloat16)
    head_count = query_flat.shape[1] // HD
    width = key_flat.shape[1]
    both = jnp.concatenate([key_flat, val_flat], axis=1)
    pieces, starts = gather_ring(both, "ctx", frame_rows)
    whole = jnp.concatenate(pieces, axis=0)
    key_pos = jnp.concatenate(
        [start + jnp.arange(frame_rows, dtype=jnp.int32) for start in starts]
    )
    queries = query_flat.reshape(frame_rows, head_count, HD)
    keys = whole[:, :width].reshape(-1, head_count, HD)
    vals = whole[:, width:].reshape(-1, head_count, HD)
    scores = jnp.einsum(
        "fhd,nhd->hfn", queries, keys, preferred_element_type=jnp.float32
    ) / math.sqrt(HD)
    valid = (key_pos < own_length)[None, None, :]
    scores = jnp.where(valid, scores, -1e30)
    rowmax = jnp.max(scores, axis=2, keepdims=True)
    weights = jnp.where(valid, jnp.exp(scores - rowmax), 0.0)
    total = jnp.sum(weights, axis=2, keepdims=True)
    summed = jnp.einsum(
        "hfn,nhd->hfd", weights.astype(jnp.bfloat16), vals, preferred_element_type=jnp.float32
    )
    out = summed / total
    query_live = (positions < own_length)[None, :, None]
    out = jnp.where(query_live, out, 0.0).transpose(1, 0, 2)
    result = out.reshape(1, frame_rows, head_count * HD).astype(jnp.bfloat16)
    return (hidden, result)


def solution(mesh):
    in_specs = (
        P("rep", "ctx", "fsdp"),
        P("rep"),
        P("fsdp", None, None, None),
        P("fsdp"),
        P(),
        P(),
        P(),
        P(),
        P(),
    )
    out_specs = (P("rep", "ctx", "fsdp"), P(("rep", "fsdp"), "ctx", None))
    return jax.shard_map(
        per_device, mesh=mesh, in_specs=in_specs, out_specs=out_specs, check_vma=False
    )
```

```python
import math

import jax
import jax.numpy as jnp
from jax import lax
from jax.sharding import PartitionSpec as P
from jax.experimental import pallas as pl
from jax.experimental.pallas import tpu as pltpu

HD = 64


def padded_2(x, sides, width):
    for axis, dim in sides:
        size, length = (lax.axis_size(axis), x.shape[dim])
        up = [(i, (i + 1) % size) for i in range(size - 1)]
        down = [(j, i) for i, j in up]
        last = lax.slice_in_dim(x, length - width, length, axis=dim)
        first = lax.slice_in_dim(x, 0, width, axis=dim)
        before = lax.ppermute(last, axis, up)
        after = lax.ppermute(first, axis, down)
        x = jnp.concatenate([before, x, after], axis=dim)
    return x


def conv_body(x_ref, w_ref, out_ref):
    recs, chans, lanes = x_ref.shape[1], x_ref.shape[2], x_ref.shape[3]
    taps = w_ref.shape[3]
    rows = out_ref.shape[2]
    outs = w_ref.shape[2]

    def octet_step(q, acc):
        base = pl.multiple_of(q * 8, 8)
        hankels = []
        for r in range(recs):
            block = x_ref[0, r, pl.ds(base, 8), :]
            per_chan = []
            for c in range(8):
                row = jnp.broadcast_to(block[c : c + 1, :], (taps, lanes))
                rolled = pltpu.roll(row, 0, 1, stride=1, stride_axis=0)
                per_chan.append(rolled[:, :rows].astype(jnp.bfloat16))
            hankels.append(per_chan)
        for pair in range(4):
            rhs = jnp.concatenate(
                [
                    jnp.concatenate([hankels[r][2 * pair + half] for r in range(recs)], axis=1)
                    for half in range(2)
                ],
                axis=0,
            )
            lhs = jnp.concatenate(
                [w_ref[0, base + 2 * pair], w_ref[0, base + 2 * pair + 1]], axis=1
            )
            acc = acc + jnp.dot(lhs, rhs, preferred_element_type=jnp.float32)
        return acc

    acc = lax.fori_loop(0, chans // 8, octet_step, jnp.zeros((outs, recs * rows), jnp.float32))
    across = lax.broadcasted_iota(jnp.int32, (rows, rows), 0) + lax.broadcasted_iota(
        jnp.int32, (rows, rows), 1
    )
    flip = jnp.where(across == rows - 1, 1.0, 0.0).astype(jnp.bfloat16)
    dims = (((1,), (1,)), ((), ()))
    for r in range(recs):
        part = acc[:, r * rows : (r + 1) * rows]
        high = part.astype(jnp.bfloat16)
        rest = part - high.astype(jnp.float32)
        middle = rest.astype(jnp.bfloat16)
        low = (rest - middle.astype(jnp.float32)).astype(jnp.bfloat16)
        total = lax.dot_general(flip, high, dims, preferred_element_type=jnp.float32)
        total = total + lax.dot_general(flip, middle, dims, preferred_element_type=jnp.float32)
        out_ref[0, r] = total + lax.dot_general(flip, low, dims, preferred_element_type=jnp.float32)


def hankel_conv(xt, wv, rows):
    groups, recs, chans, lanes = xt.shape
    taps, outs = wv.shape[3], wv.shape[2]
    return pl.pallas_call(
        conv_body,
        grid=(groups,),
        in_specs=[pl.BlockSpec((1, recs, chans, lanes), lambda g: (g, 0, 0, 0)),
                  pl.BlockSpec((1, chans, outs, taps), lambda g: (g, 0, 0, 0))],
        out_specs=pl.BlockSpec((1, recs, rows, outs), lambda g: (g, 0, 0, 0)),
        out_shape=jax.ShapeDtypeStruct((groups, recs, rows, outs), jnp.float32),
        cost_estimate=pl.CostEstimate(
            flops=2 * groups * recs * rows * taps * chans * outs,
            bytes_accessed=xt.size * 4 + wv.size * 2 + groups * recs * rows * outs * 4,
            transcendentals=0,
        ),
    )(xt, wv)


def grouped_conv(padded, conv_weight, frame_rows):
    recs, span = padded.shape[0], padded.shape[1]
    groups_here, taps, group_in, group_out = conv_weight.shape
    lanes = -(-(frame_rows + taps - 1) // 128) * 128
    grouped = jnp.pad(padded, ((0, 0), (0, lanes - span), (0, 0)))
    grouped = jnp.roll(jnp.flip(grouped, axis=1), frame_rows - lanes, axis=1)
    grouped = grouped.reshape(recs, lanes, groups_here, group_in).transpose(2, 0, 3, 1)
    out = hankel_conv(grouped.astype(jnp.float32), jnp.transpose(conv_weight, (0, 2, 3, 1)), frame_rows)
    return out.transpose(1, 2, 0, 3).reshape(recs, frame_rows, groups_here * group_out)


def conv_block(masked, conv_weight, conv_bias, half_width, frame_rows, after=None):
    padded = padded_2(masked, (("ctx", 1),), half_width)
    if after is not None:
        padded, unused = lax.optimization_barrier((padded, after))
    conv_out = grouped_conv(padded, conv_weight, frame_rows)
    return (
        masked.astype(jnp.float32)
        + jax.nn.gelu(conv_out + conv_bias.astype(jnp.float32), approximate=False)
    ).astype(jnp.bfloat16)


def conv_by_record(masked, conv_weight, conv_bias, half_width, frame_rows):
    place = lax.axis_index("fsdp")
    given = lax.dynamic_index_in_dim(masked, 1 - place, 0, keepdims=True)
    kept = lax.dynamic_index_in_dim(masked, place, 0, keepdims=True)
    hidden_given = conv_block(given, conv_weight, conv_bias, half_width, frame_rows)
    got = lax.ppermute(hidden_given, "fsdp", [(0, 1), (1, 0)])
    hidden_kept = conv_block(kept, conv_weight, conv_bias, half_width, frame_rows, hidden_given)
    first = place == 0
    hidden = jnp.where(
        first,
        jnp.concatenate([hidden_kept, hidden_given], axis=0),
        jnp.concatenate([hidden_given, hidden_kept], axis=0),
    )
    record = jnp.where(
        first,
        jnp.concatenate([hidden_kept, got], axis=2),
        jnp.concatenate([got, hidden_kept], axis=2),
    )
    return hidden, record


def swap_halves(hidden, axis):
    if lax.axis_size(axis) != 2 or hidden.shape[0] != 2:
        return lax.all_to_all(hidden, axis, split_axis=0, concat_axis=2, tiled=True)
    place = lax.axis_index(axis)
    mine = lax.dynamic_index_in_dim(hidden, place, 0, keepdims=True)
    theirs = lax.dynamic_index_in_dim(hidden, 1 - place, 0, keepdims=True)
    got = lax.ppermute(theirs, axis, [(0, 1), (1, 0)])
    return jnp.where(place == 0, jnp.concatenate([mine, got], axis=2), jnp.concatenate([got, mine], axis=2))


def gather_ring(x, axis, rows):
    size = lax.axis_size(axis)
    place = lax.axis_index(axis)
    pieces, starts = [x], [place * rows]
    for shift in range(1, size):
        pairs = [(i, (i + shift) % size) for i in range(size)]
        pieces.append(lax.ppermute(x, axis, pairs))
        starts.append(((place - shift) % size) * rows)
    return pieces, starts


def attend(carry, piece, start, queries, own_length):
    best, total, accum = carry
    keys_part, vals_part = piece
    count = keys_part.shape[0]
    head_count = queries.shape[1]
    keys_part = keys_part.reshape(count, head_count, HD)
    vals_part = vals_part.reshape(count, head_count, HD)
    scores = jnp.einsum(
        "fhd,nhd->fhn", queries, keys_part, preferred_element_type=jnp.float32
    ) / math.sqrt(HD)
    valid = (start + jnp.arange(count, dtype=jnp.int32) < own_length)[None, None, :]
    scores = jnp.where(valid, scores, -1e30)
    fresh = jnp.maximum(best, jnp.max(scores, axis=2))
    weights = jnp.where(valid, jnp.exp(scores - fresh[:, :, None]), 0.0)
    factor = jnp.exp(best - fresh)
    total = total * factor + jnp.sum(weights, axis=2)
    accum = accum * factor[:, :, None] + jnp.einsum(
        "fhn,nhd->fhd", weights.astype(jnp.bfloat16), vals_part, preferred_element_type=jnp.float32
    )
    return (fresh, total, accum)


def start_state(rows, heads_here):
    return (
        jnp.full((rows, heads_here), -1e30, jnp.float32),
        jnp.zeros((rows, heads_here), jnp.float32),
        jnp.zeros((rows, heads_here, HD), jnp.float32),
    )


def blockwise(carry, all_keys, all_vals, queries, own_length, block_rows):
    block_count = all_keys.shape[0] // block_rows

    def block_step(state, index):
        begin = index * block_rows
        piece = (
            lax.dynamic_slice_in_dim(all_keys, begin, block_rows, 0),
            lax.dynamic_slice_in_dim(all_vals, begin, block_rows, 0),
        )
        return (attend(state, piece, begin, queries, own_length), None)

    final, unused = lax.scan(block_step, carry, jnp.arange(block_count, dtype=jnp.int32))
    return final


def finish(final, query_pos, own_length):
    best, total, accum = final
    result = accum / total[:, :, None]
    query_live = (query_pos < own_length)[:, None, None]
    result = jnp.where(query_live, result, 0.0)
    return result.reshape(result.shape[0], result.shape[1] * HD).astype(jnp.bfloat16)


def per_device(
    frames_in, lengths, conv_weight, conv_bias, norm_gain, norm_shift, w_query, w_key, w_value
):
    record_count, frame_rows, channels = frames_in.shape
    ctx_place = lax.axis_index("ctx")
    positions = ctx_place * frame_rows + jnp.arange(frame_rows, dtype=jnp.int32)
    live = positions[None, :] < lengths[:, None]
    masked = jnp.where(live[:, :, None], frames_in, jnp.zeros((), frames_in.dtype))
    groups_here, kernel_width, group_in, group_out = conv_weight.shape
    half_width = kernel_width // 2
    if lax.axis_size("fsdp") == 2 and record_count == 2:
        hidden, record = conv_by_record(masked, conv_weight, conv_bias, half_width, frame_rows)
    else:
        hidden = conv_block(masked, conv_weight, conv_bias, half_width, frame_rows)
        record = swap_halves(hidden, "fsdp")
    own_length = lax.dynamic_index_in_dim(lengths, lax.axis_index("fsdp"), 0, keepdims=False)
    flat = record[0].astype(jnp.float32)
    centre = jnp.mean(flat, axis=1, keepdims=True)
    spread = jnp.mean((flat - centre) ** 2, axis=1, keepdims=True)
    normed = ((flat - centre) / jnp.sqrt(spread + 1e-05) * norm_gain + norm_shift).astype(
        jnp.bfloat16
    )
    query_flat = jnp.dot(normed, w_query, preferred_element_type=jnp.float32).astype(jnp.bfloat16)
    key_flat = jnp.dot(normed, w_key, preferred_element_type=jnp.float32).astype(jnp.bfloat16)
    val_flat = jnp.dot(normed, w_value, preferred_element_type=jnp.float32).astype(jnp.bfloat16)
    head_count = query_flat.shape[1] // HD
    width = key_flat.shape[1]
    both = jnp.concatenate([key_flat, val_flat], axis=1)
    pieces, starts = gather_ring(both, "ctx", frame_rows)
    whole = jnp.concatenate(pieces, axis=0)
    key_pos = jnp.concatenate(
        [start + jnp.arange(frame_rows, dtype=jnp.int32) for start in starts]
    )
    queries = query_flat.reshape(frame_rows, head_count, HD)
    keys = whole[:, :width].reshape(-1, head_count, HD)
    vals = whole[:, width:].reshape(-1, head_count, HD)
    scores = jnp.einsum(
        "fhd,nhd->hfn", queries, keys, preferred_element_type=jnp.float32
    ) / math.sqrt(HD)
    valid = (key_pos < own_length)[None, None, :]
    scores = jnp.where(valid, scores, -1e30)
    rowmax = jnp.max(scores, axis=2, keepdims=True)
    weights = jnp.where(valid, jnp.exp(scores - rowmax), 0.0)
    total = jnp.sum(weights, axis=2, keepdims=True)
    summed = jnp.einsum(
        "hfn,nhd->hfd", weights.astype(jnp.bfloat16), vals, preferred_element_type=jnp.float32
    )
    out = summed / total
    query_live = (positions < own_length)[None, :, None]
    out = jnp.where(query_live, out, 0.0).transpose(1, 0, 2)
    result = out.reshape(1, frame_rows, head_count * HD).astype(jnp.bfloat16)
    return (hidden, result)


def solution(mesh):
    in_specs = (
        P("rep", "ctx", "fsdp"),
        P("rep"),
        P("fsdp", None, None, None),
        P("fsdp"),
        P(),
        P(),
        P(),
        P(),
        P(),
    )
    out_specs = (P("rep", "ctx", "fsdp"), P(("rep", "fsdp"), "ctx", None))
    return jax.shard_map(
        per_device, mesh=mesh, in_specs=in_specs, out_specs=out_specs, check_vma=False
    )
```

```python
import math

import jax
import jax.numpy as jnp
from jax import lax
from jax.sharding import PartitionSpec as P
from jax.experimental import pallas as pl
from jax.experimental.pallas import tpu as pltpu

HD = 64


def padded_2(x, sides, width):
    for axis, dim in sides:
        size, length = (lax.axis_size(axis), x.shape[dim])
        up = [(i, (i + 1) % size) for i in range(size - 1)]
        down = [(j, i) for i, j in up]
        last = lax.slice_in_dim(x, length - width, length, axis=dim)
        first = lax.slice_in_dim(x, 0, width, axis=dim)
        before = lax.ppermute(last, axis, up)
        after = lax.ppermute(first, axis, down)
        x = jnp.concatenate([before, x, after], axis=dim)
    return x


def conv_body(x_ref, w_ref, out_ref):
    recs, chans, lanes = x_ref.shape[1], x_ref.shape[2], x_ref.shape[3]
    taps = w_ref.shape[3]
    rows = out_ref.shape[2]
    outs = w_ref.shape[2]

    def octet_step(q, acc):
        base = pl.multiple_of(q * 8, 8)
        hankels = []
        for r in range(recs):
            block = x_ref[0, r, pl.ds(base, 8), :]
            per_chan = []
            for c in range(8):
                row = jnp.broadcast_to(block[c : c + 1, :], (taps, lanes))
                rolled = pltpu.roll(row, 0, 1, stride=1, stride_axis=0)
                per_chan.append(rolled[:, :rows])
            hankels.append(per_chan)
        for pair in range(4):
            rhs = jnp.concatenate(
                [
                    jnp.concatenate([hankels[r][2 * pair + half] for r in range(recs)], axis=1)
                    for half in range(2)
                ],
                axis=0,
            )
            lhs = jnp.concatenate(
                [w_ref[0, base + 2 * pair], w_ref[0, base + 2 * pair + 1]], axis=1
            )
            acc = acc + jnp.dot(lhs, rhs, preferred_element_type=jnp.float32)
        return acc

    acc = lax.fori_loop(0, chans // 8, octet_step, jnp.zeros((outs, recs * rows), jnp.float32), unroll=2)
    across = lax.broadcasted_iota(jnp.int32, (rows, rows), 0) + lax.broadcasted_iota(
        jnp.int32, (rows, rows), 1
    )
    flip = jnp.where(across == rows - 1, 1.0, 0.0).astype(jnp.bfloat16)
    dims = (((1,), (1,)), ((), ()))
    for r in range(recs):
        part = acc[:, r * rows : (r + 1) * rows]
        high = part.astype(jnp.bfloat16)
        rest = part - high.astype(jnp.float32)
        middle = rest.astype(jnp.bfloat16)
        low = (rest - middle.astype(jnp.float32)).astype(jnp.bfloat16)
        total = lax.dot_general(flip, high, dims, preferred_element_type=jnp.float32)
        total = total + lax.dot_general(flip, middle, dims, preferred_element_type=jnp.float32)
        out_ref[0, r] = total + lax.dot_general(flip, low, dims, preferred_element_type=jnp.float32)


def hankel_conv(xt, wv, rows):
    groups, recs, chans, lanes = xt.shape
    taps, outs = wv.shape[3], wv.shape[2]
    return pl.pallas_call(
        conv_body,
        grid=(groups,),
        in_specs=[pl.BlockSpec((1, recs, chans, lanes), lambda g: (g, 0, 0, 0)),
                  pl.BlockSpec((1, chans, outs, taps), lambda g: (g, 0, 0, 0))],
        out_specs=pl.BlockSpec((1, recs, rows, outs), lambda g: (g, 0, 0, 0)),
        out_shape=jax.ShapeDtypeStruct((groups, recs, rows, outs), jnp.float32),
        cost_estimate=pl.CostEstimate(
            flops=2 * groups * recs * rows * taps * chans * outs,
            bytes_accessed=xt.size * 2 + wv.size * 2 + groups * recs * rows * outs * 4,
            transcendentals=0,
        ),
    )(xt, wv)


def grouped_conv(padded, conv_weight, frame_rows):
    recs, span = padded.shape[0], padded.shape[1]
    groups_here, taps, group_in, group_out = conv_weight.shape
    lanes = -(-(frame_rows + taps - 1) // 128) * 128
    grouped = jnp.pad(padded, ((0, 0), (0, lanes - span), (0, 0)))
    grouped = jnp.roll(jnp.flip(grouped, axis=1), frame_rows - lanes, axis=1)
    grouped = grouped.reshape(recs, lanes, groups_here, group_in).transpose(2, 0, 3, 1)
    out = hankel_conv(grouped, jnp.transpose(conv_weight, (0, 2, 3, 1)), frame_rows)
    return out.transpose(1, 2, 0, 3).reshape(recs, frame_rows, groups_here * group_out)


def swap_halves(hidden, axis):
    if lax.axis_size(axis) != 2 or hidden.shape[0] != 2:
        return lax.all_to_all(hidden, axis, split_axis=0, concat_axis=2, tiled=True)
    place = lax.axis_index(axis)
    mine = lax.dynamic_index_in_dim(hidden, place, 0, keepdims=True)
    theirs = lax.dynamic_index_in_dim(hidden, 1 - place, 0, keepdims=True)
    got = lax.ppermute(theirs, axis, [(0, 1), (1, 0)])
    return jnp.where(place == 0, jnp.concatenate([mine, got], axis=2), jnp.concatenate([got, mine], axis=2))


def gather_ring(x, axis, rows):
    size = lax.axis_size(axis)
    place = lax.axis_index(axis)
    pieces, starts = [x], [place * rows]
    for shift in range(1, size):
        pairs = [(i, (i + shift) % size) for i in range(size)]
        pieces.append(lax.ppermute(x, axis, pairs))
        starts.append(((place - shift) % size) * rows)
    return pieces, starts


def attend(carry, piece, start, queries, own_length):
    best, total, accum = carry
    keys_part, vals_part = piece
    count = keys_part.shape[0]
    head_count = queries.shape[1]
    keys_part = keys_part.reshape(count, head_count, HD)
    vals_part = vals_part.reshape(count, head_count, HD)
    scores = jnp.einsum(
        "fhd,nhd->fhn", queries, keys_part, preferred_element_type=jnp.float32
    ) / math.sqrt(HD)
    valid = (start + jnp.arange(count, dtype=jnp.int32) < own_length)[None, None, :]
    scores = jnp.where(valid, scores, -1e30)
    fresh = jnp.maximum(best, jnp.max(scores, axis=2))
    weights = jnp.where(valid, jnp.exp(scores - fresh[:, :, None]), 0.0)
    factor = jnp.exp(best - fresh)
    total = total * factor + jnp.sum(weights, axis=2)
    accum = accum * factor[:, :, None] + jnp.einsum(
        "fhn,nhd->fhd", weights.astype(jnp.bfloat16), vals_part, preferred_element_type=jnp.float32
    )
    return (fresh, total, accum)


def start_state(rows, heads_here):
    return (
        jnp.full((rows, heads_here), -1e30, jnp.float32),
        jnp.zeros((rows, heads_here), jnp.float32),
        jnp.zeros((rows, heads_here, HD), jnp.float32),
    )


def blockwise(carry, all_keys, all_vals, queries, own_length, block_rows):
    block_count = all_keys.shape[0] // block_rows

    def block_step(state, index):
        begin = index * block_rows
        piece = (
            lax.dynamic_slice_in_dim(all_keys, begin, block_rows, 0),
            lax.dynamic_slice_in_dim(all_vals, begin, block_rows, 0),
        )
        return (attend(state, piece, begin, queries, own_length), None)

    final, unused = lax.scan(block_step, carry, jnp.arange(block_count, dtype=jnp.int32))
    return final


def finish(final, query_pos, own_length):
    best, total, accum = final
    result = accum / total[:, :, None]
    query_live = (query_pos < own_length)[:, None, None]
    result = jnp.where(query_live, result, 0.0)
    return result.reshape(result.shape[0], result.shape[1] * HD).astype(jnp.bfloat16)


def per_device(
    frames_in, lengths, conv_weight, conv_bias, norm_gain, norm_shift, w_query, w_key, w_value
):
    record_count, frame_rows, channels = frames_in.shape
    ctx_place = lax.axis_index("ctx")
    positions = ctx_place * frame_rows + jnp.arange(frame_rows, dtype=jnp.int32)
    live = positions[None, :] < lengths[:, None]
    masked = jnp.where(live[:, :, None], frames_in, jnp.zeros((), frames_in.dtype))
    groups_here, kernel_width, group_in, group_out = conv_weight.shape
    half_width = kernel_width // 2
    padded = padded_2(masked, (("ctx", 1),), half_width)
    conv_out = grouped_conv(padded, conv_weight, frame_rows)
    hidden = (
        masked.astype(jnp.float32)
        + jax.nn.gelu(conv_out + conv_bias.astype(jnp.float32), approximate=False)
    ).astype(jnp.bfloat16)
    record = swap_halves(hidden, "fsdp")
    own_length = lax.dynamic_index_in_dim(lengths, lax.axis_index("fsdp"), 0, keepdims=False)
    flat = record[0].astype(jnp.float32)
    centre = jnp.mean(flat, axis=1, keepdims=True)
    spread = jnp.mean((flat - centre) ** 2, axis=1, keepdims=True)
    normed = ((flat - centre) / jnp.sqrt(spread + 1e-05) * norm_gain + norm_shift).astype(
        jnp.bfloat16
    )
    query_flat = jnp.dot(normed, w_query, preferred_element_type=jnp.float32).astype(jnp.bfloat16)
    key_flat = jnp.dot(normed, w_key, preferred_element_type=jnp.float32).astype(jnp.bfloat16)
    val_flat = jnp.dot(normed, w_value, preferred_element_type=jnp.float32).astype(jnp.bfloat16)
    head_count = query_flat.shape[1] // HD
    width = key_flat.shape[1]
    both = jnp.concatenate([key_flat, val_flat], axis=1)
    pieces, starts = gather_ring(both, "ctx", frame_rows)
    whole = jnp.concatenate(pieces, axis=0)
    key_pos = jnp.concatenate(
        [start + jnp.arange(frame_rows, dtype=jnp.int32) for start in starts]
    )
    queries = query_flat.reshape(frame_rows, head_count, HD)
    keys = whole[:, :width].reshape(-1, head_count, HD)
    vals = whole[:, width:].reshape(-1, head_count, HD)
    scores = jnp.einsum(
        "fhd,nhd->hfn", queries, keys, preferred_element_type=jnp.float32
    ) / math.sqrt(HD)
    valid = (key_pos < own_length)[None, None, :]
    scores = jnp.where(valid, scores, -1e30)
    rowmax = jnp.max(scores, axis=2, keepdims=True)
    weights = jnp.where(valid, jnp.exp(scores - rowmax), 0.0)
    total = jnp.sum(weights, axis=2, keepdims=True)
    summed = jnp.einsum(
        "hfn,nhd->hfd", weights.astype(jnp.bfloat16), vals, preferred_element_type=jnp.float32
    )
    out = summed / total
    query_live = (positions < own_length)[None, :, None]
    out = jnp.where(query_live, out, 0.0).transpose(1, 0, 2)
    result = out.reshape(1, frame_rows, head_count * HD).astype(jnp.bfloat16)
    return (hidden, result)


def solution(mesh):
    in_specs = (
        P("rep", "ctx", "fsdp"),
        P("rep"),
        P("fsdp", None, None, None),
        P("fsdp"),
        P(),
        P(),
        P(),
        P(),
        P(),
    )
    out_specs = (P("rep", "ctx", "fsdp"), P(("rep", "fsdp"), "ctx", None))
    return jax.shard_map(
        per_device, mesh=mesh, in_specs=in_specs, out_specs=out_specs, check_vma=False
    )
```

```python
import math

import jax
import jax.numpy as jnp
from jax import lax
from jax.sharding import PartitionSpec as P
from jax.experimental import pallas as pl
from jax.experimental.pallas import tpu as pltpu

HD = 64


def padded_2(x, sides, width):
    for axis, dim in sides:
        size, length = (lax.axis_size(axis), x.shape[dim])
        up = [(i, (i + 1) % size) for i in range(size - 1)]
        down = [(j, i) for i, j in up]
        last = lax.slice_in_dim(x, length - width, length, axis=dim)
        first = lax.slice_in_dim(x, 0, width, axis=dim)
        before = lax.ppermute(last, axis, up)
        after = lax.ppermute(first, axis, down)
        x = jnp.concatenate([before, x, after], axis=dim)
    return x


def conv_body(x_ref, w_ref, out_ref):
    recs, chans, lanes = x_ref.shape[1], x_ref.shape[2], x_ref.shape[3]
    taps = w_ref.shape[3]
    rows = out_ref.shape[2]
    outs = w_ref.shape[2]

    def octet_step(q, acc):
        base = pl.multiple_of(q * 8, 8)
        hankels = []
        for r in range(recs):
            block = x_ref[0, r, pl.ds(base, 8), :]
            per_chan = []
            for c in range(8):
                row = jnp.broadcast_to(block[c : c + 1, :], (taps, lanes))
                rolled = pltpu.roll(row, 0, 1, stride=1, stride_axis=0)
                per_chan.append(rolled[:, :rows])
            hankels.append(per_chan)
        for pair in range(4):
            rhs = jnp.concatenate(
                [
                    jnp.concatenate([hankels[r][2 * pair + half] for r in range(recs)], axis=1)
                    for half in range(2)
                ],
                axis=0,
            )
            lhs = jnp.concatenate(
                [w_ref[0, base + 2 * pair], w_ref[0, base + 2 * pair + 1]], axis=1
            )
            acc = acc + jnp.dot(lhs, rhs, preferred_element_type=jnp.float32)
        return acc

    acc = lax.fori_loop(0, chans // 8, octet_step, jnp.zeros((outs, recs * rows), jnp.float32), unroll=4)
    across = lax.broadcasted_iota(jnp.int32, (rows, rows), 0) + lax.broadcasted_iota(
        jnp.int32, (rows, rows), 1
    )
    flip = jnp.where(across == rows - 1, 1.0, 0.0).astype(jnp.bfloat16)
    dims = (((1,), (1,)), ((), ()))
    for r in range(recs):
        part = acc[:, r * rows : (r + 1) * rows]
        high = part.astype(jnp.bfloat16)
        rest = part - high.astype(jnp.float32)
        middle = rest.astype(jnp.bfloat16)
        low = (rest - middle.astype(jnp.float32)).astype(jnp.bfloat16)
        total = lax.dot_general(flip, high, dims, preferred_element_type=jnp.float32)
        total = total + lax.dot_general(flip, middle, dims, preferred_element_type=jnp.float32)
        out_ref[0, r] = total + lax.dot_general(flip, low, dims, preferred_element_type=jnp.float32)


def hankel_conv(xt, wv, rows):
    groups, recs, chans, lanes = xt.shape
    taps, outs = wv.shape[3], wv.shape[2]
    return pl.pallas_call(
        conv_body,
        grid=(groups,),
        in_specs=[pl.BlockSpec((1, recs, chans, lanes), lambda g: (g, 0, 0, 0)),
                  pl.BlockSpec((1, chans, outs, taps), lambda g: (g, 0, 0, 0))],
        out_specs=pl.BlockSpec((1, recs, rows, outs), lambda g: (g, 0, 0, 0)),
        out_shape=jax.ShapeDtypeStruct((groups, recs, rows, outs), jnp.float32),
        cost_estimate=pl.CostEstimate(
            flops=2 * groups * recs * rows * taps * chans * outs,
            bytes_accessed=xt.size * 2 + wv.size * 2 + groups * recs * rows * outs * 4,
            transcendentals=0,
        ),
    )(xt, wv)


def grouped_conv(padded, conv_weight, frame_rows):
    recs, span = padded.shape[0], padded.shape[1]
    groups_here, taps, group_in, group_out = conv_weight.shape
    lanes = -(-(frame_rows + taps - 1) // 128) * 128
    grouped = jnp.pad(padded, ((0, 0), (0, lanes - span), (0, 0)))
    grouped = jnp.roll(jnp.flip(grouped, axis=1), frame_rows - lanes, axis=1)
    grouped = grouped.reshape(recs, lanes, groups_here, group_in).transpose(2, 0, 3, 1)
    out = hankel_conv(grouped, jnp.transpose(conv_weight, (0, 2, 3, 1)), frame_rows)
    return out.transpose(1, 2, 0, 3).reshape(recs, frame_rows, groups_here * group_out)


def swap_halves(hidden, axis):
    if lax.axis_size(axis) != 2 or hidden.shape[0] != 2:
        return lax.all_to_all(hidden, axis, split_axis=0, concat_axis=2, tiled=True)
    place = lax.axis_index(axis)
    mine = lax.dynamic_index_in_dim(hidden, place, 0, keepdims=True)
    theirs = lax.dynamic_index_in_dim(hidden, 1 - place, 0, keepdims=True)
    got = lax.ppermute(theirs, axis, [(0, 1), (1, 0)])
    return jnp.where(place == 0, jnp.concatenate([mine, got], axis=2), jnp.concatenate([got, mine], axis=2))


def attend_body(*refs):
    q_ref, valid_ref, live_ref = refs[0], refs[1], refs[2]
    out_ref = refs[-1]
    block_refs = refs[3:-1]
    rows, width = q_ref.shape
    valid = valid_ref[...] > 0.0
    live = live_ref[...] > 0.0
    lanes = lax.broadcasted_iota(jnp.int32, (1, 128), 1)
    for pair in range(width // 128):
        cols = slice(pair * 128, (pair + 1) * 128)
        vcols = slice(width + pair * 128, width + (pair + 1) * 128)
        keys = jnp.concatenate([block[:, cols] for block in block_refs], axis=0)
        vals = jnp.concatenate([block[:, vcols] for block in block_refs], axis=0)
        query = q_ref[:, cols]
        results = []
        for half in range(2):
            mine = (lanes // HD) == half
            scores = lax.dot_general(
                jnp.where(mine, query, jnp.zeros_like(query)),
                keys,
                (((1,), (1,)), ((), ())),
                preferred_element_type=jnp.float32,
            ) / math.sqrt(HD)
            scores = jnp.where(valid, scores, -1e30)
            rowmax = jnp.max(scores, axis=1, keepdims=True)
            weights = jnp.where(valid, jnp.exp(scores - rowmax), 0.0)
            total = jnp.sum(weights, axis=1, keepdims=True)
            summed = jnp.dot(weights.astype(jnp.bfloat16), vals, preferred_element_type=jnp.float32)
            results.append(summed / total)
        both = jnp.where((lanes // HD) == 0, results[0], results[1])
        out_ref[:, cols] = jnp.where(live, both, 0.0).astype(out_ref.dtype)


def fused_attention(query_flat, pieces, key_pos, own_length, query_pos):
    rows, width = query_flat.shape
    keys_total = key_pos.shape[0]
    valid = (key_pos < own_length).astype(jnp.float32).reshape(1, keys_total)
    live = (query_pos < own_length).astype(jnp.float32).reshape(rows, 1)
    return pl.pallas_call(
        attend_body,
        out_shape=jax.ShapeDtypeStruct((rows, width), jnp.bfloat16),
        cost_estimate=pl.CostEstimate(
            flops=8 * rows * keys_total * width,
            bytes_accessed=2 * (rows * width * 2 + keys_total * width * 2),
            transcendentals=2 * rows * keys_total * (width // HD),
        ),
    )(query_flat, valid, live, *pieces)


def gather_ring(x, axis, rows):
    size = lax.axis_size(axis)
    place = lax.axis_index(axis)
    pieces, starts = [x], [place * rows]
    for shift in range(1, size):
        pairs = [(i, (i + shift) % size) for i in range(size)]
        pieces.append(lax.ppermute(x, axis, pairs))
        starts.append(((place - shift) % size) * rows)
    return pieces, starts


def attend(carry, piece, start, queries, own_length):
    best, total, accum = carry
    keys_part, vals_part = piece
    count = keys_part.shape[0]
    head_count = queries.shape[1]
    keys_part = keys_part.reshape(count, head_count, HD)
    vals_part = vals_part.reshape(count, head_count, HD)
    scores = jnp.einsum(
        "fhd,nhd->fhn", queries, keys_part, preferred_element_type=jnp.float32
    ) / math.sqrt(HD)
    valid = (start + jnp.arange(count, dtype=jnp.int32) < own_length)[None, None, :]
    scores = jnp.where(valid, scores, -1e30)
    fresh = jnp.maximum(best, jnp.max(scores, axis=2))
    weights = jnp.where(valid, jnp.exp(scores - fresh[:, :, None]), 0.0)
    factor = jnp.exp(best - fresh)
    total = total * factor + jnp.sum(weights, axis=2)
    accum = accum * factor[:, :, None] + jnp.einsum(
        "fhn,nhd->fhd", weights.astype(jnp.bfloat16), vals_part, preferred_element_type=jnp.float32
    )
    return (fresh, total, accum)


def start_state(rows, heads_here):
    return (
        jnp.full((rows, heads_here), -1e30, jnp.float32),
        jnp.zeros((rows, heads_here), jnp.float32),
        jnp.zeros((rows, heads_here, HD), jnp.float32),
    )


def blockwise(carry, all_keys, all_vals, queries, own_length, block_rows):
    block_count = all_keys.shape[0] // block_rows

    def block_step(state, index):
        begin = index * block_rows
        piece = (
            lax.dynamic_slice_in_dim(all_keys, begin, block_rows, 0),
            lax.dynamic_slice_in_dim(all_vals, begin, block_rows, 0),
        )
        return (attend(state, piece, begin, queries, own_length), None)

    final, unused = lax.scan(block_step, carry, jnp.arange(block_count, dtype=jnp.int32))
    return final


def finish(final, query_pos, own_length):
    best, total, accum = final
    result = accum / total[:, :, None]
    query_live = (query_pos < own_length)[:, None, None]
    result = jnp.where(query_live, result, 0.0)
    return result.reshape(result.shape[0], result.shape[1] * HD).astype(jnp.bfloat16)


def per_device(
    frames_in, lengths, conv_weight, conv_bias, norm_gain, norm_shift, w_query, w_key, w_value
):
    record_count, frame_rows, channels = frames_in.shape
    ctx_place = lax.axis_index("ctx")
    positions = ctx_place * frame_rows + jnp.arange(frame_rows, dtype=jnp.int32)
    live = positions[None, :] < lengths[:, None]
    masked = jnp.where(live[:, :, None], frames_in, jnp.zeros((), frames_in.dtype))
    groups_here, kernel_width, group_in, group_out = conv_weight.shape
    half_width = kernel_width // 2
    padded = padded_2(masked, (("ctx", 1),), half_width)
    conv_out = grouped_conv(padded, conv_weight, frame_rows)
    hidden = (
        masked.astype(jnp.float32)
        + jax.nn.gelu(conv_out + conv_bias.astype(jnp.float32), approximate=False)
    ).astype(jnp.bfloat16)
    record = swap_halves(hidden, "fsdp")
    own_length = lax.dynamic_index_in_dim(lengths, lax.axis_index("fsdp"), 0, keepdims=False)
    flat = record[0].astype(jnp.float32)
    centre = jnp.mean(flat, axis=1, keepdims=True)
    spread = jnp.mean((flat - centre) ** 2, axis=1, keepdims=True)
    normed = ((flat - centre) / jnp.sqrt(spread + 1e-05) * norm_gain + norm_shift).astype(
        jnp.bfloat16
    )
    query_flat = jnp.dot(normed, w_query, preferred_element_type=jnp.float32).astype(jnp.bfloat16)
    key_flat = jnp.dot(normed, w_key, preferred_element_type=jnp.float32).astype(jnp.bfloat16)
    val_flat = jnp.dot(normed, w_value, preferred_element_type=jnp.float32).astype(jnp.bfloat16)
    head_count = query_flat.shape[1] // HD
    width = key_flat.shape[1]
    both = jnp.concatenate([key_flat, val_flat], axis=1)
    pieces, starts = gather_ring(both, "ctx", frame_rows)
    key_pos = jnp.concatenate(
        [start + jnp.arange(frame_rows, dtype=jnp.int32) for start in starts]
    )
    result = fused_attention(query_flat, pieces, key_pos, own_length, positions)
    result = result.reshape(1, frame_rows, query_flat.shape[1])
    return (hidden, result)


def solution(mesh):
    in_specs = (
        P("rep", "ctx", "fsdp"),
        P("rep"),
        P("fsdp", None, None, None),
        P("fsdp"),
        P(),
        P(),
        P(),
        P(),
        P(),
    )
    out_specs = (P("rep", "ctx", "fsdp"), P(("rep", "fsdp"), "ctx", None))
    return jax.shard_map(
        per_device, mesh=mesh, in_specs=in_specs, out_specs=out_specs, check_vma=False
    )
```

```python
import math

import jax
import jax.numpy as jnp
from jax import lax
from jax.sharding import PartitionSpec as P
from jax.experimental import pallas as pl
from jax.experimental.pallas import tpu as pltpu

HD = 64


def padded_2(x, sides, width):
    for axis, dim in sides:
        size, length = (lax.axis_size(axis), x.shape[dim])
        up = [(i, (i + 1) % size) for i in range(size - 1)]
        down = [(j, i) for i, j in up]
        last = lax.slice_in_dim(x, length - width, length, axis=dim)
        first = lax.slice_in_dim(x, 0, width, axis=dim)
        before = lax.ppermute(last, axis, up)
        after = lax.ppermute(first, axis, down)
        x = jnp.concatenate([before, x, after], axis=dim)
    return x


def conv_body(x_ref, w_ref, out_ref):
    recs, chans, lanes = x_ref.shape[1], x_ref.shape[2], x_ref.shape[3]
    taps = w_ref.shape[3]
    rows = out_ref.shape[2]
    outs = w_ref.shape[2]

    def octet_step(q, acc):
        base = pl.multiple_of(q * 8, 8)
        hankels = []
        for r in range(recs):
            block = x_ref[0, r, pl.ds(base, 8), :]
            per_chan = []
            for c in range(8):
                row = jnp.broadcast_to(block[c : c + 1, :], (taps, lanes))
                rolled = pltpu.roll(row, 0, 1, stride=1, stride_axis=0)
                per_chan.append(rolled[:, :rows])
            hankels.append(per_chan)
        for pair in range(4):
            rhs = jnp.concatenate(
                [
                    jnp.concatenate([hankels[r][2 * pair + half] for r in range(recs)], axis=1)
                    for half in range(2)
                ],
                axis=0,
            )
            lhs = jnp.concatenate(
                [w_ref[0, base + 2 * pair], w_ref[0, base + 2 * pair + 1]], axis=1
            )
            acc = acc + jnp.dot(lhs, rhs, preferred_element_type=jnp.float32)
        return acc

    acc = lax.fori_loop(0, chans // 8, octet_step, jnp.zeros((outs, recs * rows), jnp.float32), unroll=4)
    across = lax.broadcasted_iota(jnp.int32, (rows, rows), 0) + lax.broadcasted_iota(
        jnp.int32, (rows, rows), 1
    )
    flip = jnp.where(across == rows - 1, 1.0, 0.0).astype(jnp.bfloat16)
    dims = (((1,), (1,)), ((), ()))
    for r in range(recs):
        part = acc[:, r * rows : (r + 1) * rows]
        high = part.astype(jnp.bfloat16)
        rest = part - high.astype(jnp.float32)
        middle = rest.astype(jnp.bfloat16)
        low = (rest - middle.astype(jnp.float32)).astype(jnp.bfloat16)
        total = lax.dot_general(flip, high, dims, preferred_element_type=jnp.float32)
        total = total + lax.dot_general(flip, middle, dims, preferred_element_type=jnp.float32)
        out_ref[0, r] = total + lax.dot_general(flip, low, dims, preferred_element_type=jnp.float32)


def hankel_conv(xt, wv, rows):
    groups, recs, chans, lanes = xt.shape
    taps, outs = wv.shape[3], wv.shape[2]
    return pl.pallas_call(
        conv_body,
        grid=(groups,),
        in_specs=[pl.BlockSpec((1, recs, chans, lanes), lambda g: (g, 0, 0, 0)),
                  pl.BlockSpec((1, chans, outs, taps), lambda g: (g, 0, 0, 0))],
        out_specs=pl.BlockSpec((1, recs, rows, outs), lambda g: (g, 0, 0, 0)),
        out_shape=jax.ShapeDtypeStruct((groups, recs, rows, outs), jnp.float32),
        cost_estimate=pl.CostEstimate(
            flops=2 * groups * recs * rows * taps * chans * outs,
            bytes_accessed=xt.size * 2 + wv.size * 2 + groups * recs * rows * outs * 4,
            transcendentals=0,
        ),
    )(xt, wv)


def grouped_conv(padded, conv_weight, frame_rows):
    recs, span = padded.shape[0], padded.shape[1]
    groups_here, taps, group_in, group_out = conv_weight.shape
    lanes = -(-(frame_rows + taps - 1) // 128) * 128
    grouped = jnp.pad(padded, ((0, 0), (0, lanes - span), (0, 0)))
    grouped = jnp.roll(jnp.flip(grouped, axis=1), frame_rows - lanes, axis=1)
    grouped = grouped.reshape(recs, lanes, groups_here, group_in).transpose(2, 0, 3, 1)
    out = hankel_conv(grouped, jnp.transpose(conv_weight, (0, 2, 3, 1)), frame_rows)
    return out.transpose(1, 2, 0, 3).reshape(recs, frame_rows, groups_here * group_out)


def swap_halves(hidden, axis):
    if lax.axis_size(axis) != 2 or hidden.shape[0] != 2:
        return lax.all_to_all(hidden, axis, split_axis=0, concat_axis=2, tiled=True)
    place = lax.axis_index(axis)
    mine = lax.dynamic_index_in_dim(hidden, place, 0, keepdims=True)
    theirs = lax.dynamic_index_in_dim(hidden, 1 - place, 0, keepdims=True)
    got = lax.ppermute(theirs, axis, [(0, 1), (1, 0)])
    return jnp.where(place == 0, jnp.concatenate([mine, got], axis=2), jnp.concatenate([got, mine], axis=2))


def attend_body(*refs):
    q_ref, valid_ref, live_ref = refs[0], refs[1], refs[2]
    out_ref = refs[-1]
    block_refs = refs[3:-1]
    rows, width = q_ref.shape
    valid = valid_ref[...] > 0.0
    live = live_ref[...] > 0.0
    lanes = lax.broadcasted_iota(jnp.int32, (1, 128), 1)
    for pair in range(width // 128):
        cols = slice(pair * 128, (pair + 1) * 128)
        vcols = slice(width + pair * 128, width + (pair + 1) * 128)
        keys = jnp.concatenate([block[:, cols] for block in block_refs], axis=0)
        vals = jnp.concatenate([block[:, vcols] for block in block_refs], axis=0)
        query = q_ref[:, cols]
        results = []
        for half in range(2):
            mine = (lanes // HD) == half
            scores = lax.dot_general(
                jnp.where(mine, query, jnp.zeros_like(query)),
                keys,
                (((1,), (1,)), ((), ())),
                preferred_element_type=jnp.float32,
            ) / math.sqrt(HD)
            scores = jnp.where(valid, scores, -1e30)
            rowmax = jnp.max(scores, axis=1, keepdims=True)
            weights = jnp.where(valid, jnp.exp(scores - rowmax), 0.0)
            total = jnp.sum(weights, axis=1, keepdims=True)
            summed = jnp.dot(weights.astype(jnp.bfloat16), vals, preferred_element_type=jnp.float32)
            results.append(summed / total)
        both = jnp.where((lanes // HD) == 0, results[0], results[1])
        out_ref[:, cols] = jnp.where(live, both, 0.0).astype(out_ref.dtype)


def fused_attention(query_flat, pieces, key_pos, own_length, query_pos):
    rows, width = query_flat.shape
    keys_total = key_pos.shape[0]
    valid = (key_pos < own_length).astype(jnp.float32).reshape(1, keys_total)
    live = (query_pos < own_length).astype(jnp.float32).reshape(rows, 1)
    return pl.pallas_call(
        attend_body,
        out_shape=jax.ShapeDtypeStruct((rows, width), jnp.bfloat16),
        cost_estimate=pl.CostEstimate(
            flops=8 * rows * keys_total * width,
            bytes_accessed=2 * (rows * width * 2 + keys_total * width * 2),
            transcendentals=2 * rows * keys_total * (width // HD),
        ),
    )(query_flat, valid, live, *pieces)


def gather_line4(x, axis, rows):
    place = lax.axis_index(axis)
    from_below = lax.ppermute(x, axis, [(0, 1), (1, 2), (2, 3)])
    from_above = lax.ppermute(x, axis, [(1, 0), (2, 1), (3, 2)])
    across = lax.ppermute(x, axis, [(0, 2), (1, 3), (2, 0), (3, 1)])
    passed = lax.ppermute(across, axis, [(2, 3), (1, 0)])
    pieces = [
        x,
        across,
        jnp.where(place >= 1, from_below, passed),
        jnp.where(place <= 2, from_above, passed),
    ]
    starts = [place * rows, ((place + 2) % 4) * rows, ((place + 3) % 4) * rows, ((place + 1) % 4) * rows]
    return pieces, starts


def gather_ring(x, axis, rows):
    size = lax.axis_size(axis)
    if size == 4:
        return gather_line4(x, axis, rows)
    place = lax.axis_index(axis)
    pieces, starts = [x], [place * rows]
    for shift in range(1, size):
        pairs = [(i, (i + shift) % size) for i in range(size)]
        pieces.append(lax.ppermute(x, axis, pairs))
        starts.append(((place - shift) % size) * rows)
    return pieces, starts


def attend(carry, piece, start, queries, own_length):
    best, total, accum = carry
    keys_part, vals_part = piece
    count = keys_part.shape[0]
    head_count = queries.shape[1]
    keys_part = keys_part.reshape(count, head_count, HD)
    vals_part = vals_part.reshape(count, head_count, HD)
    scores = jnp.einsum(
        "fhd,nhd->fhn", queries, keys_part, preferred_element_type=jnp.float32
    ) / math.sqrt(HD)
    valid = (start + jnp.arange(count, dtype=jnp.int32) < own_length)[None, None, :]
    scores = jnp.where(valid, scores, -1e30)
    fresh = jnp.maximum(best, jnp.max(scores, axis=2))
    weights = jnp.where(valid, jnp.exp(scores - fresh[:, :, None]), 0.0)
    factor = jnp.exp(best - fresh)
    total = total * factor + jnp.sum(weights, axis=2)
    accum = accum * factor[:, :, None] + jnp.einsum(
        "fhn,nhd->fhd", weights.astype(jnp.bfloat16), vals_part, preferred_element_type=jnp.float32
    )
    return (fresh, total, accum)


def start_state(rows, heads_here):
    return (
        jnp.full((rows, heads_here), -1e30, jnp.float32),
        jnp.zeros((rows, heads_here), jnp.float32),
        jnp.zeros((rows, heads_here, HD), jnp.float32),
    )


def blockwise(carry, all_keys, all_vals, queries, own_length, block_rows):
    block_count = all_keys.shape[0] // block_rows

    def block_step(state, index):
        begin = index * block_rows
        piece = (
            lax.dynamic_slice_in_dim(all_keys, begin, block_rows, 0),
            lax.dynamic_slice_in_dim(all_vals, begin, block_rows, 0),
        )
        return (attend(state, piece, begin, queries, own_length), None)

    final, unused = lax.scan(block_step, carry, jnp.arange(block_count, dtype=jnp.int32))
    return final


def finish(final, query_pos, own_length):
    best, total, accum = final
    result = accum / total[:, :, None]
    query_live = (query_pos < own_length)[:, None, None]
    result = jnp.where(query_live, result, 0.0)
    return result.reshape(result.shape[0], result.shape[1] * HD).astype(jnp.bfloat16)


def per_device(
    frames_in, lengths, conv_weight, conv_bias, norm_gain, norm_shift, w_query, w_key, w_value
):
    record_count, frame_rows, channels = frames_in.shape
    ctx_place = lax.axis_index("ctx")
    positions = ctx_place * frame_rows + jnp.arange(frame_rows, dtype=jnp.int32)
    live = positions[None, :] < lengths[:, None]
    masked = jnp.where(live[:, :, None], frames_in, jnp.zeros((), frames_in.dtype))
    groups_here, kernel_width, group_in, group_out = conv_weight.shape
    half_width = kernel_width // 2
    padded = padded_2(masked, (("ctx", 1),), half_width)
    conv_out = grouped_conv(padded, conv_weight, frame_rows)
    hidden = (
        masked.astype(jnp.float32)
        + jax.nn.gelu(conv_out + conv_bias.astype(jnp.float32), approximate=False)
    ).astype(jnp.bfloat16)
    record = swap_halves(hidden, "fsdp")
    own_length = lax.dynamic_index_in_dim(lengths, lax.axis_index("fsdp"), 0, keepdims=False)
    flat = record[0].astype(jnp.float32)
    centre = jnp.mean(flat, axis=1, keepdims=True)
    spread = jnp.mean((flat - centre) ** 2, axis=1, keepdims=True)
    normed = ((flat - centre) / jnp.sqrt(spread + 1e-05) * norm_gain + norm_shift).astype(
        jnp.bfloat16
    )
    query_flat = jnp.dot(normed, w_query, preferred_element_type=jnp.float32).astype(jnp.bfloat16)
    key_flat = jnp.dot(normed, w_key, preferred_element_type=jnp.float32).astype(jnp.bfloat16)
    val_flat = jnp.dot(normed, w_value, preferred_element_type=jnp.float32).astype(jnp.bfloat16)
    head_count = query_flat.shape[1] // HD
    width = key_flat.shape[1]
    both = jnp.concatenate([key_flat, val_flat], axis=1)
    pieces, starts = gather_ring(both, "ctx", frame_rows)
    key_pos = jnp.concatenate(
        [start + jnp.arange(frame_rows, dtype=jnp.int32) for start in starts]
    )
    result = fused_attention(query_flat, pieces, key_pos, own_length, positions)
    result = result.reshape(1, frame_rows, query_flat.shape[1])
    return (hidden, result)


def solution(mesh):
    in_specs = (
        P("rep", "ctx", "fsdp"),
        P("rep"),
        P("fsdp", None, None, None),
        P("fsdp"),
        P(),
        P(),
        P(),
        P(),
        P(),
    )
    out_specs = (P("rep", "ctx", "fsdp"), P(("rep", "fsdp"), "ctx", None))
    return jax.shard_map(
        per_device, mesh=mesh, in_specs=in_specs, out_specs=out_specs, check_vma=False
    )
```

```python
import math

import jax
import jax.numpy as jnp
from jax import lax
from jax.sharding import PartitionSpec as P
from jax.experimental import pallas as pl
from jax.experimental.pallas import tpu as pltpu

HD = 64


def padded_2(x, sides, width):
    for axis, dim in sides:
        size, length = (lax.axis_size(axis), x.shape[dim])
        up = [(i, (i + 1) % size) for i in range(size - 1)]
        down = [(j, i) for i, j in up]
        last = lax.slice_in_dim(x, length - width, length, axis=dim)
        first = lax.slice_in_dim(x, 0, width, axis=dim)
        before = lax.ppermute(last, axis, up)
        after = lax.ppermute(first, axis, down)
        x = jnp.concatenate([before, x, after], axis=dim)
    return x


def conv_body(x_ref, w_ref, out_ref):
    pair_groups, recs, chans, lanes = x_ref.shape
    taps = w_ref.shape[3]
    rows = out_ref.shape[1]
    outs = w_ref.shape[2]

    def one_group(group):
        def octet_step(q, acc):
            base = pl.multiple_of(q * 8, 8)
            hankels = []
            for r in range(recs):
                block = x_ref[group, r, pl.ds(base, 8), :]
                per_chan = []
                for c in range(8):
                    row = jnp.broadcast_to(block[c : c + 1, :], (taps, lanes))
                    rolled = pltpu.roll(row, 0, 1, stride=1, stride_axis=0)
                    per_chan.append(rolled[:, :rows])
                hankels.append(per_chan)
            for pair in range(4):
                rhs = jnp.concatenate(
                    [
                        jnp.concatenate([hankels[r][2 * pair + half] for r in range(recs)], axis=1)
                        for half in range(2)
                    ],
                    axis=0,
                )
                lhs = jnp.concatenate(
                    [w_ref[group, base + 2 * pair], w_ref[group, base + 2 * pair + 1]], axis=1
                )
                acc = acc + jnp.dot(lhs, rhs, preferred_element_type=jnp.float32)
            return acc

        start = jnp.zeros((outs, recs * rows), jnp.float32)
        return lax.fori_loop(0, chans // 8, octet_step, start, unroll=4)

    acc = jnp.concatenate([one_group(group) for group in range(pair_groups)], axis=0)
    across = lax.broadcasted_iota(jnp.int32, (rows, rows), 0) + lax.broadcasted_iota(
        jnp.int32, (rows, rows), 1
    )
    flip = jnp.where(across == rows - 1, 1.0, 0.0).astype(jnp.bfloat16)
    dims = (((1,), (1,)), ((), ()))
    for r in range(recs):
        part = acc[:, r * rows : (r + 1) * rows]
        high = part.astype(jnp.bfloat16)
        rest = part - high.astype(jnp.float32)
        middle = rest.astype(jnp.bfloat16)
        low = (rest - middle.astype(jnp.float32)).astype(jnp.bfloat16)
        total = lax.dot_general(flip, high, dims, preferred_element_type=jnp.float32)
        total = total + lax.dot_general(flip, middle, dims, preferred_element_type=jnp.float32)
        out_ref[r] = total + lax.dot_general(flip, low, dims, preferred_element_type=jnp.float32)


def hankel_conv(xt, wv, rows):
    groups, recs, chans, lanes = xt.shape
    taps, outs = wv.shape[3], wv.shape[2]
    return pl.pallas_call(
        conv_body,
        grid=(groups // 2,),
        in_specs=[
            pl.BlockSpec((2, recs, chans, lanes), lambda g: (g, 0, 0, 0)),
            pl.BlockSpec((2, chans, outs, taps), lambda g: (g, 0, 0, 0)),
        ],
        out_specs=pl.BlockSpec((recs, rows, 2 * outs), lambda g: (0, 0, g)),
        out_shape=jax.ShapeDtypeStruct((recs, rows, groups * outs), jnp.float32),
        cost_estimate=pl.CostEstimate(
            flops=2 * groups * recs * rows * taps * chans * outs,
            bytes_accessed=xt.size * 2 + wv.size * 2 + groups * recs * rows * outs * 4,
            transcendentals=0,
        ),
    )(xt, wv)


def grouped_conv(padded, conv_weight, frame_rows):
    recs, span = padded.shape[0], padded.shape[1]
    groups_here, taps, group_in, group_out = conv_weight.shape
    lanes = -(-(frame_rows + taps - 1) // 128) * 128
    grouped = jnp.pad(padded, ((0, 0), (0, lanes - span), (0, 0)))
    grouped = jnp.roll(jnp.flip(grouped, axis=1), frame_rows - lanes, axis=1)
    grouped = grouped.reshape(recs, lanes, groups_here, group_in).transpose(2, 0, 3, 1)
    return hankel_conv(grouped, jnp.transpose(conv_weight, (0, 2, 3, 1)), frame_rows)


def swap_halves(hidden, axis):
    if lax.axis_size(axis) != 2 or hidden.shape[0] != 2:
        return lax.all_to_all(hidden, axis, split_axis=0, concat_axis=2, tiled=True)
    place = lax.axis_index(axis)
    mine = lax.dynamic_index_in_dim(hidden, place, 0, keepdims=True)
    theirs = lax.dynamic_index_in_dim(hidden, 1 - place, 0, keepdims=True)
    got = lax.ppermute(theirs, axis, [(0, 1), (1, 0)])
    return jnp.where(place == 0, jnp.concatenate([mine, got], axis=2), jnp.concatenate([got, mine], axis=2))


def attend_body(*refs):
    q_ref, valid_ref, live_ref = refs[0], refs[1], refs[2]
    out_ref = refs[-1]
    block_refs = refs[3:-1]
    rows, width = q_ref.shape
    valid = valid_ref[...] > 0.0
    live = live_ref[...] > 0.0
    lanes = lax.broadcasted_iota(jnp.int32, (1, 128), 1)
    for pair in range(width // 128):
        cols = slice(pair * 128, (pair + 1) * 128)
        vcols = slice(width + pair * 128, width + (pair + 1) * 128)
        keys = jnp.concatenate([block[:, cols] for block in block_refs], axis=0)
        vals = jnp.concatenate([block[:, vcols] for block in block_refs], axis=0)
        query = q_ref[:, cols]
        results = []
        for half in range(2):
            mine = (lanes // HD) == half
            scores = lax.dot_general(
                jnp.where(mine, query, jnp.zeros_like(query)),
                keys,
                (((1,), (1,)), ((), ())),
                preferred_element_type=jnp.float32,
            ) / math.sqrt(HD)
            scores = jnp.where(valid, scores, -1e30)
            rowmax = jnp.max(scores, axis=1, keepdims=True)
            weights = jnp.where(valid, jnp.exp(scores - rowmax), 0.0)
            total = jnp.sum(weights, axis=1, keepdims=True)
            summed = jnp.dot(weights.astype(jnp.bfloat16), vals, preferred_element_type=jnp.float32)
            results.append(summed / total)
        both = jnp.where((lanes // HD) == 0, results[0], results[1])
        out_ref[:, cols] = jnp.where(live, both, 0.0).astype(out_ref.dtype)


def fused_attention(query_flat, pieces, key_pos, own_length, query_pos):
    rows, width = query_flat.shape
    keys_total = key_pos.shape[0]
    valid = (key_pos < own_length).astype(jnp.float32).reshape(1, keys_total)
    live = (query_pos < own_length).astype(jnp.float32).reshape(rows, 1)
    return pl.pallas_call(
        attend_body,
        out_shape=jax.ShapeDtypeStruct((rows, width), jnp.bfloat16),
        cost_estimate=pl.CostEstimate(
            flops=8 * rows * keys_total * width,
            bytes_accessed=2 * (rows * width * 2 + keys_total * width * 2),
            transcendentals=2 * rows * keys_total * (width // HD),
        ),
    )(query_flat, valid, live, *pieces)


def gather_line4(x, axis, rows):
    place = lax.axis_index(axis)
    from_below = lax.ppermute(x, axis, [(0, 1), (1, 2), (2, 3)])
    from_above = lax.ppermute(x, axis, [(1, 0), (2, 1), (3, 2)])
    across = lax.ppermute(x, axis, [(0, 2), (1, 3), (2, 0), (3, 1)])
    passed = lax.ppermute(across, axis, [(2, 3), (1, 0)])
    pieces = [
        x,
        across,
        jnp.where(place >= 1, from_below, passed),
        jnp.where(place <= 2, from_above, passed),
    ]
    starts = [place * rows, ((place + 2) % 4) * rows, ((place + 3) % 4) * rows, ((place + 1) % 4) * rows]
    return pieces, starts


def gather_ring(x, axis, rows):
    size = lax.axis_size(axis)
    if size == 4:
        return gather_line4(x, axis, rows)
    place = lax.axis_index(axis)
    pieces, starts = [x], [place * rows]
    for shift in range(1, size):
        pairs = [(i, (i + shift) % size) for i in range(size)]
        pieces.append(lax.ppermute(x, axis, pairs))
        starts.append(((place - shift) % size) * rows)
    return pieces, starts


def attend(carry, piece, start, queries, own_length):
    best, total, accum = carry
    keys_part, vals_part = piece
    count = keys_part.shape[0]
    head_count = queries.shape[1]
    keys_part = keys_part.reshape(count, head_count, HD)
    vals_part = vals_part.reshape(count, head_count, HD)
    scores = jnp.einsum(
        "fhd,nhd->fhn", queries, keys_part, preferred_element_type=jnp.float32
    ) / math.sqrt(HD)
    valid = (start + jnp.arange(count, dtype=jnp.int32) < own_length)[None, None, :]
    scores = jnp.where(valid, scores, -1e30)
    fresh = jnp.maximum(best, jnp.max(scores, axis=2))
    weights = jnp.where(valid, jnp.exp(scores - fresh[:, :, None]), 0.0)
    factor = jnp.exp(best - fresh)
    total = total * factor + jnp.sum(weights, axis=2)
    accum = accum * factor[:, :, None] + jnp.einsum(
        "fhn,nhd->fhd", weights.astype(jnp.bfloat16), vals_part, preferred_element_type=jnp.float32
    )
    return (fresh, total, accum)


def start_state(rows, heads_here):
    return (
        jnp.full((rows, heads_here), -1e30, jnp.float32),
        jnp.zeros((rows, heads_here), jnp.float32),
        jnp.zeros((rows, heads_here, HD), jnp.float32),
    )


def blockwise(carry, all_keys, all_vals, queries, own_length, block_rows):
    block_count = all_keys.shape[0] // block_rows

    def block_step(state, index):
        begin = index * block_rows
        piece = (
            lax.dynamic_slice_in_dim(all_keys, begin, block_rows, 0),
            lax.dynamic_slice_in_dim(all_vals, begin, block_rows, 0),
        )
        return (attend(state, piece, begin, queries, own_length), None)

    final, unused = lax.scan(block_step, carry, jnp.arange(block_count, dtype=jnp.int32))
    return final


def finish(final, query_pos, own_length):
    best, total, accum = final
    result = accum / total[:, :, None]
    query_live = (query_pos < own_length)[:, None, None]
    result = jnp.where(query_live, result, 0.0)
    return result.reshape(result.shape[0], result.shape[1] * HD).astype(jnp.bfloat16)


def per_device(
    frames_in, lengths, conv_weight, conv_bias, norm_gain, norm_shift, w_query, w_key, w_value
):
    record_count, frame_rows, channels = frames_in.shape
    ctx_place = lax.axis_index("ctx")
    positions = ctx_place * frame_rows + jnp.arange(frame_rows, dtype=jnp.int32)
    live = positions[None, :] < lengths[:, None]
    masked = jnp.where(live[:, :, None], frames_in, jnp.zeros((), frames_in.dtype))
    groups_here, kernel_width, group_in, group_out = conv_weight.shape
    half_width = kernel_width // 2
    padded = padded_2(masked, (("ctx", 1),), half_width)
    conv_out = grouped_conv(padded, conv_weight, frame_rows)
    hidden = (
        masked.astype(jnp.float32)
        + jax.nn.gelu(conv_out + conv_bias.astype(jnp.float32), approximate=False)
    ).astype(jnp.bfloat16)
    record = swap_halves(hidden, "fsdp")
    own_length = lax.dynamic_index_in_dim(lengths, lax.axis_index("fsdp"), 0, keepdims=False)
    flat = record[0].astype(jnp.float32)
    centre = jnp.mean(flat, axis=1, keepdims=True)
    spread = jnp.mean((flat - centre) ** 2, axis=1, keepdims=True)
    normed = ((flat - centre) / jnp.sqrt(spread + 1e-05) * norm_gain + norm_shift).astype(
        jnp.bfloat16
    )
    query_flat = jnp.dot(normed, w_query, preferred_element_type=jnp.float32).astype(jnp.bfloat16)
    key_flat = jnp.dot(normed, w_key, preferred_element_type=jnp.float32).astype(jnp.bfloat16)
    val_flat = jnp.dot(normed, w_value, preferred_element_type=jnp.float32).astype(jnp.bfloat16)
    head_count = query_flat.shape[1] // HD
    width = key_flat.shape[1]
    both = jnp.concatenate([key_flat, val_flat], axis=1)
    pieces, starts = gather_ring(both, "ctx", frame_rows)
    key_pos = jnp.concatenate(
        [start + jnp.arange(frame_rows, dtype=jnp.int32) for start in starts]
    )
    result = fused_attention(query_flat, pieces, key_pos, own_length, positions)
    result = result.reshape(1, frame_rows, query_flat.shape[1])
    return (hidden, result)


def solution(mesh):
    in_specs = (
        P("rep", "ctx", "fsdp"),
        P("rep"),
        P("fsdp", None, None, None),
        P("fsdp"),
        P(),
        P(),
        P(),
        P(),
        P(),
    )
    out_specs = (P("rep", "ctx", "fsdp"), P(("rep", "fsdp"), "ctx", None))
    return jax.shard_map(
        per_device, mesh=mesh, in_specs=in_specs, out_specs=out_specs, check_vma=False
    )
```

```python
import math

import jax
import jax.numpy as jnp
from jax import lax
from jax.sharding import PartitionSpec as P
from jax.experimental import pallas as pl
from jax.experimental.pallas import tpu as pltpu

HD = 64


def padded_2(x, sides, width):
    for axis, dim in sides:
        size, length = (lax.axis_size(axis), x.shape[dim])
        up = [(i, (i + 1) % size) for i in range(size - 1)]
        down = [(j, i) for i, j in up]
        last = lax.slice_in_dim(x, length - width, length, axis=dim)
        first = lax.slice_in_dim(x, 0, width, axis=dim)
        before = lax.ppermute(last, axis, up)
        after = lax.ppermute(first, axis, down)
        x = jnp.concatenate([before, x, after], axis=dim)
    return x


def conv_body(x_ref, w_ref, res_ref, bias_ref, out_ref):
    pair_groups, recs, chans, lanes = x_ref.shape
    taps = w_ref.shape[3]
    rows = out_ref.shape[1]
    outs = w_ref.shape[2]

    def one_group(group):
        def octet_step(q, acc):
            base = pl.multiple_of(q * 8, 8)
            hankels = []
            for r in range(recs):
                block = x_ref[group, r, pl.ds(base, 8), :]
                per_chan = []
                for c in range(8):
                    row = jnp.broadcast_to(block[c : c + 1, :], (taps, lanes))
                    rolled = pltpu.roll(row, 0, 1, stride=1, stride_axis=0)
                    per_chan.append(rolled[:, :rows])
                hankels.append(per_chan)
            for pair in range(4):
                rhs = jnp.concatenate(
                    [
                        jnp.concatenate([hankels[r][2 * pair + half] for r in range(recs)], axis=1)
                        for half in range(2)
                    ],
                    axis=0,
                )
                lhs = jnp.concatenate(
                    [w_ref[group, base + 2 * pair], w_ref[group, base + 2 * pair + 1]], axis=1
                )
                acc = acc + jnp.dot(lhs, rhs, preferred_element_type=jnp.float32)
            return acc

        start = jnp.zeros((outs, recs * rows), jnp.float32)
        return lax.fori_loop(0, chans // 8, octet_step, start, unroll=4)

    acc = jnp.concatenate([one_group(group) for group in range(pair_groups)], axis=0)
    across = lax.broadcasted_iota(jnp.int32, (rows, rows), 0) + lax.broadcasted_iota(
        jnp.int32, (rows, rows), 1
    )
    flip = jnp.where(across == rows - 1, 1.0, 0.0).astype(jnp.bfloat16)
    dims = (((1,), (1,)), ((), ()))
    for r in range(recs):
        part = acc[:, r * rows : (r + 1) * rows]
        high = part.astype(jnp.bfloat16)
        rest = part - high.astype(jnp.float32)
        middle = rest.astype(jnp.bfloat16)
        low = (rest - middle.astype(jnp.float32)).astype(jnp.bfloat16)
        total = lax.dot_general(flip, high, dims, preferred_element_type=jnp.float32)
        total = total + lax.dot_general(flip, middle, dims, preferred_element_type=jnp.float32)
        conv = total + lax.dot_general(flip, low, dims, preferred_element_type=jnp.float32)
        shifted = conv + bias_ref[...]
        gelu = 0.5 * shifted * (1.0 + lax.erf(shifted * (1.0 / math.sqrt(2.0))))
        hidden = res_ref[r].astype(jnp.float32) + gelu
        out_ref[r] = hidden.astype(out_ref.dtype)


def hankel_conv(xt, wv, residual, bias, rows):
    groups, recs, chans, lanes = xt.shape
    taps, outs = wv.shape[3], wv.shape[2]
    return pl.pallas_call(
        conv_body,
        grid=(groups // 2,),
        in_specs=[
            pl.BlockSpec((2, recs, chans, lanes), lambda g: (g, 0, 0, 0)),
            pl.BlockSpec((2, chans, outs, taps), lambda g: (g, 0, 0, 0)),
            pl.BlockSpec((recs, rows, 2 * outs), lambda g: (0, 0, g)),
            pl.BlockSpec((1, 2 * outs), lambda g: (0, g)),
        ],
        out_specs=pl.BlockSpec((recs, rows, 2 * outs), lambda g: (0, 0, g)),
        out_shape=jax.ShapeDtypeStruct((recs, rows, groups * outs), jnp.bfloat16),
        cost_estimate=pl.CostEstimate(
            flops=2 * groups * recs * rows * taps * chans * outs,
            bytes_accessed=xt.size * 2 + wv.size * 2 + groups * recs * rows * outs * 4,
            transcendentals=recs * rows * groups * outs,
        ),
    )(xt, wv, residual, bias)


def grouped_conv(padded, conv_weight, masked, conv_bias, frame_rows):
    recs, span = padded.shape[0], padded.shape[1]
    groups_here, taps, group_in, group_out = conv_weight.shape
    lanes = -(-(frame_rows + taps - 1) // 128) * 128
    grouped = jnp.pad(padded, ((0, 0), (0, lanes - span), (0, 0)))
    grouped = jnp.roll(jnp.flip(grouped, axis=1), frame_rows - lanes, axis=1)
    grouped = grouped.reshape(recs, lanes, groups_here, group_in).transpose(2, 0, 3, 1)
    bias = conv_bias.astype(jnp.float32).reshape(1, -1)
    return hankel_conv(grouped, jnp.transpose(conv_weight, (0, 2, 3, 1)), masked, bias, frame_rows)


def swap_halves(hidden, axis):
    if lax.axis_size(axis) != 2 or hidden.shape[0] != 2:
        return lax.all_to_all(hidden, axis, split_axis=0, concat_axis=2, tiled=True)
    place = lax.axis_index(axis)
    mine = lax.dynamic_index_in_dim(hidden, place, 0, keepdims=True)
    theirs = lax.dynamic_index_in_dim(hidden, 1 - place, 0, keepdims=True)
    got = lax.ppermute(theirs, axis, [(0, 1), (1, 0)])
    return jnp.where(place == 0, jnp.concatenate([mine, got], axis=2), jnp.concatenate([got, mine], axis=2))


def attend_body(*refs):
    q_ref, valid_ref, live_ref = refs[0], refs[1], refs[2]
    out_ref = refs[-1]
    block_refs = refs[3:-1]
    rows, width = q_ref.shape
    valid = valid_ref[...] > 0.0
    live = live_ref[...] > 0.0
    lanes = lax.broadcasted_iota(jnp.int32, (1, 128), 1)
    for pair in range(width // 128):
        cols = slice(pair * 128, (pair + 1) * 128)
        vcols = slice(width + pair * 128, width + (pair + 1) * 128)
        keys = jnp.concatenate([block[:, cols] for block in block_refs], axis=0)
        vals = jnp.concatenate([block[:, vcols] for block in block_refs], axis=0)
        query = q_ref[:, cols]
        results = []
        for half in range(2):
            mine = (lanes // HD) == half
            scores = lax.dot_general(
                jnp.where(mine, query, jnp.zeros_like(query)),
                keys,
                (((1,), (1,)), ((), ())),
                preferred_element_type=jnp.float32,
            ) / math.sqrt(HD)
            scores = jnp.where(valid, scores, -1e30)
            rowmax = jnp.max(scores, axis=1, keepdims=True)
            weights = jnp.where(valid, jnp.exp(scores - rowmax), 0.0)
            total = jnp.sum(weights, axis=1, keepdims=True)
            summed = jnp.dot(weights.astype(jnp.bfloat16), vals, preferred_element_type=jnp.float32)
            results.append(summed / total)
        both = jnp.where((lanes // HD) == 0, results[0], results[1])
        out_ref[:, cols] = jnp.where(live, both, 0.0).astype(out_ref.dtype)


def fused_attention(query_flat, pieces, key_pos, own_length, query_pos):
    rows, width = query_flat.shape
    keys_total = key_pos.shape[0]
    valid = (key_pos < own_length).astype(jnp.float32).reshape(1, keys_total)
    live = (query_pos < own_length).astype(jnp.float32).reshape(rows, 1)
    return pl.pallas_call(
        attend_body,
        out_shape=jax.ShapeDtypeStruct((rows, width), jnp.bfloat16),
        cost_estimate=pl.CostEstimate(
            flops=8 * rows * keys_total * width,
            bytes_accessed=2 * (rows * width * 2 + keys_total * width * 2),
            transcendentals=2 * rows * keys_total * (width // HD),
        ),
    )(query_flat, valid, live, *pieces)


def gather_line4(x, axis, rows):
    place = lax.axis_index(axis)
    from_below = lax.ppermute(x, axis, [(0, 1), (1, 2), (2, 3)])
    from_above = lax.ppermute(x, axis, [(1, 0), (2, 1), (3, 2)])
    across = lax.ppermute(x, axis, [(0, 2), (1, 3), (2, 0), (3, 1)])
    passed = lax.ppermute(across, axis, [(2, 3), (1, 0)])
    pieces = [
        x,
        across,
        jnp.where(place >= 1, from_below, passed),
        jnp.where(place <= 2, from_above, passed),
    ]
    starts = [place * rows, ((place + 2) % 4) * rows, ((place + 3) % 4) * rows, ((place + 1) % 4) * rows]
    return pieces, starts


def gather_ring(x, axis, rows):
    size = lax.axis_size(axis)
    if size == 4:
        return gather_line4(x, axis, rows)
    place = lax.axis_index(axis)
    pieces, starts = [x], [place * rows]
    for shift in range(1, size):
        pairs = [(i, (i + shift) % size) for i in range(size)]
        pieces.append(lax.ppermute(x, axis, pairs))
        starts.append(((place - shift) % size) * rows)
    return pieces, starts


def attend(carry, piece, start, queries, own_length):
    best, total, accum = carry
    keys_part, vals_part = piece
    count = keys_part.shape[0]
    head_count = queries.shape[1]
    keys_part = keys_part.reshape(count, head_count, HD)
    vals_part = vals_part.reshape(count, head_count, HD)
    scores = jnp.einsum(
        "fhd,nhd->fhn", queries, keys_part, preferred_element_type=jnp.float32
    ) / math.sqrt(HD)
    valid = (start + jnp.arange(count, dtype=jnp.int32) < own_length)[None, None, :]
    scores = jnp.where(valid, scores, -1e30)
    fresh = jnp.maximum(best, jnp.max(scores, axis=2))
    weights = jnp.where(valid, jnp.exp(scores - fresh[:, :, None]), 0.0)
    factor = jnp.exp(best - fresh)
    total = total * factor + jnp.sum(weights, axis=2)
    accum = accum * factor[:, :, None] + jnp.einsum(
        "fhn,nhd->fhd", weights.astype(jnp.bfloat16), vals_part, preferred_element_type=jnp.float32
    )
    return (fresh, total, accum)


def start_state(rows, heads_here):
    return (
        jnp.full((rows, heads_here), -1e30, jnp.float32),
        jnp.zeros((rows, heads_here), jnp.float32),
        jnp.zeros((rows, heads_here, HD), jnp.float32),
    )


def blockwise(carry, all_keys, all_vals, queries, own_length, block_rows):
    block_count = all_keys.shape[0] // block_rows

    def block_step(state, index):
        begin = index * block_rows
        piece = (
            lax.dynamic_slice_in_dim(all_keys, begin, block_rows, 0),
            lax.dynamic_slice_in_dim(all_vals, begin, block_rows, 0),
        )
        return (attend(state, piece, begin, queries, own_length), None)

    final, unused = lax.scan(block_step, carry, jnp.arange(block_count, dtype=jnp.int32))
    return final


def finish(final, query_pos, own_length):
    best, total, accum = final
    result = accum / total[:, :, None]
    query_live = (query_pos < own_length)[:, None, None]
    result = jnp.where(query_live, result, 0.0)
    return result.reshape(result.shape[0], result.shape[1] * HD).astype(jnp.bfloat16)


def per_device(
    frames_in, lengths, conv_weight, conv_bias, norm_gain, norm_shift, w_query, w_key, w_value
):
    record_count, frame_rows, channels = frames_in.shape
    ctx_place = lax.axis_index("ctx")
    positions = ctx_place * frame_rows + jnp.arange(frame_rows, dtype=jnp.int32)
    live = positions[None, :] < lengths[:, None]
    masked = jnp.where(live[:, :, None], frames_in, jnp.zeros((), frames_in.dtype))
    groups_here, kernel_width, group_in, group_out = conv_weight.shape
    half_width = kernel_width // 2
    padded = padded_2(masked, (("ctx", 1),), half_width)
    hidden = grouped_conv(padded, conv_weight, masked, conv_bias, frame_rows)
    record = swap_halves(hidden, "fsdp")
    own_length = lax.dynamic_index_in_dim(lengths, lax.axis_index("fsdp"), 0, keepdims=False)
    flat = record[0].astype(jnp.float32)
    centre = jnp.mean(flat, axis=1, keepdims=True)
    spread = jnp.mean((flat - centre) ** 2, axis=1, keepdims=True)
    normed = ((flat - centre) / jnp.sqrt(spread + 1e-05) * norm_gain + norm_shift).astype(
        jnp.bfloat16
    )
    query_flat = jnp.dot(normed, w_query, preferred_element_type=jnp.float32).astype(jnp.bfloat16)
    key_flat = jnp.dot(normed, w_key, preferred_element_type=jnp.float32).astype(jnp.bfloat16)
    val_flat = jnp.dot(normed, w_value, preferred_element_type=jnp.float32).astype(jnp.bfloat16)
    head_count = query_flat.shape[1] // HD
    width = key_flat.shape[1]
    both = jnp.concatenate([key_flat, val_flat], axis=1)
    pieces, starts = gather_ring(both, "ctx", frame_rows)
    key_pos = jnp.concatenate(
        [start + jnp.arange(frame_rows, dtype=jnp.int32) for start in starts]
    )
    result = fused_attention(query_flat, pieces, key_pos, own_length, positions)
    result = result.reshape(1, frame_rows, query_flat.shape[1])
    return (hidden, result)


def solution(mesh):
    in_specs = (
        P("rep", "ctx", "fsdp"),
        P("rep"),
        P("fsdp", None, None, None),
        P("fsdp"),
        P(),
        P(),
        P(),
        P(),
        P(),
    )
    out_specs = (P("rep", "ctx", "fsdp"), P(("rep", "fsdp"), "ctx", None))
    return jax.shard_map(
        per_device, mesh=mesh, in_specs=in_specs, out_specs=out_specs, check_vma=False
    )
```

```python
import math

import jax
import jax.numpy as jnp
from jax import lax
from jax.sharding import PartitionSpec as P
from jax.experimental import pallas as pl
from jax.experimental.pallas import tpu as pltpu

HD = 64


def halo_masked(frames_in, masked, lengths, axis, width):
    size, place = lax.axis_size(axis), lax.axis_index(axis)
    rows = frames_in.shape[1]
    up = [(i, i + 1) for i in range(size - 1)]
    down = [(i + 1, i) for i in range(size - 1)]
    before = lax.ppermute(frames_in[:, rows - width :], axis, up)
    after = lax.ppermute(frames_in[:, :width], axis, down)
    steps = jnp.arange(width, dtype=jnp.int32)
    keep_before = (place * rows - width + steps)[None, :] < lengths[:, None]
    keep_after = ((place + 1) * rows + steps)[None, :] < lengths[:, None]
    zero = jnp.zeros((), frames_in.dtype)
    before = jnp.where(keep_before[:, :, None], before, zero)
    after = jnp.where(keep_after[:, :, None], after, zero)
    return jnp.concatenate([before, masked, after], axis=1)


def padded_2(x, sides, width):
    for axis, dim in sides:
        size, length = (lax.axis_size(axis), x.shape[dim])
        up = [(i, (i + 1) % size) for i in range(size - 1)]
        down = [(j, i) for i, j in up]
        last = lax.slice_in_dim(x, length - width, length, axis=dim)
        first = lax.slice_in_dim(x, 0, width, axis=dim)
        before = lax.ppermute(last, axis, up)
        after = lax.ppermute(first, axis, down)
        x = jnp.concatenate([before, x, after], axis=dim)
    return x


def conv_body(x_ref, w_ref, res_ref, bias_ref, out_ref):
    pair_groups, recs, chans, lanes = x_ref.shape
    taps = w_ref.shape[3]
    rows = out_ref.shape[1]
    outs = w_ref.shape[2]

    def one_group(group):
        def octet_step(q, acc):
            base = pl.multiple_of(q * 8, 8)
            hankels = []
            for r in range(recs):
                block = x_ref[group, r, pl.ds(base, 8), :]
                per_chan = []
                for c in range(8):
                    row = jnp.broadcast_to(block[c : c + 1, :], (taps, lanes))
                    rolled = pltpu.roll(row, 0, 1, stride=1, stride_axis=0)
                    per_chan.append(rolled[:, :rows])
                hankels.append(per_chan)
            for pair in range(4):
                rhs = jnp.concatenate(
                    [
                        jnp.concatenate([hankels[r][2 * pair + half] for r in range(recs)], axis=1)
                        for half in range(2)
                    ],
                    axis=0,
                )
                lhs = jnp.concatenate(
                    [w_ref[group, base + 2 * pair], w_ref[group, base + 2 * pair + 1]], axis=1
                )
                acc = acc + jnp.dot(lhs, rhs, preferred_element_type=jnp.float32)
            return acc

        start = jnp.zeros((outs, recs * rows), jnp.float32)
        return lax.fori_loop(0, chans // 8, octet_step, start, unroll=4)

    acc = jnp.concatenate([one_group(group) for group in range(pair_groups)], axis=0)
    across = lax.broadcasted_iota(jnp.int32, (rows, rows), 0) + lax.broadcasted_iota(
        jnp.int32, (rows, rows), 1
    )
    flip = jnp.where(across == rows - 1, 1.0, 0.0).astype(jnp.bfloat16)
    dims = (((1,), (1,)), ((), ()))
    for r in range(recs):
        part = acc[:, r * rows : (r + 1) * rows]
        high = part.astype(jnp.bfloat16)
        rest = part - high.astype(jnp.float32)
        middle = rest.astype(jnp.bfloat16)
        low = (rest - middle.astype(jnp.float32)).astype(jnp.bfloat16)
        total = lax.dot_general(flip, high, dims, preferred_element_type=jnp.float32)
        total = total + lax.dot_general(flip, middle, dims, preferred_element_type=jnp.float32)
        conv = total + lax.dot_general(flip, low, dims, preferred_element_type=jnp.float32)
        shifted = conv + bias_ref[...]
        gelu = 0.5 * shifted * (1.0 + lax.erf(shifted * (1.0 / math.sqrt(2.0))))
        hidden = res_ref[r].astype(jnp.float32) + gelu
        out_ref[r] = hidden.astype(out_ref.dtype)


def hankel_conv(xt, wv, residual, bias, rows):
    groups, recs, chans, lanes = xt.shape
    taps, outs = wv.shape[3], wv.shape[2]
    return pl.pallas_call(
        conv_body,
        grid=(groups // 2,),
        in_specs=[
            pl.BlockSpec((2, recs, chans, lanes), lambda g: (g, 0, 0, 0)),
            pl.BlockSpec((2, chans, outs, taps), lambda g: (g, 0, 0, 0)),
            pl.BlockSpec((recs, rows, 2 * outs), lambda g: (0, 0, g)),
            pl.BlockSpec((1, 2 * outs), lambda g: (0, g)),
        ],
        out_specs=pl.BlockSpec((recs, rows, 2 * outs), lambda g: (0, 0, g)),
        out_shape=jax.ShapeDtypeStruct((recs, rows, groups * outs), jnp.bfloat16),
        cost_estimate=pl.CostEstimate(
            flops=2 * groups * recs * rows * taps * chans * outs,
            bytes_accessed=xt.size * 2 + wv.size * 2 + groups * recs * rows * outs * 4,
            transcendentals=recs * rows * groups * outs,
        ),
    )(xt, wv, residual, bias)


def grouped_conv(padded, conv_weight, masked, conv_bias, frame_rows):
    recs, span = padded.shape[0], padded.shape[1]
    groups_here, taps, group_in, group_out = conv_weight.shape
    lanes = -(-(frame_rows + taps - 1) // 128) * 128
    grouped = jnp.pad(padded, ((0, 0), (0, lanes - span), (0, 0)))
    grouped = jnp.roll(jnp.flip(grouped, axis=1), frame_rows - lanes, axis=1)
    grouped = grouped.reshape(recs, lanes, groups_here, group_in).transpose(2, 0, 3, 1)
    bias = conv_bias.astype(jnp.float32).reshape(1, -1)
    return hankel_conv(grouped, jnp.transpose(conv_weight, (0, 2, 3, 1)), masked, bias, frame_rows)


def swap_halves(hidden, axis):
    if lax.axis_size(axis) != 2 or hidden.shape[0] != 2:
        return lax.all_to_all(hidden, axis, split_axis=0, concat_axis=2, tiled=True)
    place = lax.axis_index(axis)
    mine = lax.dynamic_index_in_dim(hidden, place, 0, keepdims=True)
    theirs = lax.dynamic_index_in_dim(hidden, 1 - place, 0, keepdims=True)
    got = lax.ppermute(theirs, axis, [(0, 1), (1, 0)])
    return jnp.where(place == 0, jnp.concatenate([mine, got], axis=2), jnp.concatenate([got, mine], axis=2))


def attend_body(*refs):
    q_ref, valid_ref, live_ref = refs[0], refs[1], refs[2]
    out_ref = refs[-1]
    block_refs = refs[3:-1]
    rows, width = q_ref.shape
    valid = valid_ref[...] > 0.0
    live = live_ref[...] > 0.0
    lanes = lax.broadcasted_iota(jnp.int32, (1, 128), 1)
    for pair in range(width // 128):
        cols = slice(pair * 128, (pair + 1) * 128)
        vcols = slice(width + pair * 128, width + (pair + 1) * 128)
        keys = jnp.concatenate([block[:, cols] for block in block_refs], axis=0)
        vals = jnp.concatenate([block[:, vcols] for block in block_refs], axis=0)
        query = q_ref[:, cols]
        results = []
        for half in range(2):
            mine = (lanes // HD) == half
            scores = lax.dot_general(
                jnp.where(mine, query, jnp.zeros_like(query)),
                keys,
                (((1,), (1,)), ((), ())),
                preferred_element_type=jnp.float32,
            ) / math.sqrt(HD)
            scores = jnp.where(valid, scores, -1e30)
            rowmax = jnp.max(scores, axis=1, keepdims=True)
            weights = jnp.where(valid, jnp.exp(scores - rowmax), 0.0)
            total = jnp.sum(weights, axis=1, keepdims=True)
            summed = jnp.dot(weights.astype(jnp.bfloat16), vals, preferred_element_type=jnp.float32)
            results.append(summed / total)
        both = jnp.where((lanes // HD) == 0, results[0], results[1])
        out_ref[:, cols] = jnp.where(live, both, 0.0).astype(out_ref.dtype)


def fused_attention(query_flat, pieces, key_pos, own_length, query_pos):
    rows, width = query_flat.shape
    keys_total = key_pos.shape[0]
    valid = (key_pos < own_length).astype(jnp.float32).reshape(1, keys_total)
    live = (query_pos < own_length).astype(jnp.float32).reshape(rows, 1)
    return pl.pallas_call(
        attend_body,
        out_shape=jax.ShapeDtypeStruct((rows, width), jnp.bfloat16),
        cost_estimate=pl.CostEstimate(
            flops=8 * rows * keys_total * width,
            bytes_accessed=2 * (rows * width * 2 + keys_total * width * 2),
            transcendentals=2 * rows * keys_total * (width // HD),
        ),
    )(query_flat, valid, live, *pieces)


def gather_line4(x, axis, rows):
    place = lax.axis_index(axis)
    from_below = lax.ppermute(x, axis, [(0, 1), (1, 2), (2, 3)])
    from_above = lax.ppermute(x, axis, [(1, 0), (2, 1), (3, 2)])
    across = lax.ppermute(x, axis, [(0, 2), (1, 3), (2, 0), (3, 1)])
    passed = lax.ppermute(across, axis, [(2, 3), (1, 0)])
    pieces = [
        x,
        across,
        jnp.where(place >= 1, from_below, passed),
        jnp.where(place <= 2, from_above, passed),
    ]
    starts = [place * rows, ((place + 2) % 4) * rows, ((place + 3) % 4) * rows, ((place + 1) % 4) * rows]
    return pieces, starts


def gather_ring(x, axis, rows):
    size = lax.axis_size(axis)
    if size == 4:
        return gather_line4(x, axis, rows)
    place = lax.axis_index(axis)
    pieces, starts = [x], [place * rows]
    for shift in range(1, size):
        pairs = [(i, (i + shift) % size) for i in range(size)]
        pieces.append(lax.ppermute(x, axis, pairs))
        starts.append(((place - shift) % size) * rows)
    return pieces, starts


def attend(carry, piece, start, queries, own_length):
    best, total, accum = carry
    keys_part, vals_part = piece
    count = keys_part.shape[0]
    head_count = queries.shape[1]
    keys_part = keys_part.reshape(count, head_count, HD)
    vals_part = vals_part.reshape(count, head_count, HD)
    scores = jnp.einsum(
        "fhd,nhd->fhn", queries, keys_part, preferred_element_type=jnp.float32
    ) / math.sqrt(HD)
    valid = (start + jnp.arange(count, dtype=jnp.int32) < own_length)[None, None, :]
    scores = jnp.where(valid, scores, -1e30)
    fresh = jnp.maximum(best, jnp.max(scores, axis=2))
    weights = jnp.where(valid, jnp.exp(scores - fresh[:, :, None]), 0.0)
    factor = jnp.exp(best - fresh)
    total = total * factor + jnp.sum(weights, axis=2)
    accum = accum * factor[:, :, None] + jnp.einsum(
        "fhn,nhd->fhd", weights.astype(jnp.bfloat16), vals_part, preferred_element_type=jnp.float32
    )
    return (fresh, total, accum)


def start_state(rows, heads_here):
    return (
        jnp.full((rows, heads_here), -1e30, jnp.float32),
        jnp.zeros((rows, heads_here), jnp.float32),
        jnp.zeros((rows, heads_here, HD), jnp.float32),
    )


def blockwise(carry, all_keys, all_vals, queries, own_length, block_rows):
    block_count = all_keys.shape[0] // block_rows

    def block_step(state, index):
        begin = index * block_rows
        piece = (
            lax.dynamic_slice_in_dim(all_keys, begin, block_rows, 0),
            lax.dynamic_slice_in_dim(all_vals, begin, block_rows, 0),
        )
        return (attend(state, piece, begin, queries, own_length), None)

    final, unused = lax.scan(block_step, carry, jnp.arange(block_count, dtype=jnp.int32))
    return final


def finish(final, query_pos, own_length):
    best, total, accum = final
    result = accum / total[:, :, None]
    query_live = (query_pos < own_length)[:, None, None]
    result = jnp.where(query_live, result, 0.0)
    return result.reshape(result.shape[0], result.shape[1] * HD).astype(jnp.bfloat16)


def per_device(
    frames_in, lengths, conv_weight, conv_bias, norm_gain, norm_shift, w_query, w_key, w_value
):
    record_count, frame_rows, channels = frames_in.shape
    ctx_place = lax.axis_index("ctx")
    positions = ctx_place * frame_rows + jnp.arange(frame_rows, dtype=jnp.int32)
    live = positions[None, :] < lengths[:, None]
    masked = jnp.where(live[:, :, None], frames_in, jnp.zeros((), frames_in.dtype))
    groups_here, kernel_width, group_in, group_out = conv_weight.shape
    half_width = kernel_width // 2
    padded = halo_masked(frames_in, masked, lengths, "ctx", half_width)
    hidden = grouped_conv(padded, conv_weight, masked, conv_bias, frame_rows)
    record = swap_halves(hidden, "fsdp")
    own_length = lax.dynamic_index_in_dim(lengths, lax.axis_index("fsdp"), 0, keepdims=False)
    flat = record[0].astype(jnp.float32)
    centre = jnp.mean(flat, axis=1, keepdims=True)
    spread = jnp.mean((flat - centre) ** 2, axis=1, keepdims=True)
    normed = ((flat - centre) / jnp.sqrt(spread + 1e-05) * norm_gain + norm_shift).astype(
        jnp.bfloat16
    )
    query_flat = jnp.dot(normed, w_query, preferred_element_type=jnp.float32).astype(jnp.bfloat16)
    key_flat = jnp.dot(normed, w_key, preferred_element_type=jnp.float32).astype(jnp.bfloat16)
    val_flat = jnp.dot(normed, w_value, preferred_element_type=jnp.float32).astype(jnp.bfloat16)
    head_count = query_flat.shape[1] // HD
    width = key_flat.shape[1]
    both = jnp.concatenate([key_flat, val_flat], axis=1)
    pieces, starts = gather_ring(both, "ctx", frame_rows)
    key_pos = jnp.concatenate(
        [start + jnp.arange(frame_rows, dtype=jnp.int32) for start in starts]
    )
    result = fused_attention(query_flat, pieces, key_pos, own_length, positions)
    result = result.reshape(1, frame_rows, query_flat.shape[1])
    return (hidden, result)


def solution(mesh):
    in_specs = (
        P("rep", "ctx", "fsdp"),
        P("rep"),
        P("fsdp", None, None, None),
        P("fsdp"),
        P(),
        P(),
        P(),
        P(),
        P(),
    )
    out_specs = (P("rep", "ctx", "fsdp"), P(("rep", "fsdp"), "ctx", None))
    return jax.shard_map(
        per_device, mesh=mesh, in_specs=in_specs, out_specs=out_specs, check_vma=False
    )
```

```python
import math

import jax
import jax.numpy as jnp
from jax import lax
from jax.sharding import PartitionSpec as P
from jax.experimental import pallas as pl
from jax.experimental.pallas import tpu as pltpu

HD = 64


def padded_2(x, sides, width):
    for axis, dim in sides:
        size, length = (lax.axis_size(axis), x.shape[dim])
        up = [(i, (i + 1) % size) for i in range(size - 1)]
        down = [(j, i) for i, j in up]
        last = lax.slice_in_dim(x, length - width, length, axis=dim)
        first = lax.slice_in_dim(x, 0, width, axis=dim)
        before = lax.ppermute(last, axis, up)
        after = lax.ppermute(first, axis, down)
        x = jnp.concatenate([before, x, after], axis=dim)
    return x


def conv_body(x_ref, w_ref, res_ref, bias_ref, out_ref):
    pair_groups, recs, chans, lanes = x_ref.shape
    taps = w_ref.shape[3]
    rows = out_ref.shape[1]
    outs = w_ref.shape[2]

    def octet_step(group, q, acc):
        base = pl.multiple_of(q * 8, 8)
        hankels = []
        for r in range(recs):
            block = x_ref[group, r, pl.ds(base, 8), :]
            per_chan = []
            for c in range(8):
                row = jnp.broadcast_to(block[c : c + 1, :], (taps, lanes))
                rolled = pltpu.roll(row, 0, 1, stride=1, stride_axis=0)
                per_chan.append(rolled[:, :rows])
            hankels.append(per_chan)
        for pair in range(4):
            rhs = jnp.concatenate(
                [
                    jnp.concatenate([hankels[r][2 * pair + half] for r in range(recs)], axis=1)
                    for half in range(2)
                ],
                axis=0,
            )
            lhs = jnp.concatenate(
                [w_ref[group, base + 2 * pair], w_ref[group, base + 2 * pair + 1]], axis=1
            )
            acc = acc + jnp.dot(lhs, rhs, preferred_element_type=jnp.float32)
        return acc

    def both_groups(q, accs):
        return tuple(octet_step(group, q, acc) for group, acc in enumerate(accs))

    start = tuple(jnp.zeros((outs, recs * rows), jnp.float32) for _ in range(pair_groups))
    accs = lax.fori_loop(0, chans // 8, both_groups, start, unroll=2)
    acc = jnp.concatenate(accs, axis=0)
    across = lax.broadcasted_iota(jnp.int32, (rows, rows), 0) + lax.broadcasted_iota(
        jnp.int32, (rows, rows), 1
    )
    flip = jnp.where(across == rows - 1, 1.0, 0.0).astype(jnp.bfloat16)
    dims = (((1,), (1,)), ((), ()))
    for r in range(recs):
        part = acc[:, r * rows : (r + 1) * rows]
        high = part.astype(jnp.bfloat16)
        rest = part - high.astype(jnp.float32)
        middle = rest.astype(jnp.bfloat16)
        low = (rest - middle.astype(jnp.float32)).astype(jnp.bfloat16)
        total = lax.dot_general(flip, high, dims, preferred_element_type=jnp.float32)
        total = total + lax.dot_general(flip, middle, dims, preferred_element_type=jnp.float32)
        conv = total + lax.dot_general(flip, low, dims, preferred_element_type=jnp.float32)
        shifted = conv + bias_ref[...]
        gelu = 0.5 * shifted * (1.0 + lax.erf(shifted * (1.0 / math.sqrt(2.0))))
        hidden = res_ref[r].astype(jnp.float32) + gelu
        out_ref[r] = hidden.astype(out_ref.dtype)


def hankel_conv(xt, wv, residual, bias, rows):
    groups, recs, chans, lanes = xt.shape
    taps, outs = wv.shape[3], wv.shape[2]
    return pl.pallas_call(
        conv_body,
        grid=(groups // 2,),
        in_specs=[
            pl.BlockSpec((2, recs, chans, lanes), lambda g: (g, 0, 0, 0)),
            pl.BlockSpec((2, chans, outs, taps), lambda g: (g, 0, 0, 0)),
            pl.BlockSpec((recs, rows, 2 * outs), lambda g: (0, 0, g)),
            pl.BlockSpec((1, 2 * outs), lambda g: (0, g)),
        ],
        out_specs=pl.BlockSpec((recs, rows, 2 * outs), lambda g: (0, 0, g)),
        out_shape=jax.ShapeDtypeStruct((recs, rows, groups * outs), jnp.bfloat16),
        cost_estimate=pl.CostEstimate(
            flops=2 * groups * recs * rows * taps * chans * outs,
            bytes_accessed=xt.size * 2 + wv.size * 2 + groups * recs * rows * outs * 4,
            transcendentals=recs * rows * groups * outs,
        ),
    )(xt, wv, residual, bias)


def grouped_conv(padded, conv_weight, masked, conv_bias, frame_rows):
    recs, span = padded.shape[0], padded.shape[1]
    groups_here, taps, group_in, group_out = conv_weight.shape
    lanes = -(-(frame_rows + taps - 1) // 128) * 128
    grouped = jnp.pad(padded, ((0, 0), (0, lanes - span), (0, 0)))
    grouped = jnp.roll(jnp.flip(grouped, axis=1), frame_rows - lanes, axis=1)
    grouped = grouped.reshape(recs, lanes, groups_here, group_in).transpose(2, 0, 3, 1)
    bias = conv_bias.astype(jnp.float32).reshape(1, -1)
    return hankel_conv(grouped, jnp.transpose(conv_weight, (0, 2, 3, 1)), masked, bias, frame_rows)


def swap_halves(hidden, axis):
    if lax.axis_size(axis) != 2 or hidden.shape[0] != 2:
        return lax.all_to_all(hidden, axis, split_axis=0, concat_axis=2, tiled=True)
    place = lax.axis_index(axis)
    mine = lax.dynamic_index_in_dim(hidden, place, 0, keepdims=True)
    theirs = lax.dynamic_index_in_dim(hidden, 1 - place, 0, keepdims=True)
    got = lax.ppermute(theirs, axis, [(0, 1), (1, 0)])
    return jnp.where(place == 0, jnp.concatenate([mine, got], axis=2), jnp.concatenate([got, mine], axis=2))


def attend_body(*refs):
    q_ref, valid_ref, live_ref = refs[0], refs[1], refs[2]
    out_ref = refs[-1]
    block_refs = refs[3:-1]
    rows, width = q_ref.shape
    valid = valid_ref[...] > 0.0
    live = live_ref[...] > 0.0
    lanes = lax.broadcasted_iota(jnp.int32, (1, 128), 1)
    for pair in range(width // 128):
        cols = slice(pair * 128, (pair + 1) * 128)
        vcols = slice(width + pair * 128, width + (pair + 1) * 128)
        keys = jnp.concatenate([block[:, cols] for block in block_refs], axis=0)
        vals = jnp.concatenate([block[:, vcols] for block in block_refs], axis=0)
        query = q_ref[:, cols]
        results = []
        for half in range(2):
            mine = (lanes // HD) == half
            scores = lax.dot_general(
                jnp.where(mine, query, jnp.zeros_like(query)),
                keys,
                (((1,), (1,)), ((), ())),
                preferred_element_type=jnp.float32,
            ) / math.sqrt(HD)
            scores = jnp.where(valid, scores, -1e30)
            rowmax = jnp.max(scores, axis=1, keepdims=True)
            weights = jnp.where(valid, jnp.exp(scores - rowmax), 0.0)
            total = jnp.sum(weights, axis=1, keepdims=True)
            summed = jnp.dot(weights.astype(jnp.bfloat16), vals, preferred_element_type=jnp.float32)
            results.append(summed / total)
        both = jnp.where((lanes // HD) == 0, results[0], results[1])
        out_ref[:, cols] = jnp.where(live, both, 0.0).astype(out_ref.dtype)


def fused_attention(query_flat, pieces, key_pos, own_length, query_pos):
    rows, width = query_flat.shape
    keys_total = key_pos.shape[0]
    valid = (key_pos < own_length).astype(jnp.float32).reshape(1, keys_total)
    live = (query_pos < own_length).astype(jnp.float32).reshape(rows, 1)
    return pl.pallas_call(
        attend_body,
        out_shape=jax.ShapeDtypeStruct((rows, width), jnp.bfloat16),
        cost_estimate=pl.CostEstimate(
            flops=8 * rows * keys_total * width,
            bytes_accessed=2 * (rows * width * 2 + keys_total * width * 2),
            transcendentals=2 * rows * keys_total * (width // HD),
        ),
    )(query_flat, valid, live, *pieces)


def gather_line4(x, axis, rows):
    place = lax.axis_index(axis)
    from_below = lax.ppermute(x, axis, [(0, 1), (1, 2), (2, 3)])
    from_above = lax.ppermute(x, axis, [(1, 0), (2, 1), (3, 2)])
    across = lax.ppermute(x, axis, [(0, 2), (1, 3), (2, 0), (3, 1)])
    passed = lax.ppermute(across, axis, [(2, 3), (1, 0)])
    pieces = [
        x,
        across,
        jnp.where(place >= 1, from_below, passed),
        jnp.where(place <= 2, from_above, passed),
    ]
    starts = [place * rows, ((place + 2) % 4) * rows, ((place + 3) % 4) * rows, ((place + 1) % 4) * rows]
    return pieces, starts


def gather_ring(x, axis, rows):
    size = lax.axis_size(axis)
    if size == 4:
        return gather_line4(x, axis, rows)
    place = lax.axis_index(axis)
    pieces, starts = [x], [place * rows]
    for shift in range(1, size):
        pairs = [(i, (i + shift) % size) for i in range(size)]
        pieces.append(lax.ppermute(x, axis, pairs))
        starts.append(((place - shift) % size) * rows)
    return pieces, starts


def attend(carry, piece, start, queries, own_length):
    best, total, accum = carry
    keys_part, vals_part = piece
    count = keys_part.shape[0]
    head_count = queries.shape[1]
    keys_part = keys_part.reshape(count, head_count, HD)
    vals_part = vals_part.reshape(count, head_count, HD)
    scores = jnp.einsum(
        "fhd,nhd->fhn", queries, keys_part, preferred_element_type=jnp.float32
    ) / math.sqrt(HD)
    valid = (start + jnp.arange(count, dtype=jnp.int32) < own_length)[None, None, :]
    scores = jnp.where(valid, scores, -1e30)
    fresh = jnp.maximum(best, jnp.max(scores, axis=2))
    weights = jnp.where(valid, jnp.exp(scores - fresh[:, :, None]), 0.0)
    factor = jnp.exp(best - fresh)
    total = total * factor + jnp.sum(weights, axis=2)
    accum = accum * factor[:, :, None] + jnp.einsum(
        "fhn,nhd->fhd", weights.astype(jnp.bfloat16), vals_part, preferred_element_type=jnp.float32
    )
    return (fresh, total, accum)


def start_state(rows, heads_here):
    return (
        jnp.full((rows, heads_here), -1e30, jnp.float32),
        jnp.zeros((rows, heads_here), jnp.float32),
        jnp.zeros((rows, heads_here, HD), jnp.float32),
    )


def blockwise(carry, all_keys, all_vals, queries, own_length, block_rows):
    block_count = all_keys.shape[0] // block_rows

    def block_step(state, index):
        begin = index * block_rows
        piece = (
            lax.dynamic_slice_in_dim(all_keys, begin, block_rows, 0),
            lax.dynamic_slice_in_dim(all_vals, begin, block_rows, 0),
        )
        return (attend(state, piece, begin, queries, own_length), None)

    final, unused = lax.scan(block_step, carry, jnp.arange(block_count, dtype=jnp.int32))
    return final


def finish(final, query_pos, own_length):
    best, total, accum = final
    result = accum / total[:, :, None]
    query_live = (query_pos < own_length)[:, None, None]
    result = jnp.where(query_live, result, 0.0)
    return result.reshape(result.shape[0], result.shape[1] * HD).astype(jnp.bfloat16)


def per_device(
    frames_in, lengths, conv_weight, conv_bias, norm_gain, norm_shift, w_query, w_key, w_value
):
    record_count, frame_rows, channels = frames_in.shape
    ctx_place = lax.axis_index("ctx")
    positions = ctx_place * frame_rows + jnp.arange(frame_rows, dtype=jnp.int32)
    live = positions[None, :] < lengths[:, None]
    masked = jnp.where(live[:, :, None], frames_in, jnp.zeros((), frames_in.dtype))
    groups_here, kernel_width, group_in, group_out = conv_weight.shape
    half_width = kernel_width // 2
    padded = padded_2(masked, (("ctx", 1),), half_width)
    hidden = grouped_conv(padded, conv_weight, masked, conv_bias, frame_rows)
    record = swap_halves(hidden, "fsdp")
    own_length = lax.dynamic_index_in_dim(lengths, lax.axis_index("fsdp"), 0, keepdims=False)
    flat = record[0].astype(jnp.float32)
    centre = jnp.mean(flat, axis=1, keepdims=True)
    spread = jnp.mean((flat - centre) ** 2, axis=1, keepdims=True)
    normed = ((flat - centre) / jnp.sqrt(spread + 1e-05) * norm_gain + norm_shift).astype(
        jnp.bfloat16
    )
    query_flat = jnp.dot(normed, w_query, preferred_element_type=jnp.float32).astype(jnp.bfloat16)
    key_flat = jnp.dot(normed, w_key, preferred_element_type=jnp.float32).astype(jnp.bfloat16)
    val_flat = jnp.dot(normed, w_value, preferred_element_type=jnp.float32).astype(jnp.bfloat16)
    head_count = query_flat.shape[1] // HD
    width = key_flat.shape[1]
    both = jnp.concatenate([key_flat, val_flat], axis=1)
    pieces, starts = gather_ring(both, "ctx", frame_rows)
    key_pos = jnp.concatenate(
        [start + jnp.arange(frame_rows, dtype=jnp.int32) for start in starts]
    )
    result = fused_attention(query_flat, pieces, key_pos, own_length, positions)
    result = result.reshape(1, frame_rows, query_flat.shape[1])
    return (hidden, result)


def solution(mesh):
    in_specs = (
        P("rep", "ctx", "fsdp"),
        P("rep"),
        P("fsdp", None, None, None),
        P("fsdp"),
        P(),
        P(),
        P(),
        P(),
        P(),
    )
    out_specs = (P("rep", "ctx", "fsdp"), P(("rep", "fsdp"), "ctx", None))
    return jax.shard_map(
        per_device, mesh=mesh, in_specs=in_specs, out_specs=out_specs, check_vma=False
    )
```

```python
import math

import jax
import jax.numpy as jnp
from jax import lax
from jax.sharding import PartitionSpec as P
from jax.experimental import pallas as pl
from jax.experimental.pallas import tpu as pltpu

HD = 64


def padded_2(x, sides, width):
    for axis, dim in sides:
        size, length = (lax.axis_size(axis), x.shape[dim])
        up = [(i, (i + 1) % size) for i in range(size - 1)]
        down = [(j, i) for i, j in up]
        last = lax.slice_in_dim(x, length - width, length, axis=dim)
        first = lax.slice_in_dim(x, 0, width, axis=dim)
        before = lax.ppermute(last, axis, up)
        after = lax.ppermute(first, axis, down)
        x = jnp.concatenate([before, x, after], axis=dim)
    return x


def conv_body(x_ref, w_ref, res_ref, bias_ref, out_ref):
    pair_groups, recs, chans, lanes = x_ref.shape
    taps = w_ref.shape[3]
    rows = out_ref.shape[1]
    outs = w_ref.shape[2]

    def octet_step(group, q, acc):
        base = pl.multiple_of(q * 8, 8)
        hankels = []
        for r in range(recs):
            block = x_ref[group, r, pl.ds(base, 8), :]
            per_chan = []
            for c in range(8):
                row = jnp.broadcast_to(block[c : c + 1, :], (taps, lanes))
                rolled = pltpu.roll(row, 0, 1, stride=1, stride_axis=0)
                per_chan.append(rolled[:, :rows])
            hankels.append(per_chan)
        for pair in range(4):
            rhs = jnp.concatenate(
                [
                    jnp.concatenate([hankels[r][2 * pair + half] for r in range(recs)], axis=1)
                    for half in range(2)
                ],
                axis=0,
            )
            lhs = jnp.concatenate(
                [w_ref[group, base + 2 * pair], w_ref[group, base + 2 * pair + 1]], axis=1
            )
            acc = acc + jnp.dot(lhs, rhs, preferred_element_type=jnp.float32)
        return acc

    def both_groups(q, accs):
        return tuple(octet_step(group, q, acc) for group, acc in enumerate(accs))

    start = tuple(jnp.zeros((outs, recs * rows), jnp.float32) for _ in range(pair_groups))
    accs = lax.fori_loop(0, chans // 8, both_groups, start, unroll=4)
    acc = jnp.concatenate(accs, axis=0)
    across = lax.broadcasted_iota(jnp.int32, (rows, rows), 0) + lax.broadcasted_iota(
        jnp.int32, (rows, rows), 1
    )
    flip = jnp.where(across == rows - 1, 1.0, 0.0).astype(jnp.bfloat16)
    dims = (((1,), (1,)), ((), ()))
    for r in range(recs):
        part = acc[:, r * rows : (r + 1) * rows]
        high = part.astype(jnp.bfloat16)
        rest = part - high.astype(jnp.float32)
        middle = rest.astype(jnp.bfloat16)
        low = (rest - middle.astype(jnp.float32)).astype(jnp.bfloat16)
        total = lax.dot_general(flip, high, dims, preferred_element_type=jnp.float32)
        total = total + lax.dot_general(flip, middle, dims, preferred_element_type=jnp.float32)
        conv = total + lax.dot_general(flip, low, dims, preferred_element_type=jnp.float32)
        shifted = conv + bias_ref[...]
        gelu = 0.5 * shifted * (1.0 + lax.erf(shifted * (1.0 / math.sqrt(2.0))))
        hidden = res_ref[r].astype(jnp.float32) + gelu
        out_ref[r] = hidden.astype(out_ref.dtype)


def hankel_conv(xt, wv, residual, bias, rows):
    groups, recs, chans, lanes = xt.shape
    taps, outs = wv.shape[3], wv.shape[2]
    return pl.pallas_call(
        conv_body,
        grid=(groups // 2,),
        in_specs=[
            pl.BlockSpec((2, recs, chans, lanes), lambda g: (g, 0, 0, 0)),
            pl.BlockSpec((2, chans, outs, taps), lambda g: (g, 0, 0, 0)),
            pl.BlockSpec((recs, rows, 2 * outs), lambda g: (0, 0, g)),
            pl.BlockSpec((1, 2 * outs), lambda g: (0, g)),
        ],
        out_specs=pl.BlockSpec((recs, rows, 2 * outs), lambda g: (0, 0, g)),
        out_shape=jax.ShapeDtypeStruct((recs, rows, groups * outs), jnp.bfloat16),
        cost_estimate=pl.CostEstimate(
            flops=2 * groups * recs * rows * taps * chans * outs,
            bytes_accessed=xt.size * 2 + wv.size * 2 + groups * recs * rows * outs * 4,
            transcendentals=recs * rows * groups * outs,
        ),
    )(xt, wv, residual, bias)


def grouped_conv(padded, conv_weight, masked, conv_bias, frame_rows):
    recs, span = padded.shape[0], padded.shape[1]
    groups_here, taps, group_in, group_out = conv_weight.shape
    lanes = -(-(frame_rows + taps - 1) // 128) * 128
    grouped = jnp.pad(padded, ((0, 0), (0, lanes - span), (0, 0)))
    grouped = jnp.roll(jnp.flip(grouped, axis=1), frame_rows - lanes, axis=1)
    grouped = grouped.reshape(recs, lanes, groups_here, group_in).transpose(2, 0, 3, 1)
    bias = conv_bias.astype(jnp.float32).reshape(1, -1)
    return hankel_conv(grouped, jnp.transpose(conv_weight, (0, 2, 3, 1)), masked, bias, frame_rows)


def swap_halves(hidden, axis):
    if lax.axis_size(axis) != 2 or hidden.shape[0] != 2:
        return lax.all_to_all(hidden, axis, split_axis=0, concat_axis=2, tiled=True)
    place = lax.axis_index(axis)
    mine = lax.dynamic_index_in_dim(hidden, place, 0, keepdims=True)
    theirs = lax.dynamic_index_in_dim(hidden, 1 - place, 0, keepdims=True)
    got = lax.ppermute(theirs, axis, [(0, 1), (1, 0)])
    return jnp.where(place == 0, jnp.concatenate([mine, got], axis=2), jnp.concatenate([got, mine], axis=2))


def attend_body(*refs):
    q_ref, valid_ref, live_ref = refs[0], refs[1], refs[2]
    out_ref = refs[-1]
    block_refs = refs[3:-1]
    rows, width = q_ref.shape
    valid = valid_ref[...] > 0.0
    live = live_ref[...] > 0.0
    lanes = lax.broadcasted_iota(jnp.int32, (1, 128), 1)
    for pair in range(width // 128):
        cols = slice(pair * 128, (pair + 1) * 128)
        vcols = slice(width + pair * 128, width + (pair + 1) * 128)
        keys = jnp.concatenate([block[:, cols] for block in block_refs], axis=0)
        vals = jnp.concatenate([block[:, vcols] for block in block_refs], axis=0)
        query = q_ref[:, cols]
        results = []
        for half in range(2):
            mine = (lanes // HD) == half
            scores = lax.dot_general(
                jnp.where(mine, query, jnp.zeros_like(query)),
                keys,
                (((1,), (1,)), ((), ())),
                preferred_element_type=jnp.float32,
            ) / math.sqrt(HD)
            scores = jnp.where(valid, scores, -1e30)
            rowmax = jnp.max(scores, axis=1, keepdims=True)
            weights = jnp.where(valid, jnp.exp(scores - rowmax), 0.0)
            total = jnp.sum(weights, axis=1, keepdims=True)
            summed = jnp.dot(weights.astype(jnp.bfloat16), vals, preferred_element_type=jnp.float32)
            results.append(summed / total)
        both = jnp.where((lanes // HD) == 0, results[0], results[1])
        out_ref[:, cols] = jnp.where(live, both, 0.0).astype(out_ref.dtype)


def fused_attention(query_flat, pieces, key_pos, own_length, query_pos):
    rows, width = query_flat.shape
    keys_total = key_pos.shape[0]
    valid = (key_pos < own_length).astype(jnp.float32).reshape(1, keys_total)
    live = (query_pos < own_length).astype(jnp.float32).reshape(rows, 1)
    return pl.pallas_call(
        attend_body,
        out_shape=jax.ShapeDtypeStruct((rows, width), jnp.bfloat16),
        cost_estimate=pl.CostEstimate(
            flops=8 * rows * keys_total * width,
            bytes_accessed=2 * (rows * width * 2 + keys_total * width * 2),
            transcendentals=2 * rows * keys_total * (width // HD),
        ),
    )(query_flat, valid, live, *pieces)


def gather_line4(x, axis, rows):
    place = lax.axis_index(axis)
    from_below = lax.ppermute(x, axis, [(0, 1), (1, 2), (2, 3)])
    from_above = lax.ppermute(x, axis, [(1, 0), (2, 1), (3, 2)])
    across = lax.ppermute(x, axis, [(0, 2), (1, 3), (2, 0), (3, 1)])
    passed = lax.ppermute(across, axis, [(2, 3), (1, 0)])
    pieces = [
        x,
        across,
        jnp.where(place >= 1, from_below, passed),
        jnp.where(place <= 2, from_above, passed),
    ]
    starts = [place * rows, ((place + 2) % 4) * rows, ((place + 3) % 4) * rows, ((place + 1) % 4) * rows]
    return pieces, starts


def gather_ring(x, axis, rows):
    size = lax.axis_size(axis)
    if size == 4:
        return gather_line4(x, axis, rows)
    place = lax.axis_index(axis)
    pieces, starts = [x], [place * rows]
    for shift in range(1, size):
        pairs = [(i, (i + shift) % size) for i in range(size)]
        pieces.append(lax.ppermute(x, axis, pairs))
        starts.append(((place - shift) % size) * rows)
    return pieces, starts


def attend(carry, piece, start, queries, own_length):
    best, total, accum = carry
    keys_part, vals_part = piece
    count = keys_part.shape[0]
    head_count = queries.shape[1]
    keys_part = keys_part.reshape(count, head_count, HD)
    vals_part = vals_part.reshape(count, head_count, HD)
    scores = jnp.einsum(
        "fhd,nhd->fhn", queries, keys_part, preferred_element_type=jnp.float32
    ) / math.sqrt(HD)
    valid = (start + jnp.arange(count, dtype=jnp.int32) < own_length)[None, None, :]
    scores = jnp.where(valid, scores, -1e30)
    fresh = jnp.maximum(best, jnp.max(scores, axis=2))
    weights = jnp.where(valid, jnp.exp(scores - fresh[:, :, None]), 0.0)
    factor = jnp.exp(best - fresh)
    total = total * factor + jnp.sum(weights, axis=2)
    accum = accum * factor[:, :, None] + jnp.einsum(
        "fhn,nhd->fhd", weights.astype(jnp.bfloat16), vals_part, preferred_element_type=jnp.float32
    )
    return (fresh, total, accum)


def start_state(rows, heads_here):
    return (
        jnp.full((rows, heads_here), -1e30, jnp.float32),
        jnp.zeros((rows, heads_here), jnp.float32),
        jnp.zeros((rows, heads_here, HD), jnp.float32),
    )


def blockwise(carry, all_keys, all_vals, queries, own_length, block_rows):
    block_count = all_keys.shape[0] // block_rows

    def block_step(state, index):
        begin = index * block_rows
        piece = (
            lax.dynamic_slice_in_dim(all_keys, begin, block_rows, 0),
            lax.dynamic_slice_in_dim(all_vals, begin, block_rows, 0),
        )
        return (attend(state, piece, begin, queries, own_length), None)

    final, unused = lax.scan(block_step, carry, jnp.arange(block_count, dtype=jnp.int32))
    return final


def finish(final, query_pos, own_length):
    best, total, accum = final
    result = accum / total[:, :, None]
    query_live = (query_pos < own_length)[:, None, None]
    result = jnp.where(query_live, result, 0.0)
    return result.reshape(result.shape[0], result.shape[1] * HD).astype(jnp.bfloat16)


def per_device(
    frames_in, lengths, conv_weight, conv_bias, norm_gain, norm_shift, w_query, w_key, w_value
):
    record_count, frame_rows, channels = frames_in.shape
    ctx_place = lax.axis_index("ctx")
    positions = ctx_place * frame_rows + jnp.arange(frame_rows, dtype=jnp.int32)
    live = positions[None, :] < lengths[:, None]
    masked = jnp.where(live[:, :, None], frames_in, jnp.zeros((), frames_in.dtype))
    groups_here, kernel_width, group_in, group_out = conv_weight.shape
    half_width = kernel_width // 2
    padded = padded_2(masked, (("ctx", 1),), half_width)
    hidden = grouped_conv(padded, conv_weight, masked, conv_bias, frame_rows)
    record = swap_halves(hidden, "fsdp")
    own_length = lax.dynamic_index_in_dim(lengths, lax.axis_index("fsdp"), 0, keepdims=False)
    flat = record[0].astype(jnp.float32)
    centre = jnp.mean(flat, axis=1, keepdims=True)
    spread = jnp.mean((flat - centre) ** 2, axis=1, keepdims=True)
    normed = ((flat - centre) / jnp.sqrt(spread + 1e-05) * norm_gain + norm_shift).astype(
        jnp.bfloat16
    )
    query_flat = jnp.dot(normed, w_query, preferred_element_type=jnp.float32).astype(jnp.bfloat16)
    key_flat = jnp.dot(normed, w_key, preferred_element_type=jnp.float32).astype(jnp.bfloat16)
    val_flat = jnp.dot(normed, w_value, preferred_element_type=jnp.float32).astype(jnp.bfloat16)
    head_count = query_flat.shape[1] // HD
    width = key_flat.shape[1]
    both = jnp.concatenate([key_flat, val_flat], axis=1)
    pieces, starts = gather_ring(both, "ctx", frame_rows)
    key_pos = jnp.concatenate(
        [start + jnp.arange(frame_rows, dtype=jnp.int32) for start in starts]
    )
    result = fused_attention(query_flat, pieces, key_pos, own_length, positions)
    result = result.reshape(1, frame_rows, query_flat.shape[1])
    return (hidden, result)


def solution(mesh):
    in_specs = (
        P("rep", "ctx", "fsdp"),
        P("rep"),
        P("fsdp", None, None, None),
        P("fsdp"),
        P(),
        P(),
        P(),
        P(),
        P(),
    )
    out_specs = (P("rep", "ctx", "fsdp"), P(("rep", "fsdp"), "ctx", None))
    return jax.shard_map(
        per_device, mesh=mesh, in_specs=in_specs, out_specs=out_specs, check_vma=False
    )
```

```python
import math

import jax
import jax.numpy as jnp
from jax import lax
from jax.sharding import PartitionSpec as P
from jax.experimental import pallas as pl
from jax.experimental.pallas import tpu as pltpu

HD = 64


def padded_2(x, sides, width):
    for axis, dim in sides:
        size, length = (lax.axis_size(axis), x.shape[dim])
        up = [(i, (i + 1) % size) for i in range(size - 1)]
        down = [(j, i) for i, j in up]
        last = lax.slice_in_dim(x, length - width, length, axis=dim)
        first = lax.slice_in_dim(x, 0, width, axis=dim)
        before = lax.ppermute(last, axis, up)
        after = lax.ppermute(first, axis, down)
        x = jnp.concatenate([before, x, after], axis=dim)
    return x


def conv_body(x_ref, w_ref, res_ref, bias_ref, out_ref):
    pair_groups, recs, chans, lanes = x_ref.shape
    taps = w_ref.shape[3]
    rows = out_ref.shape[1]
    outs = w_ref.shape[2]

    def octet_step(group, q, acc):
        base = pl.multiple_of(q * 8, 8)
        hankels = []
        for r in range(recs):
            block = x_ref[group, r, pl.ds(base, 8), :]
            per_chan = []
            for c in range(8):
                row = jnp.broadcast_to(block[c : c + 1, :], (taps, lanes))
                rolled = pltpu.roll(row, 0, 1, stride=1, stride_axis=0)
                per_chan.append(rolled[:, :rows])
            hankels.append(per_chan)
        for pair in range(4):
            rhs = jnp.concatenate(
                [
                    jnp.concatenate([hankels[r][2 * pair + half] for r in range(recs)], axis=1)
                    for half in range(2)
                ],
                axis=0,
            )
            lhs = jnp.concatenate(
                [w_ref[group, base + 2 * pair], w_ref[group, base + 2 * pair + 1]], axis=1
            )
            acc = acc + jnp.dot(lhs, rhs, preferred_element_type=jnp.float32)
        return acc

    def both_groups(q, accs):
        return tuple(octet_step(group, q, acc) for group, acc in enumerate(accs))

    start = tuple(jnp.zeros((outs, recs * rows), jnp.float32) for _ in range(pair_groups))
    accs = lax.fori_loop(0, chans // 8, both_groups, start, unroll=8)
    acc = jnp.concatenate(accs, axis=0)
    across = lax.broadcasted_iota(jnp.int32, (rows, rows), 0) + lax.broadcasted_iota(
        jnp.int32, (rows, rows), 1
    )
    flip = jnp.where(across == rows - 1, 1.0, 0.0).astype(jnp.bfloat16)
    dims = (((1,), (1,)), ((), ()))
    for r in range(recs):
        part = acc[:, r * rows : (r + 1) * rows]
        high = part.astype(jnp.bfloat16)
        rest = part - high.astype(jnp.float32)
        middle = rest.astype(jnp.bfloat16)
        low = (rest - middle.astype(jnp.float32)).astype(jnp.bfloat16)
        total = lax.dot_general(flip, high, dims, preferred_element_type=jnp.float32)
        total = total + lax.dot_general(flip, middle, dims, preferred_element_type=jnp.float32)
        conv = total + lax.dot_general(flip, low, dims, preferred_element_type=jnp.float32)
        shifted = conv + bias_ref[...]
        gelu = 0.5 * shifted * (1.0 + lax.erf(shifted * (1.0 / math.sqrt(2.0))))
        hidden = res_ref[r].astype(jnp.float32) + gelu
        out_ref[r] = hidden.astype(out_ref.dtype)


def hankel_conv(xt, wv, residual, bias, rows):
    groups, recs, chans, lanes = xt.shape
    taps, outs = wv.shape[3], wv.shape[2]
    return pl.pallas_call(
        conv_body,
        grid=(groups // 2,),
        in_specs=[
            pl.BlockSpec((2, recs, chans, lanes), lambda g: (g, 0, 0, 0)),
            pl.BlockSpec((2, chans, outs, taps), lambda g: (g, 0, 0, 0)),
            pl.BlockSpec((recs, rows, 2 * outs), lambda g: (0, 0, g)),
            pl.BlockSpec((1, 2 * outs), lambda g: (0, g)),
        ],
        out_specs=pl.BlockSpec((recs, rows, 2 * outs), lambda g: (0, 0, g)),
        out_shape=jax.ShapeDtypeStruct((recs, rows, groups * outs), jnp.bfloat16),
        cost_estimate=pl.CostEstimate(
            flops=2 * groups * recs * rows * taps * chans * outs,
            bytes_accessed=xt.size * 2 + wv.size * 2 + groups * recs * rows * outs * 4,
            transcendentals=recs * rows * groups * outs,
        ),
    )(xt, wv, residual, bias)


def grouped_conv(padded, conv_weight, masked, conv_bias, frame_rows):
    recs, span = padded.shape[0], padded.shape[1]
    groups_here, taps, group_in, group_out = conv_weight.shape
    lanes = -(-(frame_rows + taps - 1) // 128) * 128
    grouped = jnp.pad(padded, ((0, 0), (0, lanes - span), (0, 0)))
    grouped = jnp.roll(jnp.flip(grouped, axis=1), frame_rows - lanes, axis=1)
    grouped = grouped.reshape(recs, lanes, groups_here, group_in).transpose(2, 0, 3, 1)
    bias = conv_bias.astype(jnp.float32).reshape(1, -1)
    return hankel_conv(grouped, jnp.transpose(conv_weight, (0, 2, 3, 1)), masked, bias, frame_rows)


def swap_halves(hidden, axis):
    if lax.axis_size(axis) != 2 or hidden.shape[0] != 2:
        return lax.all_to_all(hidden, axis, split_axis=0, concat_axis=2, tiled=True)
    place = lax.axis_index(axis)
    mine = lax.dynamic_index_in_dim(hidden, place, 0, keepdims=True)
    theirs = lax.dynamic_index_in_dim(hidden, 1 - place, 0, keepdims=True)
    got = lax.ppermute(theirs, axis, [(0, 1), (1, 0)])
    return jnp.where(place == 0, jnp.concatenate([mine, got], axis=2), jnp.concatenate([got, mine], axis=2))


def attend_body(*refs):
    q_ref, valid_ref, live_ref = refs[0], refs[1], refs[2]
    out_ref = refs[-1]
    block_refs = refs[3:-1]
    rows, width = q_ref.shape
    valid = valid_ref[...] > 0.0
    live = live_ref[...] > 0.0
    lanes = lax.broadcasted_iota(jnp.int32, (1, 128), 1)
    for pair in range(width // 128):
        cols = slice(pair * 128, (pair + 1) * 128)
        vcols = slice(width + pair * 128, width + (pair + 1) * 128)
        keys = jnp.concatenate([block[:, cols] for block in block_refs], axis=0)
        vals = jnp.concatenate([block[:, vcols] for block in block_refs], axis=0)
        query = q_ref[:, cols]
        results = []
        for half in range(2):
            mine = (lanes // HD) == half
            scores = lax.dot_general(
                jnp.where(mine, query, jnp.zeros_like(query)),
                keys,
                (((1,), (1,)), ((), ())),
                preferred_element_type=jnp.float32,
            ) / math.sqrt(HD)
            scores = jnp.where(valid, scores, -1e30)
            rowmax = jnp.max(scores, axis=1, keepdims=True)
            weights = jnp.where(valid, jnp.exp(scores - rowmax), 0.0)
            total = jnp.sum(weights, axis=1, keepdims=True)
            summed = jnp.dot(weights.astype(jnp.bfloat16), vals, preferred_element_type=jnp.float32)
            results.append(summed / total)
        both = jnp.where((lanes // HD) == 0, results[0], results[1])
        out_ref[:, cols] = jnp.where(live, both, 0.0).astype(out_ref.dtype)


def fused_attention(query_flat, pieces, key_pos, own_length, query_pos):
    rows, width = query_flat.shape
    keys_total = key_pos.shape[0]
    valid = (key_pos < own_length).astype(jnp.float32).reshape(1, keys_total)
    live = (query_pos < own_length).astype(jnp.float32).reshape(rows, 1)
    return pl.pallas_call(
        attend_body,
        out_shape=jax.ShapeDtypeStruct((rows, width), jnp.bfloat16),
        cost_estimate=pl.CostEstimate(
            flops=8 * rows * keys_total * width,
            bytes_accessed=2 * (rows * width * 2 + keys_total * width * 2),
            transcendentals=2 * rows * keys_total * (width // HD),
        ),
    )(query_flat, valid, live, *pieces)


def gather_line4(x, axis, rows):
    place = lax.axis_index(axis)
    from_below = lax.ppermute(x, axis, [(0, 1), (1, 2), (2, 3)])
    from_above = lax.ppermute(x, axis, [(1, 0), (2, 1), (3, 2)])
    across = lax.ppermute(x, axis, [(0, 2), (1, 3), (2, 0), (3, 1)])
    passed = lax.ppermute(across, axis, [(2, 3), (1, 0)])
    pieces = [
        x,
        across,
        jnp.where(place >= 1, from_below, passed),
        jnp.where(place <= 2, from_above, passed),
    ]
    starts = [place * rows, ((place + 2) % 4) * rows, ((place + 3) % 4) * rows, ((place + 1) % 4) * rows]
    return pieces, starts


def gather_ring(x, axis, rows):
    size = lax.axis_size(axis)
    if size == 4:
        return gather_line4(x, axis, rows)
    place = lax.axis_index(axis)
    pieces, starts = [x], [place * rows]
    for shift in range(1, size):
        pairs = [(i, (i + shift) % size) for i in range(size)]
        pieces.append(lax.ppermute(x, axis, pairs))
        starts.append(((place - shift) % size) * rows)
    return pieces, starts


def attend(carry, piece, start, queries, own_length):
    best, total, accum = carry
    keys_part, vals_part = piece
    count = keys_part.shape[0]
    head_count = queries.shape[1]
    keys_part = keys_part.reshape(count, head_count, HD)
    vals_part = vals_part.reshape(count, head_count, HD)
    scores = jnp.einsum(
        "fhd,nhd->fhn", queries, keys_part, preferred_element_type=jnp.float32
    ) / math.sqrt(HD)
    valid = (start + jnp.arange(count, dtype=jnp.int32) < own_length)[None, None, :]
    scores = jnp.where(valid, scores, -1e30)
    fresh = jnp.maximum(best, jnp.max(scores, axis=2))
    weights = jnp.where(valid, jnp.exp(scores - fresh[:, :, None]), 0.0)
    factor = jnp.exp(best - fresh)
    total = total * factor + jnp.sum(weights, axis=2)
    accum = accum * factor[:, :, None] + jnp.einsum(
        "fhn,nhd->fhd", weights.astype(jnp.bfloat16), vals_part, preferred_element_type=jnp.float32
    )
    return (fresh, total, accum)


def start_state(rows, heads_here):
    return (
        jnp.full((rows, heads_here), -1e30, jnp.float32),
        jnp.zeros((rows, heads_here), jnp.float32),
        jnp.zeros((rows, heads_here, HD), jnp.float32),
    )


def blockwise(carry, all_keys, all_vals, queries, own_length, block_rows):
    block_count = all_keys.shape[0] // block_rows

    def block_step(state, index):
        begin = index * block_rows
        piece = (
            lax.dynamic_slice_in_dim(all_keys, begin, block_rows, 0),
            lax.dynamic_slice_in_dim(all_vals, begin, block_rows, 0),
        )
        return (attend(state, piece, begin, queries, own_length), None)

    final, unused = lax.scan(block_step, carry, jnp.arange(block_count, dtype=jnp.int32))
    return final


def finish(final, query_pos, own_length):
    best, total, accum = final
    result = accum / total[:, :, None]
    query_live = (query_pos < own_length)[:, None, None]
    result = jnp.where(query_live, result, 0.0)
    return result.reshape(result.shape[0], result.shape[1] * HD).astype(jnp.bfloat16)


def per_device(
    frames_in, lengths, conv_weight, conv_bias, norm_gain, norm_shift, w_query, w_key, w_value
):
    record_count, frame_rows, channels = frames_in.shape
    ctx_place = lax.axis_index("ctx")
    positions = ctx_place * frame_rows + jnp.arange(frame_rows, dtype=jnp.int32)
    live = positions[None, :] < lengths[:, None]
    masked = jnp.where(live[:, :, None], frames_in, jnp.zeros((), frames_in.dtype))
    groups_here, kernel_width, group_in, group_out = conv_weight.shape
    half_width = kernel_width // 2
    padded = padded_2(masked, (("ctx", 1),), half_width)
    hidden = grouped_conv(padded, conv_weight, masked, conv_bias, frame_rows)
    record = swap_halves(hidden, "fsdp")
    own_length = lax.dynamic_index_in_dim(lengths, lax.axis_index("fsdp"), 0, keepdims=False)
    flat = record[0].astype(jnp.float32)
    centre = jnp.mean(flat, axis=1, keepdims=True)
    spread = jnp.mean((flat - centre) ** 2, axis=1, keepdims=True)
    normed = ((flat - centre) / jnp.sqrt(spread + 1e-05) * norm_gain + norm_shift).astype(
        jnp.bfloat16
    )
    query_flat = jnp.dot(normed, w_query, preferred_element_type=jnp.float32).astype(jnp.bfloat16)
    key_flat = jnp.dot(normed, w_key, preferred_element_type=jnp.float32).astype(jnp.bfloat16)
    val_flat = jnp.dot(normed, w_value, preferred_element_type=jnp.float32).astype(jnp.bfloat16)
    head_count = query_flat.shape[1] // HD
    width = key_flat.shape[1]
    both = jnp.concatenate([key_flat, val_flat], axis=1)
    pieces, starts = gather_ring(both, "ctx", frame_rows)
    key_pos = jnp.concatenate(
        [start + jnp.arange(frame_rows, dtype=jnp.int32) for start in starts]
    )
    result = fused_attention(query_flat, pieces, key_pos, own_length, positions)
    result = result.reshape(1, frame_rows, query_flat.shape[1])
    return (hidden, result)


def solution(mesh):
    in_specs = (
        P("rep", "ctx", "fsdp"),
        P("rep"),
        P("fsdp", None, None, None),
        P("fsdp"),
        P(),
        P(),
        P(),
        P(),
        P(),
    )
    out_specs = (P("rep", "ctx", "fsdp"), P(("rep", "fsdp"), "ctx", None))
    return jax.shard_map(
        per_device, mesh=mesh, in_specs=in_specs, out_specs=out_specs, check_vma=False
    )
```

```python
import math

import jax
import jax.numpy as jnp
from jax import lax
from jax.sharding import PartitionSpec as P
from jax.experimental import pallas as pl
from jax.experimental.pallas import tpu as pltpu

HD = 64


def padded_2(x, sides, width):
    for axis, dim in sides:
        size, length = (lax.axis_size(axis), x.shape[dim])
        up = [(i, (i + 1) % size) for i in range(size - 1)]
        down = [(j, i) for i, j in up]
        last = lax.slice_in_dim(x, length - width, length, axis=dim)
        first = lax.slice_in_dim(x, 0, width, axis=dim)
        before = lax.ppermute(last, axis, up)
        after = lax.ppermute(first, axis, down)
        x = jnp.concatenate([before, x, after], axis=dim)
    return x


def conv_body(x_ref, w_ref, res_ref, bias_ref, out_ref):
    pair_groups, recs, chans, lanes = x_ref.shape
    taps = w_ref.shape[3]
    rows = out_ref.shape[1]
    outs = w_ref.shape[2]

    def octet_step(group, q, acc):
        base = pl.multiple_of(q * 8, 8)
        hankels = []
        for r in range(recs):
            block = x_ref[group, r, pl.ds(base, 8), :]
            per_chan = []
            for c in range(8):
                row = jnp.broadcast_to(block[c : c + 1, :], (taps, lanes))
                rolled = pltpu.roll(row, 0, 1, stride=1, stride_axis=0)
                per_chan.append(rolled[:, :rows])
            hankels.append(per_chan)
        for pair in range(4):
            rhs = jnp.concatenate(
                [
                    jnp.concatenate([hankels[r][2 * pair + half] for r in range(recs)], axis=1)
                    for half in range(2)
                ],
                axis=0,
            )
            lhs = jnp.concatenate(
                [w_ref[group, base + 2 * pair], w_ref[group, base + 2 * pair + 1]], axis=1
            )
            acc = acc + jnp.dot(lhs, rhs, preferred_element_type=jnp.float32)
        return acc

    def both_groups(q, accs):
        return tuple(octet_step(group, q, acc) for group, acc in enumerate(accs))

    start = tuple(jnp.zeros((outs, recs * rows), jnp.float32) for _ in range(pair_groups))
    accs = lax.fori_loop(0, chans // 8, both_groups, start, unroll=8)
    acc = jnp.concatenate(accs, axis=0)
    across = lax.broadcasted_iota(jnp.int32, (rows, rows), 0) + lax.broadcasted_iota(
        jnp.int32, (rows, rows), 1
    )
    flip = jnp.where(across == rows - 1, 1.0, 0.0).astype(jnp.bfloat16)
    dims = (((1,), (1,)), ((), ()))
    for r in range(recs):
        part = acc[:, r * rows : (r + 1) * rows]
        high = part.astype(jnp.bfloat16)
        rest = part - high.astype(jnp.float32)
        middle = rest.astype(jnp.bfloat16)
        low = (rest - middle.astype(jnp.float32)).astype(jnp.bfloat16)
        total = lax.dot_general(flip, high, dims, preferred_element_type=jnp.float32)
        total = total + lax.dot_general(flip, middle, dims, preferred_element_type=jnp.float32)
        conv = total + lax.dot_general(flip, low, dims, preferred_element_type=jnp.float32)
        shifted = conv + bias_ref[...]
        gelu = 0.5 * shifted * (1.0 + lax.erf(shifted * (1.0 / math.sqrt(2.0))))
        hidden = res_ref[r].astype(jnp.float32) + gelu
        out_ref[r] = hidden.astype(out_ref.dtype)


def hankel_conv(xt, wv, residual, bias, rows):
    groups, recs, chans, lanes = xt.shape
    taps, outs = wv.shape[3], wv.shape[2]
    step = 4 if groups % 4 == 0 else 2
    return pl.pallas_call(
        conv_body,
        grid=(groups // step,),
        in_specs=[
            pl.BlockSpec((step, recs, chans, lanes), lambda g: (g, 0, 0, 0)),
            pl.BlockSpec((step, chans, outs, taps), lambda g: (g, 0, 0, 0)),
            pl.BlockSpec((recs, rows, step * outs), lambda g: (0, 0, g)),
            pl.BlockSpec((1, step * outs), lambda g: (0, g)),
        ],
        out_specs=pl.BlockSpec((recs, rows, step * outs), lambda g: (0, 0, g)),
        out_shape=jax.ShapeDtypeStruct((recs, rows, groups * outs), jnp.bfloat16),
        cost_estimate=pl.CostEstimate(
            flops=2 * groups * recs * rows * taps * chans * outs,
            bytes_accessed=xt.size * 2 + wv.size * 2 + groups * recs * rows * outs * 4,
            transcendentals=recs * rows * groups * outs,
        ),
    )(xt, wv, residual, bias)


def grouped_conv(padded, conv_weight, masked, conv_bias, frame_rows):
    recs, span = padded.shape[0], padded.shape[1]
    groups_here, taps, group_in, group_out = conv_weight.shape
    lanes = -(-(frame_rows + taps - 1) // 128) * 128
    grouped = jnp.pad(padded, ((0, 0), (0, lanes - span), (0, 0)))
    grouped = jnp.roll(jnp.flip(grouped, axis=1), frame_rows - lanes, axis=1)
    grouped = grouped.reshape(recs, lanes, groups_here, group_in).transpose(2, 0, 3, 1)
    bias = conv_bias.astype(jnp.float32).reshape(1, -1)
    return hankel_conv(grouped, jnp.transpose(conv_weight, (0, 2, 3, 1)), masked, bias, frame_rows)


def swap_halves(hidden, axis):
    if lax.axis_size(axis) != 2 or hidden.shape[0] != 2:
        return lax.all_to_all(hidden, axis, split_axis=0, concat_axis=2, tiled=True)
    place = lax.axis_index(axis)
    mine = lax.dynamic_index_in_dim(hidden, place, 0, keepdims=True)
    theirs = lax.dynamic_index_in_dim(hidden, 1 - place, 0, keepdims=True)
    got = lax.ppermute(theirs, axis, [(0, 1), (1, 0)])
    return jnp.where(place == 0, jnp.concatenate([mine, got], axis=2), jnp.concatenate([got, mine], axis=2))


def attend_body(*refs):
    q_ref, valid_ref, live_ref = refs[0], refs[1], refs[2]
    out_ref = refs[-1]
    block_refs = refs[3:-1]
    rows, width = q_ref.shape
    valid = valid_ref[...] > 0.0
    live = live_ref[...] > 0.0
    lanes = lax.broadcasted_iota(jnp.int32, (1, 128), 1)
    for pair in range(width // 128):
        cols = slice(pair * 128, (pair + 1) * 128)
        vcols = slice(width + pair * 128, width + (pair + 1) * 128)
        keys = jnp.concatenate([block[:, cols] for block in block_refs], axis=0)
        vals = jnp.concatenate([block[:, vcols] for block in block_refs], axis=0)
        query = q_ref[:, cols]
        results = []
        for half in range(2):
            mine = (lanes // HD) == half
            scores = lax.dot_general(
                jnp.where(mine, query, jnp.zeros_like(query)),
                keys,
                (((1,), (1,)), ((), ())),
                preferred_element_type=jnp.float32,
            ) / math.sqrt(HD)
            scores = jnp.where(valid, scores, -1e30)
            rowmax = jnp.max(scores, axis=1, keepdims=True)
            weights = jnp.where(valid, jnp.exp(scores - rowmax), 0.0)
            total = jnp.sum(weights, axis=1, keepdims=True)
            summed = jnp.dot(weights.astype(jnp.bfloat16), vals, preferred_element_type=jnp.float32)
            results.append(summed / total)
        both = jnp.where((lanes // HD) == 0, results[0], results[1])
        out_ref[:, cols] = jnp.where(live, both, 0.0).astype(out_ref.dtype)


def fused_attention(query_flat, pieces, key_pos, own_length, query_pos):
    rows, width = query_flat.shape
    keys_total = key_pos.shape[0]
    valid = (key_pos < own_length).astype(jnp.float32).reshape(1, keys_total)
    live = (query_pos < own_length).astype(jnp.float32).reshape(rows, 1)
    return pl.pallas_call(
        attend_body,
        out_shape=jax.ShapeDtypeStruct((rows, width), jnp.bfloat16),
        cost_estimate=pl.CostEstimate(
            flops=8 * rows * keys_total * width,
            bytes_accessed=2 * (rows * width * 2 + keys_total * width * 2),
            transcendentals=2 * rows * keys_total * (width // HD),
        ),
    )(query_flat, valid, live, *pieces)


def gather_line4(x, axis, rows):
    place = lax.axis_index(axis)
    from_below = lax.ppermute(x, axis, [(0, 1), (1, 2), (2, 3)])
    from_above = lax.ppermute(x, axis, [(1, 0), (2, 1), (3, 2)])
    across = lax.ppermute(x, axis, [(0, 2), (1, 3), (2, 0), (3, 1)])
    passed = lax.ppermute(across, axis, [(2, 3), (1, 0)])
    pieces = [
        x,
        across,
        jnp.where(place >= 1, from_below, passed),
        jnp.where(place <= 2, from_above, passed),
    ]
    starts = [place * rows, ((place + 2) % 4) * rows, ((place + 3) % 4) * rows, ((place + 1) % 4) * rows]
    return pieces, starts


def gather_ring(x, axis, rows):
    size = lax.axis_size(axis)
    if size == 4:
        return gather_line4(x, axis, rows)
    place = lax.axis_index(axis)
    pieces, starts = [x], [place * rows]
    for shift in range(1, size):
        pairs = [(i, (i + shift) % size) for i in range(size)]
        pieces.append(lax.ppermute(x, axis, pairs))
        starts.append(((place - shift) % size) * rows)
    return pieces, starts


def attend(carry, piece, start, queries, own_length):
    best, total, accum = carry
    keys_part, vals_part = piece
    count = keys_part.shape[0]
    head_count = queries.shape[1]
    keys_part = keys_part.reshape(count, head_count, HD)
    vals_part = vals_part.reshape(count, head_count, HD)
    scores = jnp.einsum(
        "fhd,nhd->fhn", queries, keys_part, preferred_element_type=jnp.float32
    ) / math.sqrt(HD)
    valid = (start + jnp.arange(count, dtype=jnp.int32) < own_length)[None, None, :]
    scores = jnp.where(valid, scores, -1e30)
    fresh = jnp.maximum(best, jnp.max(scores, axis=2))
    weights = jnp.where(valid, jnp.exp(scores - fresh[:, :, None]), 0.0)
    factor = jnp.exp(best - fresh)
    total = total * factor + jnp.sum(weights, axis=2)
    accum = accum * factor[:, :, None] + jnp.einsum(
        "fhn,nhd->fhd", weights.astype(jnp.bfloat16), vals_part, preferred_element_type=jnp.float32
    )
    return (fresh, total, accum)


def start_state(rows, heads_here):
    return (
        jnp.full((rows, heads_here), -1e30, jnp.float32),
        jnp.zeros((rows, heads_here), jnp.float32),
        jnp.zeros((rows, heads_here, HD), jnp.float32),
    )


def blockwise(carry, all_keys, all_vals, queries, own_length, block_rows):
    block_count = all_keys.shape[0] // block_rows

    def block_step(state, index):
        begin = index * block_rows
        piece = (
            lax.dynamic_slice_in_dim(all_keys, begin, block_rows, 0),
            lax.dynamic_slice_in_dim(all_vals, begin, block_rows, 0),
        )
        return (attend(state, piece, begin, queries, own_length), None)

    final, unused = lax.scan(block_step, carry, jnp.arange(block_count, dtype=jnp.int32))
    return final


def finish(final, query_pos, own_length):
    best, total, accum = final
    result = accum / total[:, :, None]
    query_live = (query_pos < own_length)[:, None, None]
    result = jnp.where(query_live, result, 0.0)
    return result.reshape(result.shape[0], result.shape[1] * HD).astype(jnp.bfloat16)


def per_device(
    frames_in, lengths, conv_weight, conv_bias, norm_gain, norm_shift, w_query, w_key, w_value
):
    record_count, frame_rows, channels = frames_in.shape
    ctx_place = lax.axis_index("ctx")
    positions = ctx_place * frame_rows + jnp.arange(frame_rows, dtype=jnp.int32)
    live = positions[None, :] < lengths[:, None]
    masked = jnp.where(live[:, :, None], frames_in, jnp.zeros((), frames_in.dtype))
    groups_here, kernel_width, group_in, group_out = conv_weight.shape
    half_width = kernel_width // 2
    padded = padded_2(masked, (("ctx", 1),), half_width)
    hidden = grouped_conv(padded, conv_weight, masked, conv_bias, frame_rows)
    record = swap_halves(hidden, "fsdp")
    own_length = lax.dynamic_index_in_dim(lengths, lax.axis_index("fsdp"), 0, keepdims=False)
    flat = record[0].astype(jnp.float32)
    centre = jnp.mean(flat, axis=1, keepdims=True)
    spread = jnp.mean((flat - centre) ** 2, axis=1, keepdims=True)
    normed = ((flat - centre) / jnp.sqrt(spread + 1e-05) * norm_gain + norm_shift).astype(
        jnp.bfloat16
    )
    query_flat = jnp.dot(normed, w_query, preferred_element_type=jnp.float32).astype(jnp.bfloat16)
    key_flat = jnp.dot(normed, w_key, preferred_element_type=jnp.float32).astype(jnp.bfloat16)
    val_flat = jnp.dot(normed, w_value, preferred_element_type=jnp.float32).astype(jnp.bfloat16)
    head_count = query_flat.shape[1] // HD
    width = key_flat.shape[1]
    both = jnp.concatenate([key_flat, val_flat], axis=1)
    pieces, starts = gather_ring(both, "ctx", frame_rows)
    key_pos = jnp.concatenate(
        [start + jnp.arange(frame_rows, dtype=jnp.int32) for start in starts]
    )
    result = fused_attention(query_flat, pieces, key_pos, own_length, positions)
    result = result.reshape(1, frame_rows, query_flat.shape[1])
    return (hidden, result)


def solution(mesh):
    in_specs = (
        P("rep", "ctx", "fsdp"),
        P("rep"),
        P("fsdp", None, None, None),
        P("fsdp"),
        P(),
        P(),
        P(),
        P(),
        P(),
    )
    out_specs = (P("rep", "ctx", "fsdp"), P(("rep", "fsdp"), "ctx", None))
    return jax.shard_map(
        per_device, mesh=mesh, in_specs=in_specs, out_specs=out_specs, check_vma=False
    )
```
